32 devices in a mesh: groups: 2 (over y), seq: 4 (over x, core), head: 4 (over z).
Axes of the slice: x: 2, y: 2, z: 4, core: 2. Of those that a mesh axis runs over, the one named last changes fastest.
Arguments:
- query_in: bfloat16 [8192, 3072], P(('groups', 'seq', 'head')), parts along dimension 0, may hold values from -4.5 to 4.5
- key_in: bfloat16 [8192, 3072], P(('groups', 'seq', 'head')), parts along dimension 0, may hold values from -4.5 to 4.5
- value_in: bfloat16 [8192, 3072], P(('groups', 'seq', 'head')), parts along dimension 0, may hold values from -6 to 6
- block_lists: int32 [64, 12], P('groups'), parts along dimension 0, may hold values from 0 to 31, as said below
Outputs:
- draft_out: bfloat16 [2048, 3072], P(('groups', 'seq'), 'head'), parts along dimension 0
- sparse_out: bfloat16 [8192, 3072], P(('groups', 'seq', 'head')), parts along dimension 0
The draws below stay inside these ranges and needn't reach their ends.
There are 2 independent parts, one for each index of `groups`. The reference program is written for one: setup_inputs(seed, part) draws one part's arguments, and reference() takes and returns one part's arrays. A program takes and returns all parts, laid end to end along the dimension named above; each array names one. Nothing has to cross between parts.
Inputs may be any that keep to these rules, and one draw needn't show every extreme that they name: block_lists[b] holds 12 distinct block numbers, b among them. Of the 8 blocks b with b // 8 = k, the query blocks with b // 8 = p (p other than k) select at most 2 distinct ones and at least one; in every draw some p selects exactly 2 from every other k.
All inputs are finite; a program needn't handle non-finite values.
Results may differ from the reference program's by a relative error of at most 0.0096.
Values may be sent and summed in bfloat16 or wider, within the bound.
No kernel may reach another device: no remote copies, remote signals or barrier semaphores. Data moves between devices by JAX's collectives and lax.ppermute only.
A program may use at most 128 MiB of HBM per device.

```python
import jax
import jax.numpy as jnp
from jax import lax

HEADS = 24
HD = 128
BLOCK = 128
POOL = 4
SEL = 12
CAP = 2
D = 3072
TOKENS = 4096
DRAFT = 1024
BPD = 8
NB = 32


def baseline_field(key):
    field_now = jnp.clip(1.6 * jax.random.normal(key, (TOKENS, D), jnp.float32), -4.5, 4.5)
    return field_now


def draw_query_in(key, part):
    field_now = baseline_field(jax.random.fold_in(key, 1))
    return field_now.astype(jnp.bfloat16)


def draw_key_in(key, part):
    field_now = baseline_field(jax.random.fold_in(key, 2))
    return field_now.astype(jnp.bfloat16)


def draw_block_lists(key, part):
    block_total = NB
    per_dev = BPD
    dev_count = block_total // per_dev
    counts = jax.random.randint(jax.random.fold_in(key, 11), (dev_count, dev_count), 1, CAP + 1)
    row_dev = jnp.arange(dev_count)[:, None]
    col_dev = jnp.arange(dev_count)[None, :]
    distance = (col_dev - row_dev) % dev_count
    full_row = jax.random.randint(jax.random.fold_in(key, 12), (), 0, dev_count)
    counts = jnp.where((distance == 1) | (distance == 2) | (row_dev == full_row), CAP, counts)
    counts = jnp.where(distance == 0, per_dev, counts)
    precedence = jax.random.randint(jax.random.fold_in(key, 13), (dev_count, dev_count, per_dev), 0, 4096) * per_dev + jnp.arange(per_dev)
    sorted_ids = jnp.argsort(precedence, axis=2)
    rank_within = jnp.argsort(sorted_ids, axis=2)
    chosen = rank_within < counts[:, :, None]
    candidate = chosen.reshape(dev_count, block_total)
    query_ids = jnp.arange(block_total)
    key_ids = jnp.arange(block_total)
    query_dev = query_ids // per_dev
    query_pos = query_ids % per_dev
    owner_of = key_ids // per_dev
    cand_rows = candidate[query_dev]
    assigned = (owner_of[None, :] % per_dev == query_pos[:, None]) & (owner_of[None, :] != query_dev[:, None])
    weight_unit = 4096 * block_total
    tiebreak = jax.random.randint(jax.random.fold_in(key, 14), (block_total, block_total), 0, 4096) * block_total + key_ids[None, :]
    ranking = tiebreak + weight_unit * cand_rows.astype(jnp.int32) + 2 * weight_unit * (cand_rows & assigned).astype(jnp.int32) + 4 * weight_unit * (key_ids[None, :] == query_ids[:, None]).astype(jnp.int32)
    ignored, picked = lax.top_k(ranking, SEL)
    return picked.astype(jnp.int32)


def levels(stream_key, shape, split, least, largest):
    level = 1.0
    for position, shards_of in split:
        steps = jax.random.uniform(jax.random.fold_in(jax.random.fold_in(stream_key, 6), position), (shards_of,), jnp.float32, least / len(split), largest / len(split))
        level = level * jnp.repeat(jnp.exp(steps), shape[position] // shards_of).reshape((-1,) + (1,) * (len(shape) - 1 - position))
    return level


def noise(rng, extent, scale, bound, shards=(), kind=jnp.bfloat16):
    values = jax.random.normal(rng, extent, jnp.float32) * scale
    if len(shards) > 0:
        values = levels(rng, extent, shards, -0.22, 0.18) * values
    return jnp.clip(values, min=-bound, max=bound).astype(kind)


def setup_inputs(seed: int = 0, part: int = 0) -> dict:
    key_of = jax.random.split(jax.random.key(seed), 5)
    own_keys = jax.random.split(jax.random.fold_in(key_of[4], part), 5)
    return {
        "query_in": draw_query_in(jax.random.fold_in(jax.random.fold_in(key_of[4], part), 71), part),
        "key_in": draw_key_in(jax.random.fold_in(jax.random.fold_in(key_of[4], part), 71), part),
        "value_in": noise(own_keys[2], (TOKENS, D), 1.0, 6.0, ((0, 16),)),
        "block_lists": draw_block_lists(jax.random.fold_in(jax.random.fold_in(key_of[4], part), 71), part),
    }


def pool_tokens(matrix):
    grouped = matrix.astype(jnp.float32).reshape(DRAFT, POOL, D)
    return (grouped.sum(axis=1) * (POOL ** -0.5)).astype(jnp.bfloat16)


def attend(query_rows, key_rows, value_rows):
    logit_values = jnp.einsum("...nd,...md->...nm", query_rows.astype(jnp.float32), key_rows.astype(jnp.float32)) * (HD ** -0.5)
    running = logit_values.max(axis=-1, keepdims=True)
    weights = jnp.exp(logit_values - running)
    totals = weights.sum(axis=-1, keepdims=True)
    rounded = weights.astype(jnp.bfloat16)
    weighted = jnp.einsum("...nm,...md->...nd", rounded.astype(jnp.float32), value_rows.astype(jnp.float32))
    return (weighted / totals).astype(jnp.bfloat16)


def split_draft(matrix):
    return matrix.reshape(DRAFT, HEADS, HD).transpose(1, 0, 2)


def split_blocks(matrix):
    return matrix.reshape(NB, BLOCK, HEADS, HD).transpose(2, 0, 1, 3)


def reference(query_in, key_in, value_in, block_lists):
    draft_query = split_draft(pool_tokens(query_in))
    draft_key = split_draft(pool_tokens(key_in))
    draft_value = split_draft(pool_tokens(value_in))
    draft_heads = lax.map(lambda triple: attend(triple[0], triple[1], triple[2]), (draft_query, draft_key, draft_value))
    draft_out = draft_heads.transpose(1, 0, 2).reshape(DRAFT, D)

    def sparse_head(triple):
        query_head, key_head, value_head = triple
        chosen_keys = key_head[block_lists].reshape(NB, SEL * BLOCK, HD)
        chosen_values = value_head[block_lists].reshape(NB, SEL * BLOCK, HD)
        return attend(query_head, chosen_keys, chosen_values)

    sparse_heads = lax.map(sparse_head, (split_blocks(query_in), split_blocks(key_in), split_blocks(value_in)))
    sparse_out = sparse_heads.transpose(1, 2, 0, 3).reshape(TOKENS, D)
    return (draft_out, sparse_out)
```

```python
import jax
import jax.numpy as jnp
from jax import lax
from jax.experimental import pallas as pl
from jax.experimental.pallas import tpu as pltpu
from jax.sharding import PartitionSpec as P

HD = 128
BLOCK = 128
POOL = 4
CAP = 2
SCALE = HD ** (-0.5)
DRAFT_ROWS = 128


def pool_tokens(matrix):
    grouped = matrix.astype(jnp.float32).reshape(matrix.shape[0] // POOL, POOL, matrix.shape[1])
    return (grouped.sum(axis=1) * POOL ** (-0.5)).astype(jnp.bfloat16)


def _scores(q, k):
    return lax.dot_general(
        q, k, (((1,), (1,)), ((), ())), preferred_element_type=jnp.float32
    ) * SCALE


def sparse_kernel(tbl_ref, q_ref, k_ref, v_ref, o_ref, s_ref):
    per_dev = q_ref.shape[0] // BLOCK
    sel = s_ref.shape[1] // BLOCK

    def body(i, carry):
        row = pl.multiple_of(i * BLOCK, BLOCK)
        q = q_ref[pl.ds(row, BLOCK), :]
        for j in range(sel):
            idx = tbl_ref[i * sel + j]
            k = k_ref[pl.ds(pl.multiple_of(idx * BLOCK, BLOCK), BLOCK), :]
            s_ref[:, j * BLOCK:(j + 1) * BLOCK] = _scores(q, k)
        s = s_ref[...]
        running = jnp.max(s, axis=1, keepdims=True)
        weights = jnp.exp(s - running)
        totals = jnp.sum(weights, axis=1, keepdims=True)
        rounded = weights.astype(jnp.bfloat16)
        acc = jnp.zeros((BLOCK, HD), jnp.float32)
        for j in range(sel):
            idx = tbl_ref[i * sel + j]
            v = v_ref[pl.ds(pl.multiple_of(idx * BLOCK, BLOCK), BLOCK), :]
            acc = acc + jnp.dot(
                rounded[:, j * BLOCK:(j + 1) * BLOCK], v, preferred_element_type=jnp.float32
            )
        o_ref[pl.ds(row, BLOCK), :] = (acc / totals).astype(o_ref.dtype)
        return carry

    lax.fori_loop(0, per_dev, body, 0)


def sparse_attention(tbl, queries, keys, values, sel):
    rows, width = queries.shape
    heads = width // HD
    key_rows = keys.shape[0]
    return pl.pallas_call(
        sparse_kernel,
        out_shape=jax.ShapeDtypeStruct((rows, width), jnp.bfloat16),
        grid_spec=pltpu.PrefetchScalarGridSpec(
            num_scalar_prefetch=1,
            grid=(heads,),
            in_specs=[
                pl.BlockSpec((rows, HD), lambda h, t: (0, h)),
                pl.BlockSpec((key_rows, HD), lambda h, t: (0, h)),
                pl.BlockSpec((key_rows, HD), lambda h, t: (0, h)),
            ],
            out_specs=pl.BlockSpec((rows, HD), lambda h, t: (0, h)),
            scratch_shapes=[pltpu.VMEM((BLOCK, sel * BLOCK), jnp.float32)],
        ),
    )(tbl, queries, keys, values)


def draft_kernel(q_ref, k_ref, v_ref, o_ref):
    s = _scores(q_ref[...], k_ref[...])
    running = jnp.max(s, axis=1, keepdims=True)
    weights = jnp.exp(s - running)
    totals = jnp.sum(weights, axis=1, keepdims=True)
    weighted = jnp.dot(weights.astype(jnp.bfloat16), v_ref[...], preferred_element_type=jnp.float32)
    o_ref[...] = (weighted / totals).astype(o_ref.dtype)


def draft_attention(queries, keys, values):
    rows, width = queries.shape
    heads = width // HD
    key_rows = keys.shape[0]
    tile = min(DRAFT_ROWS, rows)
    return pl.pallas_call(
        draft_kernel,
        out_shape=jax.ShapeDtypeStruct((rows, width), jnp.bfloat16),
        grid=(heads, rows // tile),
        in_specs=[
            pl.BlockSpec((tile, HD), lambda h, r: (r, h)),
            pl.BlockSpec((key_rows, HD), lambda h, r: (0, h)),
            pl.BlockSpec((key_rows, HD), lambda h, r: (0, h)),
        ],
        out_specs=pl.BlockSpec((tile, HD), lambda h, r: (r, h)),
    )(queries, keys, values)


def on_device(query_in, key_in, value_in, block_lists):
    key_rows = lax.all_to_all(key_in, "head", split_axis=1, concat_axis=0, tiled=True)
    value_rows = lax.all_to_all(value_in, "head", split_axis=1, concat_axis=0, tiled=True)
    queries = lax.all_to_all(query_in, "head", split_axis=1, concat_axis=0, tiled=True)
    seq_rows, width = queries.shape

    draft_keys = lax.all_gather(pool_tokens(key_rows), "seq", axis=0, tiled=True)
    draft_values = lax.all_gather(pool_tokens(value_rows), "seq", axis=0, tiled=True)

    seq_count = lax.axis_size("seq")
    seq_index = lax.axis_index("seq")
    per_dev = seq_rows // BLOCK
    block_total, select_count = block_lists.shape
    block_ids = jnp.arange(block_total, dtype=jnp.int32)
    touched = jnp.any(block_lists[:, :, None] == block_ids[None, None, :], axis=1)
    needed = jnp.any(touched.reshape(seq_count, per_dev, seq_count, per_dev), axis=1)
    slot_rank = jnp.cumsum(needed.astype(jnp.int32), axis=2) - 1
    send_need = lax.dynamic_index_in_dim(needed, seq_index, axis=1, keepdims=False)
    send_rank = lax.dynamic_index_in_dim(slot_rank, seq_index, axis=1, keepdims=False)
    slot_hit = send_need[:, None, :] & (
        send_rank[:, None, :] == jnp.arange(CAP, dtype=jnp.int32)[None, :, None]
    )
    send_idx = jnp.sum(
        jnp.where(slot_hit, jnp.arange(per_dev, dtype=jnp.int32)[None, None, :], 0), axis=2
    ).reshape(-1)
    key_blocks = key_rows.reshape(per_dev, BLOCK, width)
    value_blocks = value_rows.reshape(per_dev, BLOCK, width)
    outgoing = jnp.stack(
        [jnp.take(key_blocks, send_idx, axis=0), jnp.take(value_blocks, send_idx, axis=0)], axis=1
    ).reshape(seq_count, CAP, 2, BLOCK, width)
    arrived = lax.all_to_all(outgoing, "seq", split_axis=0, concat_axis=0, tiled=True)
    remote_keys = arrived[:, :, 0].reshape(seq_count * CAP * BLOCK, width)
    remote_values = arrived[:, :, 1].reshape(seq_count * CAP * BLOCK, width)
    all_keys = jnp.concatenate([key_rows, remote_keys], axis=0)
    all_values = jnp.concatenate([value_rows, remote_values], axis=0)

    own_lists = lax.dynamic_slice_in_dim(block_lists, seq_index * per_dev, per_dev, 0)
    owners = own_lists // per_dev
    within = own_lists % per_dev
    own_rank = lax.dynamic_index_in_dim(slot_rank, seq_index, axis=0, keepdims=False)
    ranks_used = jnp.clip(own_rank[owners, within], 0, CAP - 1)
    joint_pos = jnp.where(owners == seq_index, within, per_dev + owners * CAP + ranks_used)
    table = jnp.clip(joint_pos, 0, per_dev + seq_count * CAP - 1).reshape(-1).astype(jnp.int32)

    sparse_rows = sparse_attention(table, queries, all_keys, all_values, select_count)
    sparse_out = lax.all_to_all(sparse_rows, "head", split_axis=0, concat_axis=1, tiled=True)

    draft_out = draft_attention(pool_tokens(queries), draft_keys, draft_values)
    return (draft_out, sparse_out)


def solution(mesh):
    return jax.shard_map(
        on_device,
        mesh=mesh,
        in_specs=(
            P(("groups", "seq", "head"), None),
            P(("groups", "seq", "head"), None),
            P(("groups", "seq", "head"), None),
            P("groups", None),
        ),
        out_specs=(P(("groups", "seq"), "head"), P(("groups", "seq", "head"), None)),
        check_vma=False,
    )
```

```python
import jax
import jax.numpy as jnp
from jax import lax
from jax.experimental import pallas as pl
from jax.experimental.pallas import tpu as pltpu
from jax.sharding import PartitionSpec as P

HD = 128
BLOCK = 128
POOL = 4
CAP = 2
SCALE = HD ** (-0.5)
DRAFT_ROWS = 128


def pool_tokens(matrix):
    grouped = matrix.astype(jnp.float32).reshape(matrix.shape[0] // POOL, POOL, matrix.shape[1])
    return (grouped.sum(axis=1) * POOL ** (-0.5)).astype(jnp.bfloat16)


def _scores(q, k):
    return lax.dot_general(
        q, k, (((1,), (1,)), ((), ())), preferred_element_type=jnp.float32
    ) * SCALE


def sparse_kernel(tbl_ref, q_ref, k_ref, v_ref, o_ref, ks_ref, vs_ref):
    per_dev = q_ref.shape[0] // BLOCK
    sel = ks_ref.shape[0] // BLOCK

    def body(i, carry):
        row = pl.multiple_of(i * BLOCK, BLOCK)
        for j in range(sel):
            start = pl.multiple_of(tbl_ref[i * sel + j] * BLOCK, BLOCK)
            ks_ref[j * BLOCK:(j + 1) * BLOCK, :] = k_ref[pl.ds(start, BLOCK), :]
            vs_ref[j * BLOCK:(j + 1) * BLOCK, :] = v_ref[pl.ds(start, BLOCK), :]
        s = _scores(q_ref[pl.ds(row, BLOCK), :], ks_ref[...])
        running = jnp.max(s, axis=1, keepdims=True)
        weights = jnp.exp(s - running)
        totals = jnp.sum(weights, axis=1, keepdims=True)
        weighted = jnp.dot(
            weights.astype(jnp.bfloat16), vs_ref[...], preferred_element_type=jnp.float32
        )
        o_ref[pl.ds(row, BLOCK), :] = (weighted / totals).astype(o_ref.dtype)
        return carry

    lax.fori_loop(0, per_dev, body, 0)


def sparse_attention(tbl, queries, keys, values, sel):
    rows, width = queries.shape
    heads = width // HD
    key_rows = keys.shape[0]
    return pl.pallas_call(
        sparse_kernel,
        out_shape=jax.ShapeDtypeStruct((rows, width), jnp.bfloat16),
        grid_spec=pltpu.PrefetchScalarGridSpec(
            num_scalar_prefetch=1,
            grid=(heads,),
            in_specs=[
                pl.BlockSpec((rows, HD), lambda h, t: (0, h)),
                pl.BlockSpec((key_rows, HD), lambda h, t: (0, h)),
                pl.BlockSpec((key_rows, HD), lambda h, t: (0, h)),
            ],
            out_specs=pl.BlockSpec((rows, HD), lambda h, t: (0, h)),
            scratch_shapes=[
                pltpu.VMEM((sel * BLOCK, HD), jnp.bfloat16),
                pltpu.VMEM((sel * BLOCK, HD), jnp.bfloat16),
            ],
        ),
    )(tbl, queries, keys, values)


def draft_kernel(q_ref, k_ref, v_ref, o_ref):
    s = _scores(q_ref[...], k_ref[...])
    running = jnp.max(s, axis=1, keepdims=True)
    weights = jnp.exp(s - running)
    totals = jnp.sum(weights, axis=1, keepdims=True)
    weighted = jnp.dot(weights.astype(jnp.bfloat16), v_ref[...], preferred_element_type=jnp.float32)
    o_ref[...] = (weighted / totals).astype(o_ref.dtype)


def draft_attention(queries, keys, values):
    rows, width = queries.shape
    heads = width // HD
    key_rows = keys.shape[0]
    tile = min(DRAFT_ROWS, rows)
    return pl.pallas_call(
        draft_kernel,
        out_shape=jax.ShapeDtypeStruct((rows, width), jnp.bfloat16),
        grid=(heads, rows // tile),
        in_specs=[
            pl.BlockSpec((tile, HD), lambda h, r: (r, h)),
            pl.BlockSpec((key_rows, HD), lambda h, r: (0, h)),
            pl.BlockSpec((key_rows, HD), lambda h, r: (0, h)),
        ],
        out_specs=pl.BlockSpec((tile, HD), lambda h, r: (r, h)),
    )(queries, keys, values)


def on_device(query_in, key_in, value_in, block_lists):
    key_rows = lax.all_to_all(key_in, "head", split_axis=1, concat_axis=0, tiled=True)
    value_rows = lax.all_to_all(value_in, "head", split_axis=1, concat_axis=0, tiled=True)
    queries = lax.all_to_all(query_in, "head", split_axis=1, concat_axis=0, tiled=True)
    seq_rows, width = queries.shape

    draft_keys = lax.all_gather(pool_tokens(key_rows), "seq", axis=0, tiled=True)
    draft_values = lax.all_gather(pool_tokens(value_rows), "seq", axis=0, tiled=True)

    seq_count = lax.axis_size("seq")
    seq_index = lax.axis_index("seq")
    per_dev = seq_rows // BLOCK
    block_total, select_count = block_lists.shape
    block_ids = jnp.arange(block_total, dtype=jnp.int32)
    touched = jnp.any(block_lists[:, :, None] == block_ids[None, None, :], axis=1)
    needed = jnp.any(touched.reshape(seq_count, per_dev, seq_count, per_dev), axis=1)
    slot_rank = jnp.cumsum(needed.astype(jnp.int32), axis=2) - 1
    send_need = lax.dynamic_index_in_dim(needed, seq_index, axis=1, keepdims=False)
    send_rank = lax.dynamic_index_in_dim(slot_rank, seq_index, axis=1, keepdims=False)
    slot_hit = send_need[:, None, :] & (
        send_rank[:, None, :] == jnp.arange(CAP, dtype=jnp.int32)[None, :, None]
    )
    send_idx = jnp.sum(
        jnp.where(slot_hit, jnp.arange(per_dev, dtype=jnp.int32)[None, None, :], 0), axis=2
    ).reshape(-1)
    key_blocks = key_rows.reshape(per_dev, BLOCK, width)
    value_blocks = value_rows.reshape(per_dev, BLOCK, width)
    outgoing = jnp.stack(
        [jnp.take(key_blocks, send_idx, axis=0), jnp.take(value_blocks, send_idx, axis=0)], axis=1
    ).reshape(seq_count, CAP, 2, BLOCK, width)
    arrived = lax.all_to_all(outgoing, "seq", split_axis=0, concat_axis=0, tiled=True)
    remote_keys = arrived[:, :, 0].reshape(seq_count * CAP * BLOCK, width)
    remote_values = arrived[:, :, 1].reshape(seq_count * CAP * BLOCK, width)
    all_keys = jnp.concatenate([key_rows, remote_keys], axis=0)
    all_values = jnp.concatenate([value_rows, remote_values], axis=0)

    own_lists = lax.dynamic_slice_in_dim(block_lists, seq_index * per_dev, per_dev, 0)
    owners = own_lists // per_dev
    within = own_lists % per_dev
    own_rank = lax.dynamic_index_in_dim(slot_rank, seq_index, axis=0, keepdims=False)
    ranks_used = jnp.clip(own_rank[owners, within], 0, CAP - 1)
    joint_pos = jnp.where(owners == seq_index, within, per_dev + owners * CAP + ranks_used)
    table = jnp.clip(joint_pos, 0, per_dev + seq_count * CAP - 1).reshape(-1).astype(jnp.int32)

    sparse_rows = sparse_attention(table, queries, all_keys, all_values, select_count)
    sparse_out = lax.all_to_all(sparse_rows, "head", split_axis=0, concat_axis=1, tiled=True)

    draft_out = draft_attention(pool_tokens(queries), draft_keys, draft_values)
    return (draft_out, sparse_out)


def solution(mesh):
    return jax.shard_map(
        on_device,
        mesh=mesh,
        in_specs=(
            P(("groups", "seq", "head"), None),
            P(("groups", "seq", "head"), None),
            P(("groups", "seq", "head"), None),
            P("groups", None),
        ),
        out_specs=(P(("groups", "seq"), "head"), P(("groups", "seq", "head"), None)),
        check_vma=False,
    )
```

```python
import jax
import jax.numpy as jnp
from jax import lax
from jax.experimental import pallas as pl
from jax.experimental.pallas import tpu as pltpu
from jax.sharding import PartitionSpec as P

HD = 128
BLOCK = 128
POOL = 4
CAP = 2
SCALE = HD ** (-0.5)
DRAFT_ROWS = 128


def pool_tokens(matrix):
    grouped = matrix.astype(jnp.float32).reshape(matrix.shape[0] // POOL, POOL, matrix.shape[1])
    return (grouped.sum(axis=1) * POOL ** (-0.5)).astype(jnp.bfloat16)


def _scores(q, k):
    return lax.dot_general(
        q, k, (((1,), (1,)), ((), ())), preferred_element_type=jnp.float32
    ) * SCALE


def sparse_kernel(tbl_ref, q_ref, k_ref, v_ref, o_ref, ks_ref, vs_ref):
    per_dev = q_ref.shape[0] // BLOCK
    sel = ks_ref.shape[0] // BLOCK

    def body(i, carry):
        row = pl.multiple_of(i * BLOCK, BLOCK)
        for j in range(sel):
            start = pl.multiple_of(tbl_ref[i * sel + j] * BLOCK, BLOCK)
            ks_ref[j * BLOCK:(j + 1) * BLOCK, :] = k_ref[pl.ds(start, BLOCK), :]
            vs_ref[j * BLOCK:(j + 1) * BLOCK, :] = v_ref[pl.ds(start, BLOCK), :]
        s = _scores(q_ref[pl.ds(row, BLOCK), :], ks_ref[...])
        running = jnp.max(s, axis=1, keepdims=True)
        weights = jnp.exp(s - running)
        totals = jnp.sum(weights, axis=1, keepdims=True)
        weighted = jnp.dot(
            weights.astype(jnp.bfloat16), vs_ref[...], preferred_element_type=jnp.float32
        )
        o_ref[pl.ds(row, BLOCK), :] = (weighted / totals).astype(o_ref.dtype)
        return carry

    lax.fori_loop(0, per_dev, body, 0)


def sparse_attention(tbl, queries, keys, values, sel):
    rows, width = queries.shape
    heads = width // HD
    key_rows = keys.shape[0]
    return pl.pallas_call(
        sparse_kernel,
        out_shape=jax.ShapeDtypeStruct((rows, width), jnp.bfloat16),
        grid_spec=pltpu.PrefetchScalarGridSpec(
            num_scalar_prefetch=1,
            grid=(heads,),
            in_specs=[
                pl.BlockSpec((rows, HD), lambda h, t: (0, h)),
                pl.BlockSpec((key_rows, HD), lambda h, t: (0, h)),
                pl.BlockSpec((key_rows, HD), lambda h, t: (0, h)),
            ],
            out_specs=pl.BlockSpec((rows, HD), lambda h, t: (0, h)),
            scratch_shapes=[
                pltpu.VMEM((sel * BLOCK, HD), jnp.bfloat16),
                pltpu.VMEM((sel * BLOCK, HD), jnp.bfloat16),
            ],
        ),
    )(tbl, queries, keys, values)


def draft_kernel(q_ref, k_ref, v_ref, o_ref):
    s = _scores(q_ref[...], k_ref[...])
    running = jnp.max(s, axis=1, keepdims=True)
    weights = jnp.exp(s - running)
    totals = jnp.sum(weights, axis=1, keepdims=True)
    weighted = jnp.dot(weights.astype(jnp.bfloat16), v_ref[...], preferred_element_type=jnp.float32)
    o_ref[...] = (weighted / totals).astype(o_ref.dtype)


def draft_attention(queries, keys, values):
    rows, width = queries.shape
    heads = width // HD
    key_rows = keys.shape[0]
    tile = min(DRAFT_ROWS, rows)
    return pl.pallas_call(
        draft_kernel,
        out_shape=jax.ShapeDtypeStruct((rows, width), jnp.bfloat16),
        grid=(heads, rows // tile),
        in_specs=[
            pl.BlockSpec((tile, HD), lambda h, r: (r, h)),
            pl.BlockSpec((key_rows, HD), lambda h, r: (0, h)),
            pl.BlockSpec((key_rows, HD), lambda h, r: (0, h)),
        ],
        out_specs=pl.BlockSpec((tile, HD), lambda h, r: (r, h)),
    )(queries, keys, values)


def on_device(query_in, key_in, value_in, block_lists):
    key_rows = lax.all_to_all(key_in, "head", split_axis=1, concat_axis=0, tiled=True)
    value_rows = lax.all_to_all(value_in, "head", split_axis=1, concat_axis=0, tiled=True)
    queries = lax.all_to_all(query_in, "head", split_axis=1, concat_axis=0, tiled=True)
    seq_rows, width = queries.shape

    draft_keys = lax.all_gather(pool_tokens(key_rows), "seq", axis=0, tiled=True)
    draft_values = lax.all_gather(pool_tokens(value_rows), "seq", axis=0, tiled=True)

    seq_count = lax.axis_size("seq")
    seq_index = lax.axis_index("seq")
    per_dev = seq_rows // BLOCK
    block_total, select_count = block_lists.shape
    block_ids = jnp.arange(block_total, dtype=jnp.int32)
    touched = jnp.any(block_lists[:, :, None] == block_ids[None, None, :], axis=1)
    needed = jnp.any(touched.reshape(seq_count, per_dev, seq_count, per_dev), axis=1)
    slot_rank = jnp.cumsum(needed.astype(jnp.int32), axis=2) - 1
    send_need = lax.dynamic_index_in_dim(needed, seq_index, axis=1, keepdims=False)
    send_rank = lax.dynamic_index_in_dim(slot_rank, seq_index, axis=1, keepdims=False)
    slot_hit = send_need[:, None, :] & (
        send_rank[:, None, :] == jnp.arange(CAP, dtype=jnp.int32)[None, :, None]
    )
    send_idx = jnp.sum(
        jnp.where(slot_hit, jnp.arange(per_dev, dtype=jnp.int32)[None, None, :], 0), axis=2
    ).reshape(-1)
    key_blocks = key_rows.reshape(per_dev, BLOCK, width)
    value_blocks = value_rows.reshape(per_dev, BLOCK, width)
    outgoing = jnp.stack(
        [jnp.take(key_blocks, send_idx, axis=0), jnp.take(value_blocks, send_idx, axis=0)], axis=1
    ).reshape(seq_count, CAP, 2, BLOCK, width)
    arrivals = []
    for shift in range(1, seq_count):
        parcel = lax.dynamic_index_in_dim(
            outgoing, (seq_index + shift) % seq_count, axis=0, keepdims=False
        )
        arrivals.append(
            lax.ppermute(
                parcel, "seq", [(i, (i + shift) % seq_count) for i in range(seq_count)]
            )
        )
    arrived = jnp.stack(arrivals, axis=0)
    remote_keys = arrived[:, :, 0].reshape((seq_count - 1) * CAP * BLOCK, width)
    remote_values = arrived[:, :, 1].reshape((seq_count - 1) * CAP * BLOCK, width)
    all_keys = jnp.concatenate([key_rows, remote_keys], axis=0)
    all_values = jnp.concatenate([value_rows, remote_values], axis=0)

    own_lists = lax.dynamic_slice_in_dim(block_lists, seq_index * per_dev, per_dev, 0)
    owners = own_lists // per_dev
    within = own_lists % per_dev
    own_rank = lax.dynamic_index_in_dim(slot_rank, seq_index, axis=0, keepdims=False)
    ranks_used = jnp.clip(own_rank[owners, within], 0, CAP - 1)
    distance = (seq_index - owners) % seq_count
    joint_pos = jnp.where(distance == 0, within, per_dev + (distance - 1) * CAP + ranks_used)
    table = jnp.clip(joint_pos, 0, per_dev + (seq_count - 1) * CAP - 1).reshape(-1).astype(jnp.int32)

    sparse_rows = sparse_attention(table, queries, all_keys, all_values, select_count)
    sparse_out = lax.all_to_all(sparse_rows, "head", split_axis=0, concat_axis=1, tiled=True)

    draft_out = draft_attention(pool_tokens(queries), draft_keys, draft_values)
    return (draft_out, sparse_out)


def solution(mesh):
    return jax.shard_map(
        on_device,
        mesh=mesh,
        in_specs=(
            P(("groups", "seq", "head"), None),
            P(("groups", "seq", "head"), None),
            P(("groups", "seq", "head"), None),
            P("groups", None),
        ),
        out_specs=(P(("groups", "seq"), "head"), P(("groups", "seq", "head"), None)),
        check_vma=False,
    )
```

```python
import jax
import jax.numpy as jnp
from jax import lax
from jax.experimental import pallas as pl
from jax.experimental.pallas import tpu as pltpu
from jax.sharding import PartitionSpec as P

HD = 128
BLOCK = 128
POOL = 4
CAP = 2
SCALE = HD ** (-0.5)
DRAFT_ROWS = 128


def pool_tokens(matrix):
    grouped = matrix.astype(jnp.float32).reshape(matrix.shape[0] // POOL, POOL, matrix.shape[1])
    return (grouped.sum(axis=1) * POOL ** (-0.5)).astype(jnp.bfloat16)


def _scores(q, k):
    return lax.dot_general(
        q, k, (((1,), (1,)), ((), ())), preferred_element_type=jnp.float32
    ) * SCALE


def sparse_kernel(tbl_ref, q_ref, k_ref, v_ref, kr_ref, vr_ref, o_ref, ks_ref, vs_ref):
    per_dev = q_ref.shape[0] // BLOCK
    sel = ks_ref.shape[0] // BLOCK
    remote_count = kr_ref.shape[0] // BLOCK

    def body(i, carry):
        row = pl.multiple_of(i * BLOCK, BLOCK)
        for j in range(sel):
            idx = tbl_ref[i * sel + j]
            dest = slice(j * BLOCK, (j + 1) * BLOCK)

            @pl.when(idx < per_dev)
            def _():
                start = pl.multiple_of(jnp.minimum(idx, per_dev - 1) * BLOCK, BLOCK)
                ks_ref[dest, :] = k_ref[pl.ds(start, BLOCK), :]
                vs_ref[dest, :] = v_ref[pl.ds(start, BLOCK), :]

            @pl.when(idx >= per_dev)
            def _():
                far = jnp.clip(idx - per_dev, 0, remote_count - 1)
                start = pl.multiple_of(far * BLOCK, BLOCK)
                ks_ref[dest, :] = kr_ref[pl.ds(start, BLOCK), :]
                vs_ref[dest, :] = vr_ref[pl.ds(start, BLOCK), :]

        s = _scores(q_ref[pl.ds(row, BLOCK), :], ks_ref[...])
        running = jnp.max(s, axis=1, keepdims=True)
        weights = jnp.exp(s - running)
        totals = jnp.sum(weights, axis=1, keepdims=True)
        weighted = jnp.dot(
            weights.astype(jnp.bfloat16), vs_ref[...], preferred_element_type=jnp.float32
        )
        o_ref[pl.ds(row, BLOCK), :] = (weighted / totals).astype(o_ref.dtype)
        return carry

    lax.fori_loop(0, per_dev, body, 0)


def sparse_attention(tbl, queries, keys, values, far_keys, far_values, sel, head_lo, heads):
    rows = queries.shape[0]
    near_rows = keys.shape[0]
    far_rows = far_keys.shape[0]

    def column(h, t):
        return (0, h + head_lo)

    return pl.pallas_call(
        sparse_kernel,
        out_shape=jax.ShapeDtypeStruct((rows, heads * HD), jnp.bfloat16),
        grid_spec=pltpu.PrefetchScalarGridSpec(
            num_scalar_prefetch=1,
            grid=(heads,),
            in_specs=[
                pl.BlockSpec((rows, HD), column),
                pl.BlockSpec((near_rows, HD), column),
                pl.BlockSpec((near_rows, HD), column),
                pl.BlockSpec((far_rows, HD), column),
                pl.BlockSpec((far_rows, HD), column),
            ],
            out_specs=pl.BlockSpec((rows, HD), lambda h, t: (0, h)),
            scratch_shapes=[
                pltpu.VMEM((sel * BLOCK, HD), jnp.bfloat16),
                pltpu.VMEM((sel * BLOCK, HD), jnp.bfloat16),
            ],
        ),
    )(tbl, queries, keys, values, far_keys, far_values)


def draft_kernel(q_ref, k_ref, v_ref, o_ref):
    s = _scores(q_ref[...], k_ref[...])
    running = jnp.max(s, axis=1, keepdims=True)
    weights = jnp.exp(s - running)
    totals = jnp.sum(weights, axis=1, keepdims=True)
    weighted = jnp.dot(weights.astype(jnp.bfloat16), v_ref[...], preferred_element_type=jnp.float32)
    o_ref[...] = (weighted / totals).astype(o_ref.dtype)


def draft_attention(queries, keys, values):
    rows, width = queries.shape
    heads = width // HD
    key_rows = keys.shape[0]
    tile = min(DRAFT_ROWS, rows)
    return pl.pallas_call(
        draft_kernel,
        out_shape=jax.ShapeDtypeStruct((rows, width), jnp.bfloat16),
        grid=(heads, rows // tile),
        in_specs=[
            pl.BlockSpec((tile, HD), lambda h, r: (r, h)),
            pl.BlockSpec((key_rows, HD), lambda h, r: (0, h)),
            pl.BlockSpec((key_rows, HD), lambda h, r: (0, h)),
        ],
        out_specs=pl.BlockSpec((tile, HD), lambda h, r: (r, h)),
    )(queries, keys, values)


def on_device(query_in, key_in, value_in, block_lists):
    pair_rows = lax.all_to_all(
        jnp.stack([key_in, value_in], axis=0), "head", split_axis=2, concat_axis=1, tiled=True
    )
    key_rows, value_rows = pair_rows[0], pair_rows[1]
    queries = lax.all_to_all(query_in, "head", split_axis=1, concat_axis=0, tiled=True)
    seq_rows, width = queries.shape

    draft_keys = lax.all_gather(pool_tokens(key_rows), "seq", axis=0, tiled=True)
    draft_values = lax.all_gather(pool_tokens(value_rows), "seq", axis=0, tiled=True)

    seq_count = lax.axis_size("seq")
    seq_index = lax.axis_index("seq")
    per_dev = seq_rows // BLOCK
    block_total, select_count = block_lists.shape
    block_ids = jnp.arange(block_total, dtype=jnp.int32)
    touched = jnp.any(block_lists[:, :, None] == block_ids[None, None, :], axis=1)
    needed = jnp.any(touched.reshape(seq_count, per_dev, seq_count, per_dev), axis=1)
    slot_rank = jnp.cumsum(needed.astype(jnp.int32), axis=2) - 1
    send_need = lax.dynamic_index_in_dim(needed, seq_index, axis=1, keepdims=False)
    send_rank = lax.dynamic_index_in_dim(slot_rank, seq_index, axis=1, keepdims=False)
    slot_hit = send_need[:, None, :] & (
        send_rank[:, None, :] == jnp.arange(CAP, dtype=jnp.int32)[None, :, None]
    )
    send_idx = jnp.sum(
        jnp.where(slot_hit, jnp.arange(per_dev, dtype=jnp.int32)[None, None, :], 0), axis=2
    ).reshape(-1)
    key_blocks = key_rows.reshape(per_dev, BLOCK, width)
    value_blocks = value_rows.reshape(per_dev, BLOCK, width)
    outgoing = jnp.stack(
        [jnp.take(key_blocks, send_idx, axis=0), jnp.take(value_blocks, send_idx, axis=0)], axis=1
    ).reshape(seq_count, CAP, 2, BLOCK, width)
    arrivals = []
    for shift in range(1, seq_count):
        parcel = lax.dynamic_index_in_dim(
            outgoing, (seq_index + shift) % seq_count, axis=0, keepdims=False
        )
        arrivals.append(
            lax.ppermute(
                parcel, "seq", [(i, (i + shift) % seq_count) for i in range(seq_count)]
            )
        )
    arrived = jnp.stack(arrivals, axis=0)
    remote_keys = arrived[:, :, 0].reshape((seq_count - 1) * CAP * BLOCK, width)
    remote_values = arrived[:, :, 1].reshape((seq_count - 1) * CAP * BLOCK, width)

    own_lists = lax.dynamic_slice_in_dim(block_lists, seq_index * per_dev, per_dev, 0)
    owners = own_lists // per_dev
    within = own_lists % per_dev
    own_rank = lax.dynamic_index_in_dim(slot_rank, seq_index, axis=0, keepdims=False)
    ranks_used = jnp.clip(own_rank[owners, within], 0, CAP - 1)
    distance = (seq_index - owners) % seq_count
    joint_pos = jnp.where(distance == 0, within, per_dev + (distance - 1) * CAP + ranks_used)
    table = jnp.clip(joint_pos, 0, per_dev + (seq_count - 1) * CAP - 1).reshape(-1).astype(jnp.int32)

    heads = width // HD
    first = max(1, heads // 2)
    pieces = []
    for head_lo, count in ((0, first), (first, heads - first)):
        if count == 0:
            continue
        rows_part = sparse_attention(
            table, queries, key_rows, value_rows, remote_keys, remote_values,
            select_count, head_lo, count,
        )
        back = lax.all_to_all(rows_part, "head", split_axis=0, concat_axis=1, tiled=True)
        pieces.append(back.reshape(back.shape[0], -1, count * HD))
    sparse_out = jnp.concatenate(pieces, axis=2).reshape(pieces[0].shape[0], -1)

    draft_out = draft_attention(pool_tokens(queries), draft_keys, draft_values)
    return (draft_out, sparse_out)


def solution(mesh):
    return jax.shard_map(
        on_device,
        mesh=mesh,
        in_specs=(
            P(("groups", "seq", "head"), None),
            P(("groups", "seq", "head"), None),
            P(("groups", "seq", "head"), None),
            P("groups", None),
        ),
        out_specs=(P(("groups", "seq"), "head"), P(("groups", "seq", "head"), None)),
        check_vma=False,
    )
```

```python
import jax
import jax.numpy as jnp
from jax import lax
from jax.experimental import pallas as pl
from jax.experimental.pallas import tpu as pltpu
from jax.sharding import PartitionSpec as P

HD = 128
BLOCK = 128
POOL = 4
CAP = 2
SCALE = HD ** (-0.5)
DRAFT_ROWS = 128


def pool_tokens(matrix):
    grouped = matrix.astype(jnp.float32).reshape(matrix.shape[0] // POOL, POOL, matrix.shape[1])
    return (grouped.sum(axis=1) * POOL ** (-0.5)).astype(jnp.bfloat16)


def _scores(q, k):
    return lax.dot_general(
        q, k, (((1,), (1,)), ((), ())), preferred_element_type=jnp.float32
    ) * SCALE


def sparse_kernel(tbl_ref, q_ref, k_ref, v_ref, kr_ref, vr_ref, o_ref, ks_ref, vs_ref):
    per_dev = q_ref.shape[0] // BLOCK
    sel = ks_ref.shape[0] // BLOCK
    remote_count = kr_ref.shape[0] // BLOCK

    def body(i, carry):
        row = pl.multiple_of(i * BLOCK, BLOCK)
        for j in range(sel):
            idx = tbl_ref[i * sel + j]
            near = pl.multiple_of(jnp.minimum(idx, per_dev - 1) * BLOCK, BLOCK)
            far = pl.multiple_of(jnp.clip(idx - per_dev, 0, remote_count - 1) * BLOCK, BLOCK)
            is_near = idx < per_dev
            ks_ref[j * BLOCK:(j + 1) * BLOCK, :] = jnp.where(
                is_near, k_ref[pl.ds(near, BLOCK), :], kr_ref[pl.ds(far, BLOCK), :]
            )
            vs_ref[j * BLOCK:(j + 1) * BLOCK, :] = jnp.where(
                is_near, v_ref[pl.ds(near, BLOCK), :], vr_ref[pl.ds(far, BLOCK), :]
            )
        s = _scores(q_ref[pl.ds(row, BLOCK), :], ks_ref[...])
        running = jnp.max(s, axis=1, keepdims=True)
        weights = jnp.exp(s - running)
        totals = jnp.sum(weights, axis=1, keepdims=True)
        weighted = jnp.dot(
            weights.astype(jnp.bfloat16), vs_ref[...], preferred_element_type=jnp.float32
        )
        o_ref[pl.ds(row, BLOCK), :] = (weighted / totals).astype(o_ref.dtype)
        return carry

    lax.fori_loop(0, per_dev, body, 0)


def sparse_attention(tbl, queries, keys, values, far_keys, far_values, sel, head_lo, heads):
    rows = queries.shape[0]
    near_rows = keys.shape[0]
    far_rows = far_keys.shape[0]

    def column(h, t):
        return (0, h + head_lo)

    return pl.pallas_call(
        sparse_kernel,
        out_shape=jax.ShapeDtypeStruct((rows, heads * HD), jnp.bfloat16),
        grid_spec=pltpu.PrefetchScalarGridSpec(
            num_scalar_prefetch=1,
            grid=(heads,),
            in_specs=[
                pl.BlockSpec((rows, HD), column),
                pl.BlockSpec((near_rows, HD), column),
                pl.BlockSpec((near_rows, HD), column),
                pl.BlockSpec((far_rows, HD), column),
                pl.BlockSpec((far_rows, HD), column),
            ],
            out_specs=pl.BlockSpec((rows, HD), lambda h, t: (0, h)),
            scratch_shapes=[
                pltpu.VMEM((sel * BLOCK, HD), jnp.bfloat16),
                pltpu.VMEM((sel * BLOCK, HD), jnp.bfloat16),
            ],
        ),
    )(tbl, queries, keys, values, far_keys, far_values)


def draft_kernel(q_ref, k_ref, v_ref, o_ref):
    s = _scores(q_ref[...], k_ref[...])
    running = jnp.max(s, axis=1, keepdims=True)
    weights = jnp.exp(s - running)
    totals = jnp.sum(weights, axis=1, keepdims=True)
    weighted = jnp.dot(weights.astype(jnp.bfloat16), v_ref[...], preferred_element_type=jnp.float32)
    o_ref[...] = (weighted / totals).astype(o_ref.dtype)


def draft_attention(queries, keys, values):
    rows, width = queries.shape
    heads = width // HD
    key_rows = keys.shape[0]
    tile = min(DRAFT_ROWS, rows)
    return pl.pallas_call(
        draft_kernel,
        out_shape=jax.ShapeDtypeStruct((rows, width), jnp.bfloat16),
        grid=(heads, rows // tile),
        in_specs=[
            pl.BlockSpec((tile, HD), lambda h, r: (r, h)),
            pl.BlockSpec((key_rows, HD), lambda h, r: (0, h)),
            pl.BlockSpec((key_rows, HD), lambda h, r: (0, h)),
        ],
        out_specs=pl.BlockSpec((tile, HD), lambda h, r: (r, h)),
    )(queries, keys, values)


def on_device(query_in, key_in, value_in, block_lists):
    key_rows = lax.all_to_all(key_in, "head", split_axis=1, concat_axis=0, tiled=True)
    value_rows = lax.all_to_all(value_in, "head", split_axis=1, concat_axis=0, tiled=True)
    queries = lax.all_to_all(query_in, "head", split_axis=1, concat_axis=0, tiled=True)
    seq_rows, width = queries.shape

    draft_keys = lax.all_gather(pool_tokens(key_rows), "seq", axis=0, tiled=True)
    draft_values = lax.all_gather(pool_tokens(value_rows), "seq", axis=0, tiled=True)

    seq_count = lax.axis_size("seq")
    seq_index = lax.axis_index("seq")
    per_dev = seq_rows // BLOCK
    block_total, select_count = block_lists.shape
    block_ids = jnp.arange(block_total, dtype=jnp.int32)
    touched = jnp.any(block_lists[:, :, None] == block_ids[None, None, :], axis=1)
    needed = jnp.any(touched.reshape(seq_count, per_dev, seq_count, per_dev), axis=1)
    slot_rank = jnp.cumsum(needed.astype(jnp.int32), axis=2) - 1
    send_need = lax.dynamic_index_in_dim(needed, seq_index, axis=1, keepdims=False)
    send_rank = lax.dynamic_index_in_dim(slot_rank, seq_index, axis=1, keepdims=False)
    slot_hit = send_need[:, None, :] & (
        send_rank[:, None, :] == jnp.arange(CAP, dtype=jnp.int32)[None, :, None]
    )
    send_idx = jnp.sum(
        jnp.where(slot_hit, jnp.arange(per_dev, dtype=jnp.int32)[None, None, :], 0), axis=2
    ).reshape(-1)
    def exchange(rows):
        blocks = jnp.take(rows.reshape(per_dev, BLOCK, width), send_idx, axis=0)
        outgoing = blocks.reshape(seq_count, CAP, BLOCK, width)
        arrivals = []
        for shift in range(1, seq_count):
            parcel = lax.dynamic_index_in_dim(
                outgoing, (seq_index + shift) % seq_count, axis=0, keepdims=False
            )
            arrivals.append(
                lax.ppermute(
                    parcel, "seq", [(i, (i + shift) % seq_count) for i in range(seq_count)]
                )
            )
        return jnp.stack(arrivals, axis=0).reshape((seq_count - 1) * CAP * BLOCK, width)

    remote_keys = exchange(key_rows)
    remote_values = exchange(value_rows)

    own_lists = lax.dynamic_slice_in_dim(block_lists, seq_index * per_dev, per_dev, 0)
    owners = own_lists // per_dev
    within = own_lists % per_dev
    own_rank = lax.dynamic_index_in_dim(slot_rank, seq_index, axis=0, keepdims=False)
    ranks_used = jnp.clip(own_rank[owners, within], 0, CAP - 1)
    distance = (seq_index - owners) % seq_count
    joint_pos = jnp.where(distance == 0, within, per_dev + (distance - 1) * CAP + ranks_used)
    table = jnp.clip(joint_pos, 0, per_dev + (seq_count - 1) * CAP - 1).reshape(-1).astype(jnp.int32)

    heads = width // HD
    first = max(1, heads // 2)
    pieces = []
    for head_lo, count in ((0, first), (first, heads - first)):
        if count == 0:
            continue
        rows_part = sparse_attention(
            table, queries, key_rows, value_rows, remote_keys, remote_values,
            select_count, head_lo, count,
        )
        back = lax.all_to_all(rows_part, "head", split_axis=0, concat_axis=1, tiled=True)
        pieces.append(back.reshape(back.shape[0], -1, count * HD))
    sparse_out = jnp.concatenate(pieces, axis=2).reshape(pieces[0].shape[0], -1)

    draft_out = draft_attention(pool_tokens(queries), draft_keys, draft_values)
    return (draft_out, sparse_out)


def solution(mesh):
    return jax.shard_map(
        on_device,
        mesh=mesh,
        in_specs=(
            P(("groups", "seq", "head"), None),
            P(("groups", "seq", "head"), None),
            P(("groups", "seq", "head"), None),
            P("groups", None),
        ),
        out_specs=(P(("groups", "seq"), "head"), P(("groups", "seq", "head"), None)),
        check_vma=False,
    )
```

```python
import jax
import jax.numpy as jnp
from jax import lax
from jax.experimental import pallas as pl
from jax.experimental.pallas import tpu as pltpu
from jax.sharding import PartitionSpec as P

HD = 128
BLOCK = 128
POOL = 4
CAP = 2
SCALE = HD ** (-0.5)
DRAFT_ROWS = 128
PAIR = 2
EXP2_SCALE = SCALE * 1.4426950408889634


def pool_tokens(matrix):
    grouped = matrix.astype(jnp.float32).reshape(matrix.shape[0] // POOL, POOL, matrix.shape[1])
    return (grouped.sum(axis=1) * POOL ** (-0.5)).astype(jnp.bfloat16)


def sparse_kernel(tbl_ref, q_ref, *refs):
    near_k, near_v = refs[0], refs[1]
    far_count = (len(refs) - 5) // 2
    far_k = refs[2:2 + far_count]
    far_v = refs[2 + far_count:2 + 2 * far_count]
    o_ref, kall_ref, vall_ref = refs[2 + 2 * far_count:]
    per_dev = q_ref.shape[0] // BLOCK
    sel = tbl_ref.shape[0] // per_dev
    near_rows = near_k.shape[0]
    kall_ref[0:near_rows, :] = near_k[...]
    vall_ref[0:near_rows, :] = near_v[...]
    offset = near_rows
    for kr, vr in zip(far_k, far_v):
        kall_ref[offset:offset + kr.shape[0], :] = kr[...]
        vall_ref[offset:offset + vr.shape[0], :] = vr[...]
        offset += kr.shape[0]
    last = offset // BLOCK - 1

    def one_block(i):
        row = pl.multiple_of(i * BLOCK, BLOCK)
        keys = []
        values = []
        for j in range(sel):
            start = pl.multiple_of(jnp.clip(tbl_ref[i * sel + j], 0, last) * BLOCK, BLOCK)
            keys.append(kall_ref[pl.ds(start, BLOCK), :])
            values.append(vall_ref[pl.ds(start, BLOCK), :])
        raw = lax.dot_general(
            q_ref[pl.ds(row, BLOCK), :], jnp.concatenate(keys, axis=0),
            (((1,), (1,)), ((), ())), preferred_element_type=jnp.float32,
        )
        running = jnp.max(raw, axis=1, keepdims=True)
        weights = jnp.exp2((raw - running) * EXP2_SCALE)
        totals = jnp.sum(weights, axis=1, keepdims=True)
        weighted = jnp.dot(
            weights.astype(jnp.bfloat16), jnp.concatenate(values, axis=0),
            preferred_element_type=jnp.float32,
        )
        o_ref[pl.ds(row, BLOCK), :] = (weighted / totals).astype(o_ref.dtype)

    def body(i, carry):
        for lane in range(PAIR):
            one_block(i * PAIR + lane)
        return carry

    lax.fori_loop(0, per_dev // PAIR, body, 0)
    for i in range(per_dev - per_dev % PAIR, per_dev):
        one_block(i)


def sparse_attention(tbl, queries, keys, values, far_keys, far_values, head_lo, heads):
    rows = queries.shape[0]

    def column(h, t):
        return (0, h + head_lo)

    operands = [queries, keys, values] + list(far_keys) + list(far_values)
    total_rows = keys.shape[0] + sum(k.shape[0] for k in far_keys)
    return pl.pallas_call(
        sparse_kernel,
        out_shape=jax.ShapeDtypeStruct((rows, heads * HD), jnp.bfloat16),
        grid_spec=pltpu.PrefetchScalarGridSpec(
            num_scalar_prefetch=1,
            grid=(heads,),
            in_specs=[pl.BlockSpec((x.shape[0], HD), column) for x in operands],
            out_specs=pl.BlockSpec((rows, HD), lambda h, t: (0, h)),
            scratch_shapes=[
                pltpu.VMEM((total_rows, HD), jnp.bfloat16),
                pltpu.VMEM((total_rows, HD), jnp.bfloat16),
            ],
        ),
    )(tbl, *operands)


def draft_kernel(q_ref, k_ref, v_ref, o_ref):
    raw = lax.dot_general(
        q_ref[...], k_ref[...], (((1,), (1,)), ((), ())), preferred_element_type=jnp.float32
    )
    running = jnp.max(raw, axis=1, keepdims=True)
    weights = jnp.exp2((raw - running) * EXP2_SCALE)
    totals = jnp.sum(weights, axis=1, keepdims=True)
    weighted = jnp.dot(weights.astype(jnp.bfloat16), v_ref[...], preferred_element_type=jnp.float32)
    o_ref[...] = (weighted / totals).astype(o_ref.dtype)


def draft_attention(queries, keys, values):
    rows, width = queries.shape
    heads = width // HD
    key_rows = keys.shape[0]
    tile = min(DRAFT_ROWS, rows)
    return pl.pallas_call(
        draft_kernel,
        out_shape=jax.ShapeDtypeStruct((rows, width), jnp.bfloat16),
        grid=(heads, rows // tile),
        in_specs=[
            pl.BlockSpec((tile, HD), lambda h, r: (r, h)),
            pl.BlockSpec((key_rows, HD), lambda h, r: (0, h)),
            pl.BlockSpec((key_rows, HD), lambda h, r: (0, h)),
        ],
        out_specs=pl.BlockSpec((tile, HD), lambda h, r: (r, h)),
    )(queries, keys, values)


def on_device(query_in, key_in, value_in, block_lists):
    key_rows = lax.all_to_all(key_in, "head", split_axis=1, concat_axis=0, tiled=True)
    value_rows = lax.all_to_all(value_in, "head", split_axis=1, concat_axis=0, tiled=True)
    queries = lax.all_to_all(query_in, "head", split_axis=1, concat_axis=0, tiled=True)
    seq_rows, width = queries.shape

    draft_keys = lax.all_gather(pool_tokens(key_rows), "seq", axis=0, tiled=True)
    draft_values = lax.all_gather(pool_tokens(value_rows), "seq", axis=0, tiled=True)

    seq_count = lax.axis_size("seq")
    seq_index = lax.axis_index("seq")
    per_dev = seq_rows // BLOCK
    block_total, select_count = block_lists.shape
    block_ids = jnp.arange(block_total, dtype=jnp.int32)
    touched = jnp.any(block_lists[:, :, None] == block_ids[None, None, :], axis=1)
    needed = jnp.any(touched.reshape(seq_count, per_dev, seq_count, per_dev), axis=1)
    slot_rank = jnp.cumsum(needed.astype(jnp.int32), axis=2) - 1
    send_need = lax.dynamic_index_in_dim(needed, seq_index, axis=1, keepdims=False)
    send_rank = lax.dynamic_index_in_dim(slot_rank, seq_index, axis=1, keepdims=False)
    slot_hit = send_need[:, None, :] & (
        send_rank[:, None, :] == jnp.arange(CAP, dtype=jnp.int32)[None, :, None]
    )
    send_idx = jnp.sum(
        jnp.where(slot_hit, jnp.arange(per_dev, dtype=jnp.int32)[None, None, :], 0), axis=2
    ).reshape(-1)
    def exchange(rows):
        blocks = jnp.take(rows.reshape(per_dev, BLOCK, width), send_idx, axis=0)
        outgoing = blocks.reshape(seq_count, CAP, BLOCK, width)
        arrivals = []
        for shift in range(1, seq_count):
            parcel = lax.dynamic_index_in_dim(
                outgoing, (seq_index + shift) % seq_count, axis=0, keepdims=False
            )
            arrivals.append(
                lax.ppermute(
                    parcel, "seq", [(i, (i + shift) % seq_count) for i in range(seq_count)]
                )
            )
        return [a.reshape(CAP * BLOCK, width) for a in arrivals]

    remote_keys = exchange(key_rows)
    remote_values = exchange(value_rows)

    own_lists = lax.dynamic_slice_in_dim(block_lists, seq_index * per_dev, per_dev, 0)
    owners = own_lists // per_dev
    within = own_lists % per_dev
    own_rank = lax.dynamic_index_in_dim(slot_rank, seq_index, axis=0, keepdims=False)
    ranks_used = jnp.clip(own_rank[owners, within], 0, CAP - 1)
    distance = (seq_index - owners) % seq_count
    joint_pos = jnp.where(distance == 0, within, per_dev + (distance - 1) * CAP + ranks_used)
    table = jnp.clip(joint_pos, 0, per_dev + (seq_count - 1) * CAP - 1).reshape(-1).astype(jnp.int32)

    draft_out = draft_attention(pool_tokens(queries), draft_keys, draft_values)
    queries, draft_out = lax.optimization_barrier((queries, draft_out))
    heads = width // HD
    first = max(1, heads // 2)
    pieces = []
    for head_lo, count in ((0, first), (first, heads - first)):
        if count == 0:
            continue
        rows_part = sparse_attention(
            table, queries, key_rows, value_rows, remote_keys, remote_values, head_lo, count,
        )
        back = lax.all_to_all(rows_part, "head", split_axis=0, concat_axis=1, tiled=True)
        pieces.append(back.reshape(back.shape[0], -1, count * HD))
    sparse_out = jnp.concatenate(pieces, axis=2).reshape(pieces[0].shape[0], -1)
    return (draft_out, sparse_out)


def solution(mesh):
    return jax.shard_map(
        on_device,
        mesh=mesh,
        in_specs=(
            P(("groups", "seq", "head"), None),
            P(("groups", "seq", "head"), None),
            P(("groups", "seq", "head"), None),
            P("groups", None),
        ),
        out_specs=(P(("groups", "seq"), "head"), P(("groups", "seq", "head"), None)),
        check_vma=False,
    )
```

```python
import jax
import jax.numpy as jnp
from jax import lax
from jax.experimental import pallas as pl
from jax.experimental.pallas import tpu as pltpu
from jax.sharding import PartitionSpec as P

HD = 128
BLOCK = 128
POOL = 4
CAP = 2
SCALE = HD ** (-0.5)
DRAFT_ROWS = 128
PAIR = 2
EXP2_SCALE = SCALE * 1.4426950408889634


def pool_tokens(matrix):
    grouped = matrix.astype(jnp.float32).reshape(matrix.shape[0] // POOL, POOL, matrix.shape[1])
    return (grouped.sum(axis=1) * POOL ** (-0.5)).astype(jnp.bfloat16)


def sparse_kernel(tbl_ref, q_ref, *refs):
    near_k, near_v = refs[0], refs[1]
    far_count = (len(refs) - 5) // 2
    far_k = refs[2:2 + far_count]
    far_v = refs[2 + far_count:2 + 2 * far_count]
    o_ref, kall_ref, vall_ref = refs[2 + 2 * far_count:]
    per_dev = q_ref.shape[0] // BLOCK
    sel = tbl_ref.shape[0] // per_dev
    near_rows = near_k.shape[0]
    kall_ref[0:near_rows, :] = near_k[...]
    vall_ref[0:near_rows, :] = near_v[...]
    offset = near_rows
    for kr, vr in zip(far_k, far_v):
        kall_ref[offset:offset + kr.shape[0], :] = kr[...]
        vall_ref[offset:offset + vr.shape[0], :] = vr[...]
        offset += kr.shape[0]
    last = offset // BLOCK - 1

    def one_block(i):
        row = pl.multiple_of(i * BLOCK, BLOCK)
        keys = []
        values = []
        for j in range(sel):
            start = pl.multiple_of(jnp.clip(tbl_ref[i * sel + j], 0, last) * BLOCK, BLOCK)
            keys.append(kall_ref[pl.ds(start, BLOCK), :])
            values.append(vall_ref[pl.ds(start, BLOCK), :])
        raw = lax.dot_general(
            q_ref[pl.ds(row, BLOCK), :], jnp.concatenate(keys, axis=0),
            (((1,), (1,)), ((), ())), preferred_element_type=jnp.float32,
        )
        running = jnp.max(raw, axis=1, keepdims=True)
        weights = jnp.exp2((raw - running) * EXP2_SCALE)
        totals = jnp.sum(weights, axis=1, keepdims=True)
        weighted = jnp.dot(
            weights.astype(jnp.bfloat16), jnp.concatenate(values, axis=0),
            preferred_element_type=jnp.float32,
        )
        o_ref[pl.ds(row, BLOCK), :] = (weighted / totals).astype(o_ref.dtype)

    def body(i, carry):
        for lane in range(PAIR):
            one_block(i * PAIR + lane)
        return carry

    lax.fori_loop(0, per_dev // PAIR, body, 0)
    for i in range(per_dev - per_dev % PAIR, per_dev):
        one_block(i)


def sparse_attention(tbl, queries, keys, values, far_keys, far_values, head_lo, heads):
    rows = queries.shape[0]

    def column(h, t):
        return (0, h + head_lo)

    operands = [keys, values] + list(far_keys) + list(far_values)
    total_rows = keys.shape[0] + sum(k.shape[0] for k in far_keys)
    sel = tbl.shape[0] * BLOCK // rows
    cost = pl.CostEstimate(
        flops=4 * rows * sel * BLOCK * HD * heads,
        transcendentals=rows * sel * BLOCK * heads,
        bytes_accessed=2 * HD * heads * (2 * rows + 2 * total_rows),
    )
    return pl.pallas_call(
        sparse_kernel,
        out_shape=jax.ShapeDtypeStruct((rows, heads * HD), jnp.bfloat16),
        cost_estimate=cost,
        grid_spec=pltpu.PrefetchScalarGridSpec(
            num_scalar_prefetch=1,
            grid=(heads,),
            in_specs=[pl.BlockSpec((rows, HD), lambda h, t: (0, h))]
            + [pl.BlockSpec((x.shape[0], HD), column) for x in operands],
            out_specs=pl.BlockSpec((rows, HD), lambda h, t: (0, h)),
            scratch_shapes=[
                pltpu.VMEM((total_rows, HD), jnp.bfloat16),
                pltpu.VMEM((total_rows, HD), jnp.bfloat16),
            ],
        ),
    )(tbl, queries, *operands)


def draft_kernel(q_ref, k_ref, v_ref, o_ref):
    raw = lax.dot_general(
        q_ref[...], k_ref[...], (((1,), (1,)), ((), ())), preferred_element_type=jnp.float32
    )
    running = jnp.max(raw, axis=1, keepdims=True)
    weights = jnp.exp2((raw - running) * EXP2_SCALE)
    totals = jnp.sum(weights, axis=1, keepdims=True)
    weighted = jnp.dot(weights.astype(jnp.bfloat16), v_ref[...], preferred_element_type=jnp.float32)
    o_ref[...] = (weighted / totals).astype(o_ref.dtype)


def draft_attention(queries, keys, values):
    rows, width = queries.shape
    heads = width // HD
    key_rows = keys.shape[0]
    tile = min(DRAFT_ROWS, rows)
    cost = pl.CostEstimate(
        flops=4 * rows * key_rows * HD * heads,
        transcendentals=rows * key_rows * heads,
        bytes_accessed=2 * HD * heads * (2 * rows + 2 * key_rows),
    )
    return pl.pallas_call(
        draft_kernel,
        out_shape=jax.ShapeDtypeStruct((rows, width), jnp.bfloat16),
        cost_estimate=cost,
        grid=(heads, rows // tile),
        in_specs=[
            pl.BlockSpec((tile, HD), lambda h, r: (r, h)),
            pl.BlockSpec((key_rows, HD), lambda h, r: (0, h)),
            pl.BlockSpec((key_rows, HD), lambda h, r: (0, h)),
        ],
        out_specs=pl.BlockSpec((tile, HD), lambda h, r: (r, h)),
    )(queries, keys, values)


def on_device(query_in, key_in, value_in, block_lists):
    key_rows = lax.all_to_all(key_in, "head", split_axis=1, concat_axis=0, tiled=True)
    value_rows = lax.all_to_all(value_in, "head", split_axis=1, concat_axis=0, tiled=True)
    seq_rows, width = key_rows.shape
    head_count = lax.axis_size("head")
    heads = width // HD
    first = max(1, heads // 2)
    spans = [(lo, n) for lo, n in ((0, first), (first, heads - first)) if n > 0]
    grouped_q = query_in.reshape(query_in.shape[0], head_count, width)
    query_parts = [
        lax.all_to_all(
            grouped_q[:, :, lo * HD:(lo + n) * HD].reshape(query_in.shape[0], -1),
            "head", split_axis=1, concat_axis=0, tiled=True,
        )
        for lo, n in spans
    ]

    draft_keys = lax.all_gather(pool_tokens(key_rows), "seq", axis=0, tiled=True)
    draft_values = lax.all_gather(pool_tokens(value_rows), "seq", axis=0, tiled=True)

    seq_count = lax.axis_size("seq")
    seq_index = lax.axis_index("seq")
    per_dev = seq_rows // BLOCK
    block_total, select_count = block_lists.shape
    block_ids = jnp.arange(block_total, dtype=jnp.int32)
    touched = jnp.any(block_lists[:, :, None] == block_ids[None, None, :], axis=1)
    needed = jnp.any(touched.reshape(seq_count, per_dev, seq_count, per_dev), axis=1)
    slot_rank = jnp.cumsum(needed.astype(jnp.int32), axis=2) - 1
    send_need = lax.dynamic_index_in_dim(needed, seq_index, axis=1, keepdims=False)
    send_rank = lax.dynamic_index_in_dim(slot_rank, seq_index, axis=1, keepdims=False)
    slot_hit = send_need[:, None, :] & (
        send_rank[:, None, :] == jnp.arange(CAP, dtype=jnp.int32)[None, :, None]
    )
    send_idx = jnp.sum(
        jnp.where(slot_hit, jnp.arange(per_dev, dtype=jnp.int32)[None, None, :], 0), axis=2
    ).reshape(-1)
    def exchange(rows):
        blocks = jnp.take(rows.reshape(per_dev, BLOCK, width), send_idx, axis=0)
        outgoing = blocks.reshape(seq_count, CAP, BLOCK, width)
        arrivals = []
        for shift in range(1, seq_count):
            parcel = lax.dynamic_index_in_dim(
                outgoing, (seq_index + shift) % seq_count, axis=0, keepdims=False
            )
            arrivals.append(
                lax.ppermute(
                    parcel, "seq", [(i, (i + shift) % seq_count) for i in range(seq_count)]
                )
            )
        return [a.reshape(CAP * BLOCK, width) for a in arrivals]

    remote_keys = exchange(key_rows)
    remote_values = exchange(value_rows)

    own_lists = lax.dynamic_slice_in_dim(block_lists, seq_index * per_dev, per_dev, 0)
    owners = own_lists // per_dev
    within = own_lists % per_dev
    own_rank = lax.dynamic_index_in_dim(slot_rank, seq_index, axis=0, keepdims=False)
    ranks_used = jnp.clip(own_rank[owners, within], 0, CAP - 1)
    distance = (seq_index - owners) % seq_count
    joint_pos = jnp.where(distance == 0, within, per_dev + (distance - 1) * CAP + ranks_used)
    table = jnp.clip(joint_pos, 0, per_dev + (seq_count - 1) * CAP - 1).reshape(-1).astype(jnp.int32)

    pooled = None
    pieces = []
    for index, ((head_lo, count), queries) in enumerate(zip(spans, query_parts)):
        rows_part = sparse_attention(
            table, queries, key_rows, value_rows, remote_keys, remote_values, head_lo, count,
        )
        if index == len(spans) - 1:
            pooled = jnp.concatenate([pool_tokens(q) for q in query_parts], axis=1)
            rows_part, pooled, draft_keys, draft_values = lax.optimization_barrier(
                (rows_part, pooled, draft_keys, draft_values)
            )
        back = lax.all_to_all(rows_part, "head", split_axis=0, concat_axis=1, tiled=True)
        pieces.append(back.reshape(back.shape[0], -1, count * HD))
    sparse_out = jnp.concatenate(pieces, axis=2).reshape(pieces[0].shape[0], -1)
    draft_out = draft_attention(pooled, draft_keys, draft_values)
    return (draft_out, sparse_out)


def solution(mesh):
    return jax.shard_map(
        on_device,
        mesh=mesh,
        in_specs=(
            P(("groups", "seq", "head"), None),
            P(("groups", "seq", "head"), None),
            P(("groups", "seq", "head"), None),
            P("groups", None),
        ),
        out_specs=(P(("groups", "seq"), "head"), P(("groups", "seq", "head"), None)),
        check_vma=False,
    )
```

```python
import jax
import jax.numpy as jnp
from jax import lax
from jax.experimental import pallas as pl
from jax.experimental.pallas import tpu as pltpu
from jax.sharding import PartitionSpec as P

HD = 128
BLOCK = 128
POOL = 4
CAP = 2
SCALE = HD ** (-0.5)
DRAFT_ROWS = 128
PAIR = 2
EXP2_SCALE = SCALE * 1.4426950408889634


def pool_tokens(matrix):
    grouped = matrix.astype(jnp.float32).reshape(matrix.shape[0] // POOL, POOL, matrix.shape[1])
    return (grouped.sum(axis=1) * POOL ** (-0.5)).astype(jnp.bfloat16)


def sparse_kernel(tbl_ref, q_ref, *refs):
    near_k, near_v = refs[0], refs[1]
    far_count = (len(refs) - 5) // 2
    far_k = refs[2:2 + far_count]
    far_v = refs[2 + far_count:2 + 2 * far_count]
    o_ref, kall_ref, vall_ref = refs[2 + 2 * far_count:]
    per_dev = q_ref.shape[0] // BLOCK
    sel = tbl_ref.shape[0] // per_dev
    near_rows = near_k.shape[0]
    kall_ref[0:near_rows, :] = near_k[...]
    vall_ref[0:near_rows, :] = near_v[...]
    offset = near_rows
    for kr, vr in zip(far_k, far_v):
        kall_ref[offset:offset + kr.shape[0], :] = kr[...]
        vall_ref[offset:offset + vr.shape[0], :] = vr[...]
        offset += kr.shape[0]
    last = offset // BLOCK - 1

    def one_block(i):
        row = pl.multiple_of(i * BLOCK, BLOCK)
        keys = []
        values = []
        for j in range(sel):
            start = pl.multiple_of(jnp.clip(tbl_ref[i * sel + j], 0, last) * BLOCK, BLOCK)
            keys.append(kall_ref[pl.ds(start, BLOCK), :])
            values.append(vall_ref[pl.ds(start, BLOCK), :])
        raw = lax.dot_general(
            q_ref[pl.ds(row, BLOCK), :], jnp.concatenate(keys, axis=0),
            (((1,), (1,)), ((), ())), preferred_element_type=jnp.float32,
        )
        running = jnp.max(raw, axis=1, keepdims=True)
        weights = jnp.exp2((raw - running) * EXP2_SCALE)
        totals = jnp.sum(weights, axis=1, keepdims=True)
        weighted = jnp.dot(
            weights.astype(jnp.bfloat16), jnp.concatenate(values, axis=0),
            preferred_element_type=jnp.float32,
        )
        o_ref[pl.ds(row, BLOCK), :] = (weighted / totals).astype(o_ref.dtype)

    def body(i, carry):
        for lane in range(PAIR):
            one_block(i * PAIR + lane)
        return carry

    lax.fori_loop(0, per_dev // PAIR, body, 0)
    for i in range(per_dev - per_dev % PAIR, per_dev):
        one_block(i)


def sparse_attention(tbl, queries, keys, values, far_keys, far_values, head_lo, heads):
    rows = queries.shape[0]

    def column(h, t):
        return (0, h + head_lo)

    operands = [keys, values] + list(far_keys) + list(far_values)
    total_rows = keys.shape[0] + sum(k.shape[0] for k in far_keys)
    sel = tbl.shape[0] * BLOCK // rows
    cost = pl.CostEstimate(
        flops=4 * rows * sel * BLOCK * HD * heads,
        transcendentals=rows * sel * BLOCK * heads,
        bytes_accessed=2 * HD * heads * (2 * rows + 2 * total_rows),
    )
    return pl.pallas_call(
        sparse_kernel,
        out_shape=jax.ShapeDtypeStruct((rows, heads * HD), jnp.bfloat16),
        cost_estimate=cost,
        grid_spec=pltpu.PrefetchScalarGridSpec(
            num_scalar_prefetch=1,
            grid=(heads,),
            in_specs=[pl.BlockSpec((rows, HD), lambda h, t: (0, h))]
            + [pl.BlockSpec((x.shape[0], HD), column) for x in operands],
            out_specs=pl.BlockSpec((rows, HD), lambda h, t: (0, h)),
            scratch_shapes=[
                pltpu.VMEM((total_rows, HD), jnp.bfloat16),
                pltpu.VMEM((total_rows, HD), jnp.bfloat16),
            ],
        ),
    )(tbl, queries, *operands)


def draft_kernel(q_ref, k_ref, v_ref, o_ref):
    raw = lax.dot_general(
        q_ref[...], k_ref[...], (((1,), (1,)), ((), ())), preferred_element_type=jnp.float32
    )
    running = jnp.max(raw, axis=1, keepdims=True)
    weights = jnp.exp2((raw - running) * EXP2_SCALE)
    totals = jnp.sum(weights, axis=1, keepdims=True)
    weighted = jnp.dot(weights.astype(jnp.bfloat16), v_ref[...], preferred_element_type=jnp.float32)
    o_ref[...] = (weighted / totals).astype(o_ref.dtype)


def draft_attention(queries, keys, values):
    rows, width = queries.shape
    heads = width // HD
    key_rows = keys.shape[0]
    tile = min(DRAFT_ROWS, rows)
    cost = pl.CostEstimate(
        flops=4 * rows * key_rows * HD * heads,
        transcendentals=rows * key_rows * heads,
        bytes_accessed=2 * HD * heads * (2 * rows + 2 * key_rows),
    )
    return pl.pallas_call(
        draft_kernel,
        out_shape=jax.ShapeDtypeStruct((rows, width), jnp.bfloat16),
        cost_estimate=cost,
        grid=(heads, rows // tile),
        in_specs=[
            pl.BlockSpec((tile, HD), lambda h, r: (r, h)),
            pl.BlockSpec((key_rows, HD), lambda h, r: (0, h)),
            pl.BlockSpec((key_rows, HD), lambda h, r: (0, h)),
        ],
        out_specs=pl.BlockSpec((tile, HD), lambda h, r: (r, h)),
    )(queries, keys, values)


def on_device(query_in, key_in, value_in, block_lists):
    key_rows = lax.all_to_all(key_in, "head", split_axis=1, concat_axis=0, tiled=True)
    value_rows = lax.all_to_all(value_in, "head", split_axis=1, concat_axis=0, tiled=True)
    seq_rows, width = key_rows.shape
    head_count = lax.axis_size("head")
    heads = width // HD
    first = max(1, heads // 2)
    spans = [(lo, n) for lo, n in ((0, first), (first, heads - first)) if n > 0]
    grouped_q = query_in.reshape(query_in.shape[0], head_count, width)
    query_slices = [
        grouped_q[:, :, lo * HD:(lo + n) * HD].reshape(query_in.shape[0], -1) for lo, n in spans
    ]

    def query_a2a(piece):
        return lax.all_to_all(piece, "head", split_axis=1, concat_axis=0, tiled=True)

    draft_keys = lax.all_gather(pool_tokens(key_rows), "seq", axis=0, tiled=True)
    draft_values = lax.all_gather(pool_tokens(value_rows), "seq", axis=0, tiled=True)

    seq_count = lax.axis_size("seq")
    seq_index = lax.axis_index("seq")
    per_dev = seq_rows // BLOCK
    block_total, select_count = block_lists.shape
    block_ids = jnp.arange(block_total, dtype=jnp.int32)
    touched = jnp.any(block_lists[:, :, None] == block_ids[None, None, :], axis=1)
    needed = jnp.any(touched.reshape(seq_count, per_dev, seq_count, per_dev), axis=1)
    slot_rank = jnp.cumsum(needed.astype(jnp.int32), axis=2) - 1
    send_need = lax.dynamic_index_in_dim(needed, seq_index, axis=1, keepdims=False)
    send_rank = lax.dynamic_index_in_dim(slot_rank, seq_index, axis=1, keepdims=False)
    slot_hit = send_need[:, None, :] & (
        send_rank[:, None, :] == jnp.arange(CAP, dtype=jnp.int32)[None, :, None]
    )
    send_idx = jnp.sum(
        jnp.where(slot_hit, jnp.arange(per_dev, dtype=jnp.int32)[None, None, :], 0), axis=2
    ).reshape(-1)
    def exchange(rows):
        blocks = jnp.take(rows.reshape(per_dev, BLOCK, width), send_idx, axis=0)
        outgoing = blocks.reshape(seq_count, CAP, BLOCK, width)
        arrivals = []
        for shift in range(1, seq_count):
            parcel = lax.dynamic_index_in_dim(
                outgoing, (seq_index + shift) % seq_count, axis=0, keepdims=False
            )
            arrivals.append(
                lax.ppermute(
                    parcel, "seq", [(i, (i + shift) % seq_count) for i in range(seq_count)]
                )
            )
        return [a.reshape(CAP * BLOCK, width) for a in arrivals]

    remote_keys = exchange(key_rows)
    remote_values = exchange(value_rows)
    query_parts = [query_a2a(query_slices[0])]
    later, remote_keys, remote_values = lax.optimization_barrier(
        (query_slices[1:], remote_keys, remote_values)
    )
    query_parts += [query_a2a(piece) for piece in later]

    own_lists = lax.dynamic_slice_in_dim(block_lists, seq_index * per_dev, per_dev, 0)
    owners = own_lists // per_dev
    within = own_lists % per_dev
    own_rank = lax.dynamic_index_in_dim(slot_rank, seq_index, axis=0, keepdims=False)
    ranks_used = jnp.clip(own_rank[owners, within], 0, CAP - 1)
    distance = (seq_index - owners) % seq_count
    joint_pos = jnp.where(distance == 0, within, per_dev + (distance - 1) * CAP + ranks_used)
    table = jnp.clip(joint_pos, 0, per_dev + (seq_count - 1) * CAP - 1).reshape(-1).astype(jnp.int32)

    pooled = None
    pieces = []
    for index, ((head_lo, count), queries) in enumerate(zip(spans, query_parts)):
        rows_part = sparse_attention(
            table, queries, key_rows, value_rows, remote_keys, remote_values, head_lo, count,
        )
        if index == len(spans) - 1:
            pooled = jnp.concatenate([pool_tokens(q) for q in query_parts], axis=1)
            rows_part, pooled, draft_keys, draft_values = lax.optimization_barrier(
                (rows_part, pooled, draft_keys, draft_values)
            )
        back = lax.all_to_all(rows_part, "head", split_axis=0, concat_axis=1, tiled=True)
        pieces.append(back.reshape(back.shape[0], -1, count * HD))
    sparse_out = jnp.concatenate(pieces, axis=2).reshape(pieces[0].shape[0], -1)
    draft_out = draft_attention(pooled, draft_keys, draft_values)
    return (draft_out, sparse_out)


def solution(mesh):
    return jax.shard_map(
        on_device,
        mesh=mesh,
        in_specs=(
            P(("groups", "seq", "head"), None),
            P(("groups", "seq", "head"), None),
            P(("groups", "seq", "head"), None),
            P("groups", None),
        ),
        out_specs=(P(("groups", "seq"), "head"), P(("groups", "seq", "head"), None)),
        check_vma=False,
    )
```

```python
import jax
import jax.numpy as jnp
from jax import lax
from jax.experimental import pallas as pl
from jax.experimental.pallas import tpu as pltpu
from jax.sharding import PartitionSpec as P

HD = 128
BLOCK = 128
POOL = 4
CAP = 2
SCALE = HD ** (-0.5)
DRAFT_ROWS = 128
PAIR = 2
EXP2_SCALE = SCALE * 1.4426950408889634


def pool_tokens(matrix):
    grouped = matrix.astype(jnp.float32).reshape(matrix.shape[0] // POOL, POOL, matrix.shape[1])
    return (grouped.sum(axis=1) * POOL ** (-0.5)).astype(jnp.bfloat16)


def sparse_kernel(tbl_ref, q_ref, *refs):
    near_k, near_v = refs[0], refs[1]
    far_count = (len(refs) - 5) // 2
    far_k = refs[2:2 + far_count]
    far_v = refs[2 + far_count:2 + 2 * far_count]
    o_ref, kall_ref, vall_ref = refs[2 + 2 * far_count:]
    per_dev = q_ref.shape[0] // BLOCK
    sel = tbl_ref.shape[0] // per_dev
    near_rows = near_k.shape[0]
    kall_ref[0:near_rows, :] = near_k[...]
    vall_ref[0:near_rows, :] = near_v[...]
    offset = near_rows
    for kr, vr in zip(far_k, far_v):
        kall_ref[offset:offset + kr.shape[0], :] = kr[...]
        vall_ref[offset:offset + vr.shape[0], :] = vr[...]
        offset += kr.shape[0]
    last = offset // BLOCK - 1

    def one_block(i):
        row = pl.multiple_of(i * BLOCK, BLOCK)
        keys = []
        values = []
        for j in range(sel):
            start = pl.multiple_of(jnp.clip(tbl_ref[i * sel + j], 0, last) * BLOCK, BLOCK)
            keys.append(kall_ref[pl.ds(start, BLOCK), :])
            values.append(vall_ref[pl.ds(start, BLOCK), :])
        raw = lax.dot_general(
            q_ref[pl.ds(row, BLOCK), :], jnp.concatenate(keys, axis=0),
            (((1,), (1,)), ((), ())), preferred_element_type=jnp.float32,
        )
        running = jnp.max(raw, axis=1, keepdims=True)
        weights = jnp.exp2((raw - running) * EXP2_SCALE)
        totals = jnp.sum(weights, axis=1, keepdims=True)
        weighted = jnp.dot(
            weights.astype(jnp.bfloat16), jnp.concatenate(values, axis=0),
            preferred_element_type=jnp.float32,
        )
        o_ref[pl.ds(row, BLOCK), :] = (weighted / totals).astype(o_ref.dtype)

    def body(i, carry):
        for lane in range(PAIR):
            one_block(i * PAIR + lane)
        return carry

    lax.fori_loop(0, per_dev // PAIR, body, 0)
    for i in range(per_dev - per_dev % PAIR, per_dev):
        one_block(i)


def sparse_attention(tbl, queries, keys, values, far_keys, far_values, head_lo, heads):
    rows = queries.shape[0]

    def column(h, t):
        return (0, h + head_lo)

    operands = [keys, values] + list(far_keys) + list(far_values)
    total_rows = keys.shape[0] + sum(k.shape[0] for k in far_keys)
    sel = tbl.shape[0] * BLOCK // rows
    cost = pl.CostEstimate(
        flops=4 * rows * sel * BLOCK * HD * heads,
        transcendentals=rows * sel * BLOCK * heads,
        bytes_accessed=2 * HD * heads * (2 * rows + 2 * total_rows),
    )
    return pl.pallas_call(
        sparse_kernel,
        out_shape=jax.ShapeDtypeStruct((rows, heads * HD), jnp.bfloat16),
        cost_estimate=cost,
        grid_spec=pltpu.PrefetchScalarGridSpec(
            num_scalar_prefetch=1,
            grid=(heads,),
            in_specs=[pl.BlockSpec((rows, HD), lambda h, t: (0, h))]
            + [pl.BlockSpec((x.shape[0], HD), column) for x in operands],
            out_specs=pl.BlockSpec((rows, HD), lambda h, t: (0, h)),
            scratch_shapes=[
                pltpu.VMEM((total_rows, HD), jnp.bfloat16),
                pltpu.VMEM((total_rows, HD), jnp.bfloat16),
            ],
        ),
    )(tbl, queries, *operands)


def draft_kernel(q_ref, k_ref, v_ref, o_ref):
    tile = o_ref.shape[0]
    token = lax.broadcasted_iota(jnp.int32, (tile, tile * POOL), 1)
    draft = lax.broadcasted_iota(jnp.int32, (tile, tile * POOL), 0)
    pooling = jnp.where(token // POOL == draft, POOL ** (-0.5), 0.0).astype(jnp.bfloat16)
    pooled = jnp.dot(pooling, q_ref[...], preferred_element_type=jnp.float32).astype(jnp.bfloat16)
    raw = lax.dot_general(
        pooled, k_ref[...], (((1,), (1,)), ((), ())), preferred_element_type=jnp.float32
    )
    running = jnp.max(raw, axis=1, keepdims=True)
    weights = jnp.exp2((raw - running) * EXP2_SCALE)
    totals = jnp.sum(weights, axis=1, keepdims=True)
    weighted = jnp.dot(weights.astype(jnp.bfloat16), v_ref[...], preferred_element_type=jnp.float32)
    o_ref[...] = (weighted / totals).astype(o_ref.dtype)


def draft_attention(queries, keys, values, head_lo):
    token_rows, width = queries.shape
    rows = token_rows // POOL
    heads = width // HD
    key_rows = keys.shape[0]
    tile = min(DRAFT_ROWS, rows)
    cost = pl.CostEstimate(
        flops=4 * rows * key_rows * HD * heads + 2 * rows * tile * POOL * HD * heads,
        transcendentals=rows * key_rows * heads,
        bytes_accessed=2 * HD * heads * (token_rows + rows + 2 * key_rows),
    )
    return pl.pallas_call(
        draft_kernel,
        out_shape=jax.ShapeDtypeStruct((rows, width), jnp.bfloat16),
        cost_estimate=cost,
        grid=(heads, rows // tile),
        in_specs=[
            pl.BlockSpec((tile * POOL, HD), lambda h, r: (r, h)),
            pl.BlockSpec((key_rows, HD), lambda h, r: (0, h + head_lo)),
            pl.BlockSpec((key_rows, HD), lambda h, r: (0, h + head_lo)),
        ],
        out_specs=pl.BlockSpec((tile, HD), lambda h, r: (r, h)),
    )(queries, keys, values)


def on_device(query_in, key_in, value_in, block_lists):
    key_rows = lax.all_to_all(key_in, "head", split_axis=1, concat_axis=0, tiled=True)
    value_rows = lax.all_to_all(value_in, "head", split_axis=1, concat_axis=0, tiled=True)
    seq_rows, width = key_rows.shape
    head_count = lax.axis_size("head")
    heads = width // HD
    first = max(1, heads // 2)
    spans = [(lo, n) for lo, n in ((0, first), (first, heads - first)) if n > 0]
    grouped_q = query_in.reshape(query_in.shape[0], head_count, width)
    query_slices = [
        grouped_q[:, :, lo * HD:(lo + n) * HD].reshape(query_in.shape[0], -1) for lo, n in spans
    ]

    def query_a2a(piece):
        return lax.all_to_all(piece, "head", split_axis=1, concat_axis=0, tiled=True)

    draft_keys = lax.all_gather(pool_tokens(key_rows), "seq", axis=0, tiled=True)
    draft_values = lax.all_gather(pool_tokens(value_rows), "seq", axis=0, tiled=True)

    seq_count = lax.axis_size("seq")
    seq_index = lax.axis_index("seq")
    per_dev = seq_rows // BLOCK
    block_total, select_count = block_lists.shape
    block_ids = jnp.arange(block_total, dtype=jnp.int32)
    touched = jnp.any(block_lists[:, :, None] == block_ids[None, None, :], axis=1)
    needed = jnp.any(touched.reshape(seq_count, per_dev, seq_count, per_dev), axis=1)
    slot_rank = jnp.cumsum(needed.astype(jnp.int32), axis=2) - 1
    send_need = lax.dynamic_index_in_dim(needed, seq_index, axis=1, keepdims=False)
    send_rank = lax.dynamic_index_in_dim(slot_rank, seq_index, axis=1, keepdims=False)
    slot_hit = send_need[:, None, :] & (
        send_rank[:, None, :] == jnp.arange(CAP, dtype=jnp.int32)[None, :, None]
    )
    send_idx = jnp.sum(
        jnp.where(slot_hit, jnp.arange(per_dev, dtype=jnp.int32)[None, None, :], 0), axis=2
    ).reshape(-1)
    def exchange(rows):
        blocks = jnp.take(rows.reshape(per_dev, BLOCK, width), send_idx, axis=0)
        outgoing = blocks.reshape(seq_count, CAP, BLOCK, width)
        arrivals = []
        for shift in range(1, seq_count):
            parcel = lax.dynamic_index_in_dim(
                outgoing, (seq_index + shift) % seq_count, axis=0, keepdims=False
            )
            arrivals.append(
                lax.ppermute(
                    parcel, "seq", [(i, (i + shift) % seq_count) for i in range(seq_count)]
                )
            )
        return [a.reshape(CAP * BLOCK, width) for a in arrivals]

    remote_keys = exchange(key_rows)
    remote_values = exchange(value_rows)
    query_parts = [query_a2a(query_slices[0])]
    later, remote_keys, remote_values = lax.optimization_barrier(
        (query_slices[1:], remote_keys, remote_values)
    )
    query_parts += [query_a2a(piece) for piece in later]

    own_lists = lax.dynamic_slice_in_dim(block_lists, seq_index * per_dev, per_dev, 0)
    owners = own_lists // per_dev
    within = own_lists % per_dev
    own_rank = lax.dynamic_index_in_dim(slot_rank, seq_index, axis=0, keepdims=False)
    ranks_used = jnp.clip(own_rank[owners, within], 0, CAP - 1)
    distance = (seq_index - owners) % seq_count
    joint_pos = jnp.where(distance == 0, within, per_dev + (distance - 1) * CAP + ranks_used)
    table = jnp.clip(joint_pos, 0, per_dev + (seq_count - 1) * CAP - 1).reshape(-1).astype(jnp.int32)

    pieces = []
    for index, ((head_lo, count), queries) in enumerate(zip(spans, query_parts)):
        rows_part = sparse_attention(
            table, queries, key_rows, value_rows, remote_keys, remote_values, head_lo, count,
        )
        if index == len(spans) - 1:
            rows_part, draft_keys, draft_values = lax.optimization_barrier(
                (rows_part, draft_keys, draft_values)
            )
        back = lax.all_to_all(rows_part, "head", split_axis=0, concat_axis=1, tiled=True)
        pieces.append(back.reshape(back.shape[0], -1, count * HD))
    sparse_out = jnp.concatenate(pieces, axis=2).reshape(pieces[0].shape[0], -1)
    draft_out = jnp.concatenate(
        [
            draft_attention(queries, draft_keys, draft_values, head_lo)
            for (head_lo, count), queries in zip(spans, query_parts)
        ],
        axis=1,
    )
    return (draft_out, sparse_out)


def solution(mesh):
    return jax.shard_map(
        on_device,
        mesh=mesh,
        in_specs=(
            P(("groups", "seq", "head"), None),
            P(("groups", "seq", "head"), None),
            P(("groups", "seq", "head"), None),
            P("groups", None),
        ),
        out_specs=(P(("groups", "seq"), "head"), P(("groups", "seq", "head"), None)),
        check_vma=False,
    )
```

```python
import jax
import jax.numpy as jnp
from jax import lax
from jax.experimental import pallas as pl
from jax.experimental.pallas import tpu as pltpu
from jax.sharding import PartitionSpec as P

HD = 128
BLOCK = 128
POOL = 4
CAP = 2
SCALE = HD ** (-0.5)
DRAFT_ROWS = 128
PAIR = 2
EXP2_SCALE = SCALE * 1.4426950408889634


def pool_tokens(matrix):
    grouped = matrix.astype(jnp.float32).reshape(matrix.shape[0] // POOL, POOL, matrix.shape[1])
    return (grouped.sum(axis=1) * POOL ** (-0.5)).astype(jnp.bfloat16)


def sparse_kernel(tbl_ref, q_ref, *refs):
    near_k, near_v = refs[0], refs[1]
    far_count = (len(refs) - 5) // 2
    far_k = refs[2:2 + far_count]
    far_v = refs[2 + far_count:2 + 2 * far_count]
    o_ref, kall_ref, vall_ref = refs[2 + 2 * far_count:]
    per_dev = q_ref.shape[0] // BLOCK
    sel = tbl_ref.shape[0] // per_dev
    near_rows = near_k.shape[0]
    kall_ref[0:near_rows, :] = near_k[...]
    vall_ref[0:near_rows, :] = near_v[...]
    offset = near_rows
    for kr, vr in zip(far_k, far_v):
        kall_ref[offset:offset + kr.shape[0], :] = kr[...]
        vall_ref[offset:offset + vr.shape[0], :] = vr[...]
        offset += kr.shape[0]
    last = offset // BLOCK - 1

    def one_block(i):
        row = pl.multiple_of(i * BLOCK, BLOCK)
        keys = []
        values = []
        for j in range(sel):
            start = pl.multiple_of(jnp.clip(tbl_ref[i * sel + j], 0, last) * BLOCK, BLOCK)
            keys.append(kall_ref[pl.ds(start, BLOCK), :])
            values.append(vall_ref[pl.ds(start, BLOCK), :])
        raw = lax.dot_general(
            q_ref[pl.ds(row, BLOCK), :], jnp.concatenate(keys, axis=0),
            (((1,), (1,)), ((), ())), preferred_element_type=jnp.float32,
        )
        running = jnp.max(raw, axis=1, keepdims=True)
        weights = jnp.exp2((raw - running) * EXP2_SCALE)
        totals = jnp.sum(weights, axis=1, keepdims=True)
        weighted = jnp.dot(
            weights.astype(jnp.bfloat16), jnp.concatenate(values, axis=0),
            preferred_element_type=jnp.float32,
        )
        o_ref[pl.ds(row, BLOCK), :] = (weighted / totals).astype(o_ref.dtype)

    def body(i, carry):
        for lane in range(PAIR):
            one_block(i * PAIR + lane)
        return carry

    lax.fori_loop(0, per_dev // PAIR, body, 0)
    for i in range(per_dev - per_dev % PAIR, per_dev):
        one_block(i)


def sparse_attention(tbl, queries, keys, values, far_keys, far_values, head_lo, heads):
    rows = queries.shape[0]

    def column(h, t):
        return (0, h + head_lo)

    operands = [keys, values] + list(far_keys) + list(far_values)
    total_rows = keys.shape[0] + sum(k.shape[0] for k in far_keys)
    sel = tbl.shape[0] * BLOCK // rows
    cost = pl.CostEstimate(
        flops=4 * rows * sel * BLOCK * HD * heads,
        transcendentals=rows * sel * BLOCK * heads,
        bytes_accessed=2 * HD * heads * (2 * rows + 2 * total_rows),
    )
    return pl.pallas_call(
        sparse_kernel,
        out_shape=jax.ShapeDtypeStruct((rows, heads * HD), jnp.bfloat16),
        cost_estimate=cost,
        grid_spec=pltpu.PrefetchScalarGridSpec(
            num_scalar_prefetch=1,
            grid=(heads,),
            in_specs=[pl.BlockSpec((rows, HD), lambda h, t: (0, h))]
            + [pl.BlockSpec((x.shape[0], HD), column) for x in operands],
            out_specs=pl.BlockSpec((rows, HD), lambda h, t: (0, h)),
            scratch_shapes=[
                pltpu.VMEM((total_rows, HD), jnp.bfloat16),
                pltpu.VMEM((total_rows, HD), jnp.bfloat16),
            ],
        ),
    )(tbl, queries, *operands)


def draft_kernel(q_ref, k_ref, v_ref, o_ref):
    tile = o_ref.shape[0]
    token = lax.broadcasted_iota(jnp.int32, (tile, tile * POOL), 1)
    draft = lax.broadcasted_iota(jnp.int32, (tile, tile * POOL), 0)
    pooling = jnp.where(token // POOL == draft, POOL ** (-0.5), 0.0).astype(jnp.bfloat16)
    pooled = jnp.dot(pooling, q_ref[...], preferred_element_type=jnp.float32).astype(jnp.bfloat16)
    raw = lax.dot_general(
        pooled, k_ref[...], (((1,), (1,)), ((), ())), preferred_element_type=jnp.float32
    )
    running = jnp.max(raw, axis=1, keepdims=True)
    weights = jnp.exp2((raw - running) * EXP2_SCALE)
    totals = jnp.sum(weights, axis=1, keepdims=True)
    weighted = jnp.dot(weights.astype(jnp.bfloat16), v_ref[...], preferred_element_type=jnp.float32)
    o_ref[...] = (weighted / totals).astype(o_ref.dtype)


def draft_attention(queries, keys, values, head_lo):
    token_rows, width = queries.shape
    rows = token_rows // POOL
    heads = width // HD
    key_rows = keys.shape[0]
    tile = min(DRAFT_ROWS, rows)
    cost = pl.CostEstimate(
        flops=4 * rows * key_rows * HD * heads + 2 * rows * tile * POOL * HD * heads,
        transcendentals=rows * key_rows * heads,
        bytes_accessed=2 * HD * heads * (token_rows + rows + 2 * key_rows),
    )
    return pl.pallas_call(
        draft_kernel,
        out_shape=jax.ShapeDtypeStruct((rows, width), jnp.bfloat16),
        cost_estimate=cost,
        grid=(heads, rows // tile),
        in_specs=[
            pl.BlockSpec((tile * POOL, HD), lambda h, r: (r, h)),
            pl.BlockSpec((key_rows, HD), lambda h, r: (0, h + head_lo)),
            pl.BlockSpec((key_rows, HD), lambda h, r: (0, h + head_lo)),
        ],
        out_specs=pl.BlockSpec((tile, HD), lambda h, r: (r, h)),
    )(queries, keys, values)


def head_permutes(matrix):
    count = lax.axis_size("head")
    me = lax.axis_index("head")
    rows, total = matrix.shape
    chunks = matrix.reshape(rows, count, total // count)
    by_shift = [lax.dynamic_index_in_dim(chunks, me, axis=1, keepdims=False)]
    for shift in range(1, count):
        piece = lax.dynamic_index_in_dim(chunks, (me + shift) % count, axis=1, keepdims=False)
        by_shift.append(
            lax.ppermute(piece, "head", [(i, (i + shift) % count) for i in range(count)])
        )
    stacked = jnp.stack(by_shift, axis=0)
    order = (me - jnp.arange(count, dtype=jnp.int32)) % count
    return jnp.take(stacked, order, axis=0).reshape(count * rows, total // count)


def on_device(query_in, key_in, value_in, block_lists):
    key_rows = lax.all_to_all(key_in, "head", split_axis=1, concat_axis=0, tiled=True)
    value_rows = head_permutes(value_in)
    seq_rows, width = key_rows.shape
    head_count = lax.axis_size("head")
    heads = width // HD
    first = max(1, heads // 2)
    spans = [(lo, n) for lo, n in ((0, first), (first, heads - first)) if n > 0]
    grouped_q = query_in.reshape(query_in.shape[0], head_count, width)
    query_slices = [
        grouped_q[:, :, lo * HD:(lo + n) * HD].reshape(query_in.shape[0], -1) for lo, n in spans
    ]

    def query_a2a(piece):
        return lax.all_to_all(piece, "head", split_axis=1, concat_axis=0, tiled=True)

    draft_keys = lax.all_gather(pool_tokens(key_rows), "seq", axis=0, tiled=True)
    draft_values = lax.all_gather(pool_tokens(value_rows), "seq", axis=0, tiled=True)

    seq_count = lax.axis_size("seq")
    seq_index = lax.axis_index("seq")
    per_dev = seq_rows // BLOCK
    block_total, select_count = block_lists.shape
    block_ids = jnp.arange(block_total, dtype=jnp.int32)
    touched = jnp.any(block_lists[:, :, None] == block_ids[None, None, :], axis=1)
    needed = jnp.any(touched.reshape(seq_count, per_dev, seq_count, per_dev), axis=1)
    slot_rank = jnp.cumsum(needed.astype(jnp.int32), axis=2) - 1
    send_need = lax.dynamic_index_in_dim(needed, seq_index, axis=1, keepdims=False)
    send_rank = lax.dynamic_index_in_dim(slot_rank, seq_index, axis=1, keepdims=False)
    slot_hit = send_need[:, None, :] & (
        send_rank[:, None, :] == jnp.arange(CAP, dtype=jnp.int32)[None, :, None]
    )
    send_idx = jnp.sum(
        jnp.where(slot_hit, jnp.arange(per_dev, dtype=jnp.int32)[None, None, :], 0), axis=2
    ).reshape(-1)
    def exchange(rows):
        blocks = jnp.take(rows.reshape(per_dev, BLOCK, width), send_idx, axis=0)
        outgoing = blocks.reshape(seq_count, CAP, BLOCK, width)
        arrivals = []
        for shift in range(1, seq_count):
            parcel = lax.dynamic_index_in_dim(
                outgoing, (seq_index + shift) % seq_count, axis=0, keepdims=False
            )
            arrivals.append(
                lax.ppermute(
                    parcel, "seq", [(i, (i + shift) % seq_count) for i in range(seq_count)]
                )
            )
        return [a.reshape(CAP * BLOCK, width) for a in arrivals]

    remote_keys = exchange(key_rows)
    remote_values = exchange(value_rows)
    query_parts = [query_a2a(query_slices[0])]
    later, remote_keys, remote_values = lax.optimization_barrier(
        (query_slices[1:], remote_keys, remote_values)
    )
    query_parts += [query_a2a(piece) for piece in later]

    own_lists = lax.dynamic_slice_in_dim(block_lists, seq_index * per_dev, per_dev, 0)
    owners = own_lists // per_dev
    within = own_lists % per_dev
    own_rank = lax.dynamic_index_in_dim(slot_rank, seq_index, axis=0, keepdims=False)
    ranks_used = jnp.clip(own_rank[owners, within], 0, CAP - 1)
    distance = (seq_index - owners) % seq_count
    joint_pos = jnp.where(distance == 0, within, per_dev + (distance - 1) * CAP + ranks_used)
    table = jnp.clip(joint_pos, 0, per_dev + (seq_count - 1) * CAP - 1).reshape(-1).astype(jnp.int32)

    pieces = []
    for index, ((head_lo, count), queries) in enumerate(zip(spans, query_parts)):
        rows_part = sparse_attention(
            table, queries, key_rows, value_rows, remote_keys, remote_values, head_lo, count,
        )
        if index == len(spans) - 1:
            rows_part, draft_keys, draft_values = lax.optimization_barrier(
                (rows_part, draft_keys, draft_values)
            )
        back = lax.all_to_all(rows_part, "head", split_axis=0, concat_axis=1, tiled=True)
        pieces.append(back.reshape(back.shape[0], -1, count * HD))
    sparse_out = jnp.concatenate(pieces, axis=2).reshape(pieces[0].shape[0], -1)
    draft_out = jnp.concatenate(
        [
            draft_attention(queries, draft_keys, draft_values, head_lo)
            for (head_lo, count), queries in zip(spans, query_parts)
        ],
        axis=1,
    )
    return (draft_out, sparse_out)


def solution(mesh):
    return jax.shard_map(
        on_device,
        mesh=mesh,
        in_specs=(
            P(("groups", "seq", "head"), None),
            P(("groups", "seq", "head"), None),
            P(("groups", "seq", "head"), None),
            P("groups", None),
        ),
        out_specs=(P(("groups", "seq"), "head"), P(("groups", "seq", "head"), None)),
        check_vma=False,
    )
```

```python
import jax
import jax.numpy as jnp
from jax import lax
from jax.experimental import pallas as pl
from jax.experimental.pallas import tpu as pltpu
from jax.sharding import PartitionSpec as P

HD = 128
BLOCK = 128
POOL = 4
CAP = 2
SCALE = HD ** (-0.5)
DRAFT_ROWS = 128
PAIR = 2
EXP2_SCALE = SCALE * 1.4426950408889634


def pool_tokens(matrix):
    grouped = matrix.astype(jnp.float32).reshape(matrix.shape[0] // POOL, POOL, matrix.shape[1])
    return (grouped.sum(axis=1) * POOL ** (-0.5)).astype(jnp.bfloat16)


def sparse_kernel(tbl_ref, q_ref, *refs):
    near_k, near_v = refs[0], refs[1]
    far_count = (len(refs) - 5) // 2
    far_k = refs[2:2 + far_count]
    far_v = refs[2 + far_count:2 + 2 * far_count]
    o_ref, kall_ref, vall_ref = refs[2 + 2 * far_count:]
    per_dev = q_ref.shape[0] // BLOCK
    sel = tbl_ref.shape[0] // per_dev
    near_rows = near_k.shape[0]
    kall_ref[0:near_rows, :] = near_k[...]
    vall_ref[0:near_rows, :] = near_v[...]
    offset = near_rows
    for kr, vr in zip(far_k, far_v):
        kall_ref[offset:offset + kr.shape[0], :] = kr[...]
        vall_ref[offset:offset + vr.shape[0], :] = vr[...]
        offset += kr.shape[0]
    last = offset // BLOCK - 1

    def one_block(i):
        row = pl.multiple_of(i * BLOCK, BLOCK)
        keys = []
        values = []
        for j in range(sel):
            start = pl.multiple_of(jnp.clip(tbl_ref[i * sel + j], 0, last) * BLOCK, BLOCK)
            keys.append(kall_ref[pl.ds(start, BLOCK), :])
            values.append(vall_ref[pl.ds(start, BLOCK), :])
        raw = lax.dot_general(
            q_ref[pl.ds(row, BLOCK), :], jnp.concatenate(keys, axis=0),
            (((1,), (1,)), ((), ())), preferred_element_type=jnp.float32,
        )
        running = jnp.max(raw, axis=1, keepdims=True)
        weights = jnp.exp2((raw - running) * EXP2_SCALE)
        totals = jnp.sum(weights, axis=1, keepdims=True)
        weighted = jnp.dot(
            weights.astype(jnp.bfloat16), jnp.concatenate(values, axis=0),
            preferred_element_type=jnp.float32,
        )
        o_ref[pl.ds(row, BLOCK), :] = (weighted / totals).astype(o_ref.dtype)

    def body(i, carry):
        for lane in range(PAIR):
            one_block(i * PAIR + lane)
        return carry

    lax.fori_loop(0, per_dev // PAIR, body, 0)
    for i in range(per_dev - per_dev % PAIR, per_dev):
        one_block(i)


def sparse_attention(tbl, queries, keys, values, far_keys, far_values, head_lo, heads):
    rows = queries.shape[0]

    def column(h, t):
        return (0, h + head_lo)

    operands = [keys, values] + list(far_keys) + list(far_values)
    total_rows = keys.shape[0] + sum(k.shape[0] for k in far_keys)
    sel = tbl.shape[0] * BLOCK // rows
    cost = pl.CostEstimate(
        flops=4 * rows * sel * BLOCK * HD * heads,
        transcendentals=rows * sel * BLOCK * heads,
        bytes_accessed=2 * HD * heads * (2 * rows + 2 * total_rows),
    )
    return pl.pallas_call(
        sparse_kernel,
        out_shape=jax.ShapeDtypeStruct((rows, heads * HD), jnp.bfloat16),
        cost_estimate=cost,
        grid_spec=pltpu.PrefetchScalarGridSpec(
            num_scalar_prefetch=1,
            grid=(heads,),
            in_specs=[pl.BlockSpec((rows, HD), lambda h, t: (0, h))]
            + [pl.BlockSpec((x.shape[0], HD), column) for x in operands],
            out_specs=pl.BlockSpec((rows, HD), lambda h, t: (0, h)),
            scratch_shapes=[
                pltpu.VMEM((total_rows, HD), jnp.bfloat16),
                pltpu.VMEM((total_rows, HD), jnp.bfloat16),
            ],
        ),
    )(tbl, queries, *operands)


def draft_kernel(q_ref, k_ref, v_ref, o_ref):
    tile = o_ref.shape[0]
    token = lax.broadcasted_iota(jnp.int32, (tile, tile * POOL), 1)
    draft = lax.broadcasted_iota(jnp.int32, (tile, tile * POOL), 0)
    pooling = jnp.where(token // POOL == draft, POOL ** (-0.5), 0.0).astype(jnp.bfloat16)
    pooled = jnp.dot(pooling, q_ref[...], preferred_element_type=jnp.float32).astype(jnp.bfloat16)
    raw = lax.dot_general(
        pooled, k_ref[...], (((1,), (1,)), ((), ())), preferred_element_type=jnp.float32
    )
    running = jnp.max(raw, axis=1, keepdims=True)
    weights = jnp.exp2((raw - running) * EXP2_SCALE)
    totals = jnp.sum(weights, axis=1, keepdims=True)
    weighted = jnp.dot(weights.astype(jnp.bfloat16), v_ref[...], preferred_element_type=jnp.float32)
    o_ref[...] = (weighted / totals).astype(o_ref.dtype)


def draft_attention(queries, keys, values, head_lo):
    token_rows, width = queries.shape
    rows = token_rows // POOL
    heads = width // HD
    key_rows = keys.shape[0]
    tile = min(DRAFT_ROWS, rows)
    cost = pl.CostEstimate(
        flops=4 * rows * key_rows * HD * heads + 2 * rows * tile * POOL * HD * heads,
        transcendentals=rows * key_rows * heads,
        bytes_accessed=2 * HD * heads * (token_rows + rows + 2 * key_rows),
    )
    return pl.pallas_call(
        draft_kernel,
        out_shape=jax.ShapeDtypeStruct((rows, width), jnp.bfloat16),
        cost_estimate=cost,
        grid=(heads, rows // tile),
        in_specs=[
            pl.BlockSpec((tile * POOL, HD), lambda h, r: (r, h)),
            pl.BlockSpec((key_rows, HD), lambda h, r: (0, h + head_lo)),
            pl.BlockSpec((key_rows, HD), lambda h, r: (0, h + head_lo)),
        ],
        out_specs=pl.BlockSpec((tile, HD), lambda h, r: (r, h)),
    )(queries, keys, values)


def head_permutes(matrix):
    count = lax.axis_size("head")
    me = lax.axis_index("head")
    rows, total = matrix.shape
    chunks = matrix.reshape(rows, count, total // count)
    by_shift = [lax.dynamic_index_in_dim(chunks, me, axis=1, keepdims=False)]
    for shift in range(1, count):
        piece = lax.dynamic_index_in_dim(chunks, (me + shift) % count, axis=1, keepdims=False)
        by_shift.append(
            lax.ppermute(piece, "head", [(i, (i + shift) % count) for i in range(count)])
        )
    stacked = jnp.stack(by_shift, axis=0)
    order = (me - jnp.arange(count, dtype=jnp.int32)) % count
    return jnp.take(stacked, order, axis=0).reshape(count * rows, total // count)


def on_device(query_in, key_in, value_in, block_lists):
    key_rows = lax.all_to_all(key_in, "head", split_axis=1, concat_axis=0, tiled=True)
    value_rows = head_permutes(value_in)
    seq_rows, width = key_rows.shape
    head_count = lax.axis_size("head")
    heads = width // HD
    first = max(1, heads // 2)
    spans = [(lo, n) for lo, n in ((0, first), (first, heads - first)) if n > 0]
    grouped_q = query_in.reshape(query_in.shape[0], head_count, width)
    query_slices = [
        grouped_q[:, :, lo * HD:(lo + n) * HD].reshape(query_in.shape[0], -1) for lo, n in spans
    ]

    def query_a2a(piece):
        return head_permutes(piece)

    draft_keys = lax.all_gather(pool_tokens(key_rows), "seq", axis=0, tiled=True)
    draft_values = lax.all_gather(pool_tokens(value_rows), "seq", axis=0, tiled=True)

    seq_count = lax.axis_size("seq")
    seq_index = lax.axis_index("seq")
    per_dev = seq_rows // BLOCK
    block_total, select_count = block_lists.shape
    block_ids = jnp.arange(block_total, dtype=jnp.int32)
    touched = jnp.any(block_lists[:, :, None] == block_ids[None, None, :], axis=1)
    needed = jnp.any(touched.reshape(seq_count, per_dev, seq_count, per_dev), axis=1)
    slot_rank = jnp.cumsum(needed.astype(jnp.int32), axis=2) - 1
    send_need = lax.dynamic_index_in_dim(needed, seq_index, axis=1, keepdims=False)
    send_rank = lax.dynamic_index_in_dim(slot_rank, seq_index, axis=1, keepdims=False)
    slot_hit = send_need[:, None, :] & (
        send_rank[:, None, :] == jnp.arange(CAP, dtype=jnp.int32)[None, :, None]
    )
    send_idx = jnp.sum(
        jnp.where(slot_hit, jnp.arange(per_dev, dtype=jnp.int32)[None, None, :], 0), axis=2
    ).reshape(-1)
    def exchange(rows):
        blocks = jnp.take(rows.reshape(per_dev, BLOCK, width), send_idx, axis=0)
        outgoing = blocks.reshape(seq_count, CAP, BLOCK, width)
        arrivals = []
        for shift in range(1, seq_count):
            parcel = lax.dynamic_index_in_dim(
                outgoing, (seq_index + shift) % seq_count, axis=0, keepdims=False
            )
            arrivals.append(
                lax.ppermute(
                    parcel, "seq", [(i, (i + shift) % seq_count) for i in range(seq_count)]
                )
            )
        return [a.reshape(CAP * BLOCK, width) for a in arrivals]

    remote_keys = exchange(key_rows)
    remote_values = exchange(value_rows)
    query_parts = [query_a2a(piece) for piece in query_slices]

    own_lists = lax.dynamic_slice_in_dim(block_lists, seq_index * per_dev, per_dev, 0)
    owners = own_lists // per_dev
    within = own_lists % per_dev
    own_rank = lax.dynamic_index_in_dim(slot_rank, seq_index, axis=0, keepdims=False)
    ranks_used = jnp.clip(own_rank[owners, within], 0, CAP - 1)
    distance = (seq_index - owners) % seq_count
    joint_pos = jnp.where(distance == 0, within, per_dev + (distance - 1) * CAP + ranks_used)
    table = jnp.clip(joint_pos, 0, per_dev + (seq_count - 1) * CAP - 1).reshape(-1).astype(jnp.int32)

    pieces = []
    for index, ((head_lo, count), queries) in enumerate(zip(spans, query_parts)):
        rows_part = sparse_attention(
            table, queries, key_rows, value_rows, remote_keys, remote_values, head_lo, count,
        )
        if index == len(spans) - 1:
            rows_part, draft_keys, draft_values = lax.optimization_barrier(
                (rows_part, draft_keys, draft_values)
            )
        back = lax.all_to_all(rows_part, "head", split_axis=0, concat_axis=1, tiled=True)
        pieces.append(back.reshape(back.shape[0], -1, count * HD))
    sparse_out = jnp.concatenate(pieces, axis=2).reshape(pieces[0].shape[0], -1)
    draft_out = jnp.concatenate(
        [
            draft_attention(queries, draft_keys, draft_values, head_lo)
            for (head_lo, count), queries in zip(spans, query_parts)
        ],
        axis=1,
    )
    return (draft_out, sparse_out)


def solution(mesh):
    return jax.shard_map(
        on_device,
        mesh=mesh,
        in_specs=(
            P(("groups", "seq", "head"), None),
            P(("groups", "seq", "head"), None),
            P(("groups", "seq", "head"), None),
            P("groups", None),
        ),
        out_specs=(P(("groups", "seq"), "head"), P(("groups", "seq", "head"), None)),
        check_vma=False,
    )
```

```python
import jax
import jax.numpy as jnp
from jax import lax
from jax.experimental import pallas as pl
from jax.experimental.pallas import tpu as pltpu
from jax.sharding import PartitionSpec as P

HD = 128
BLOCK = 128
POOL = 4
CAP = 2
SCALE = HD ** (-0.5)
DRAFT_ROWS = 128
PAIR = 2
EXP2_SCALE = SCALE * 1.4426950408889634


def pool_tokens(matrix):
    grouped = matrix.astype(jnp.float32).reshape(matrix.shape[0] // POOL, POOL, matrix.shape[1])
    return (grouped.sum(axis=1) * POOL ** (-0.5)).astype(jnp.bfloat16)


def sparse_kernel(tbl_ref, q_ref, *refs):
    near_k, near_v = refs[0], refs[1]
    far_count = (len(refs) - 5) // 2
    far_k = refs[2:2 + far_count]
    far_v = refs[2 + far_count:2 + 2 * far_count]
    o_ref, kall_ref, vall_ref = refs[2 + 2 * far_count:]
    per_dev = q_ref.shape[0] // BLOCK
    sel = tbl_ref.shape[0] // per_dev
    near_rows = near_k.shape[0]
    kall_ref[0:near_rows, :] = near_k[...]
    vall_ref[0:near_rows, :] = near_v[...]
    offset = near_rows
    for kr, vr in zip(far_k, far_v):
        kall_ref[offset:offset + kr.shape[0], :] = kr[...]
        vall_ref[offset:offset + vr.shape[0], :] = vr[...]
        offset += kr.shape[0]
    last = offset // BLOCK - 1

    def one_block(i):
        row = pl.multiple_of(i * BLOCK, BLOCK)
        keys = []
        values = []
        for j in range(sel):
            start = pl.multiple_of(jnp.clip(tbl_ref[i * sel + j], 0, last) * BLOCK, BLOCK)
            keys.append(kall_ref[pl.ds(start, BLOCK), :])
            values.append(vall_ref[pl.ds(start, BLOCK), :])
        raw = lax.dot_general(
            q_ref[pl.ds(row, BLOCK), :], jnp.concatenate(keys, axis=0),
            (((1,), (1,)), ((), ())), preferred_element_type=jnp.float32,
        )
        running = jnp.max(raw, axis=1, keepdims=True)
        weights = jnp.exp2((raw - running) * EXP2_SCALE)
        totals = jnp.sum(weights, axis=1, keepdims=True)
        weighted = jnp.dot(
            weights.astype(jnp.bfloat16), jnp.concatenate(values, axis=0),
            preferred_element_type=jnp.float32,
        )
        o_ref[pl.ds(row, BLOCK), :] = (weighted / totals).astype(o_ref.dtype)

    def body(i, carry):
        for lane in range(PAIR):
            one_block(i * PAIR + lane)
        return carry

    lax.fori_loop(0, per_dev // PAIR, body, 0)
    for i in range(per_dev - per_dev % PAIR, per_dev):
        one_block(i)


def sparse_attention(tbl, queries, keys, values, far_keys, far_values, head_lo, heads, q_lo):
    rows = queries.shape[0]

    def column(h, t):
        return (0, h + head_lo)

    operands = [keys, values] + list(far_keys) + list(far_values)
    total_rows = keys.shape[0] + sum(k.shape[0] for k in far_keys)
    sel = tbl.shape[0] * BLOCK // rows
    cost = pl.CostEstimate(
        flops=4 * rows * sel * BLOCK * HD * heads,
        transcendentals=rows * sel * BLOCK * heads,
        bytes_accessed=2 * HD * heads * (2 * rows + 2 * total_rows),
    )
    return pl.pallas_call(
        sparse_kernel,
        out_shape=jax.ShapeDtypeStruct((rows, heads * HD), jnp.bfloat16),
        cost_estimate=cost,
        grid_spec=pltpu.PrefetchScalarGridSpec(
            num_scalar_prefetch=1,
            grid=(heads,),
            in_specs=[pl.BlockSpec((rows, HD), lambda h, t: (0, h + q_lo))]
            + [pl.BlockSpec((x.shape[0], HD), column) for x in operands],
            out_specs=pl.BlockSpec((rows, HD), lambda h, t: (0, h)),
            scratch_shapes=[
                pltpu.VMEM((total_rows, HD), jnp.bfloat16),
                pltpu.VMEM((total_rows, HD), jnp.bfloat16),
            ],
        ),
    )(tbl, queries, *operands)


def draft_kernel(q_ref, k_ref, v_ref, o_ref):
    tile = o_ref.shape[0]
    token = lax.broadcasted_iota(jnp.int32, (tile, tile * POOL), 1)
    draft = lax.broadcasted_iota(jnp.int32, (tile, tile * POOL), 0)
    pooling = jnp.where(token // POOL == draft, POOL ** (-0.5), 0.0).astype(jnp.bfloat16)
    pooled = jnp.dot(pooling, q_ref[...], preferred_element_type=jnp.float32).astype(jnp.bfloat16)
    raw = lax.dot_general(
        pooled, k_ref[...], (((1,), (1,)), ((), ())), preferred_element_type=jnp.float32
    )
    running = jnp.max(raw, axis=1, keepdims=True)
    weights = jnp.exp2((raw - running) * EXP2_SCALE)
    totals = jnp.sum(weights, axis=1, keepdims=True)
    weighted = jnp.dot(weights.astype(jnp.bfloat16), v_ref[...], preferred_element_type=jnp.float32)
    o_ref[...] = (weighted / totals).astype(o_ref.dtype)


def draft_attention(queries, keys, values, head_lo):
    token_rows, width = queries.shape
    rows = token_rows // POOL
    heads = width // HD
    key_rows = keys.shape[0]
    tile = min(DRAFT_ROWS, rows)
    cost = pl.CostEstimate(
        flops=4 * rows * key_rows * HD * heads + 2 * rows * tile * POOL * HD * heads,
        transcendentals=rows * key_rows * heads,
        bytes_accessed=2 * HD * heads * (token_rows + rows + 2 * key_rows),
    )
    return pl.pallas_call(
        draft_kernel,
        out_shape=jax.ShapeDtypeStruct((rows, width), jnp.bfloat16),
        cost_estimate=cost,
        grid=(heads, rows // tile),
        in_specs=[
            pl.BlockSpec((tile * POOL, HD), lambda h, r: (r, h)),
            pl.BlockSpec((key_rows, HD), lambda h, r: (0, h + head_lo)),
            pl.BlockSpec((key_rows, HD), lambda h, r: (0, h + head_lo)),
        ],
        out_specs=pl.BlockSpec((tile, HD), lambda h, r: (r, h)),
    )(queries, keys, values)


def head_permutes(matrix):
    count = lax.axis_size("head")
    me = lax.axis_index("head")
    rows, total = matrix.shape
    chunks = matrix.reshape(rows, count, total // count)
    by_shift = [lax.dynamic_index_in_dim(chunks, me, axis=1, keepdims=False)]
    for shift in range(1, count):
        piece = lax.dynamic_index_in_dim(chunks, (me + shift) % count, axis=1, keepdims=False)
        by_shift.append(
            lax.ppermute(piece, "head", [(i, (i + shift) % count) for i in range(count)])
        )
    stacked = jnp.stack(by_shift, axis=0)
    order = (me - jnp.arange(count, dtype=jnp.int32)) % count
    return jnp.take(stacked, order, axis=0).reshape(count * rows, total // count)


def on_device(query_in, key_in, value_in, block_lists):
    key_rows = lax.all_to_all(key_in, "head", split_axis=1, concat_axis=0, tiled=True)
    value_rows = head_permutes(value_in)
    seq_rows, width = key_rows.shape
    head_count = lax.axis_size("head")
    heads = width // HD
    first = max(1, heads // 2)
    spans = [(lo, n) for lo, n in ((0, first), (first, heads - first)) if n > 0]
    queries = lax.all_to_all(query_in, "head", split_axis=1, concat_axis=0, tiled=True)

    draft_keys = lax.all_gather(pool_tokens(key_rows), "seq", axis=0, tiled=True)
    draft_values = lax.all_gather(pool_tokens(value_rows), "seq", axis=0, tiled=True)

    seq_count = lax.axis_size("seq")
    seq_index = lax.axis_index("seq")
    per_dev = seq_rows // BLOCK
    block_total, select_count = block_lists.shape
    block_ids = jnp.arange(block_total, dtype=jnp.int32)
    touched = jnp.any(block_lists[:, :, None] == block_ids[None, None, :], axis=1)
    needed = jnp.any(touched.reshape(seq_count, per_dev, seq_count, per_dev), axis=1)
    slot_rank = jnp.cumsum(needed.astype(jnp.int32), axis=2) - 1
    send_need = lax.dynamic_index_in_dim(needed, seq_index, axis=1, keepdims=False)
    send_rank = lax.dynamic_index_in_dim(slot_rank, seq_index, axis=1, keepdims=False)
    slot_hit = send_need[:, None, :] & (
        send_rank[:, None, :] == jnp.arange(CAP, dtype=jnp.int32)[None, :, None]
    )
    send_idx = jnp.sum(
        jnp.where(slot_hit, jnp.arange(per_dev, dtype=jnp.int32)[None, None, :], 0), axis=2
    ).reshape(-1)
    def exchange(rows):
        blocks = jnp.take(rows.reshape(per_dev, BLOCK, width), send_idx, axis=0)
        outgoing = blocks.reshape(seq_count, CAP, BLOCK, width)
        arrivals = []
        for shift in range(1, seq_count):
            parcel = lax.dynamic_index_in_dim(
                outgoing, (seq_index + shift) % seq_count, axis=0, keepdims=False
            )
            arrivals.append(
                lax.ppermute(
                    parcel, "seq", [(i, (i + shift) % seq_count) for i in range(seq_count)]
                )
            )
        return [a.reshape(CAP * BLOCK, width) for a in arrivals]

    remote_keys = exchange(key_rows)
    remote_values = exchange(value_rows)

    own_lists = lax.dynamic_slice_in_dim(block_lists, seq_index * per_dev, per_dev, 0)
    owners = own_lists // per_dev
    within = own_lists % per_dev
    own_rank = lax.dynamic_index_in_dim(slot_rank, seq_index, axis=0, keepdims=False)
    ranks_used = jnp.clip(own_rank[owners, within], 0, CAP - 1)
    distance = (seq_index - owners) % seq_count
    joint_pos = jnp.where(distance == 0, within, per_dev + (distance - 1) * CAP + ranks_used)
    table = jnp.clip(joint_pos, 0, per_dev + (seq_count - 1) * CAP - 1).reshape(-1).astype(jnp.int32)

    pieces = []
    for index, (head_lo, count) in enumerate(spans):
        rows_part = sparse_attention(
            table, queries, key_rows, value_rows, remote_keys, remote_values,
            head_lo, count, head_lo,
        )
        if index == len(spans) - 1:
            rows_part, draft_keys, draft_values = lax.optimization_barrier(
                (rows_part, draft_keys, draft_values)
            )
        back = lax.all_to_all(rows_part, "head", split_axis=0, concat_axis=1, tiled=True)
        pieces.append(back.reshape(back.shape[0], -1, count * HD))
    sparse_out = jnp.concatenate(pieces, axis=2).reshape(pieces[0].shape[0], -1)
    draft_out = draft_attention(queries, draft_keys, draft_values, 0)
    return (draft_out, sparse_out)


def solution(mesh):
    return jax.shard_map(
        on_device,
        mesh=mesh,
        in_specs=(
            P(("groups", "seq", "head"), None),
            P(("groups", "seq", "head"), None),
            P(("groups", "seq", "head"), None),
            P("groups", None),
        ),
        out_specs=(P(("groups", "seq"), "head"), P(("groups", "seq", "head"), None)),
        check_vma=False,
    )
```

```python
import jax
import jax.numpy as jnp
from jax import lax
from jax.experimental import pallas as pl
from jax.experimental.pallas import tpu as pltpu
from jax.sharding import PartitionSpec as P

HD = 128
BLOCK = 128
POOL = 4
CAP = 2
SCALE = HD ** (-0.5)
DRAFT_ROWS = 128
PAIR = 2
EXP2_SCALE = SCALE * 1.4426950408889634


def pooling_matrix(tile):
    token = lax.broadcasted_iota(jnp.int32, (tile, tile * POOL), 1)
    draft = lax.broadcasted_iota(jnp.int32, (tile, tile * POOL), 0)
    return jnp.where(token // POOL == draft, POOL ** (-0.5), 0.0).astype(jnp.bfloat16)


def pool_kernel(x_ref, o_ref):
    pooled = jnp.dot(pooling_matrix(o_ref.shape[0]), x_ref[...], preferred_element_type=jnp.float32)
    o_ref[...] = pooled.astype(o_ref.dtype)


def pool_tokens(matrix):
    token_rows, width = matrix.shape
    rows = token_rows // POOL
    tile = min(DRAFT_ROWS, rows)
    return pl.pallas_call(
        pool_kernel,
        out_shape=jax.ShapeDtypeStruct((rows, width), jnp.bfloat16),
        grid=(width // HD, rows // tile),
        in_specs=[pl.BlockSpec((tile * POOL, HD), lambda h, r: (r, h))],
        out_specs=pl.BlockSpec((tile, HD), lambda h, r: (r, h)),
        cost_estimate=pl.CostEstimate(
            flops=2 * rows * tile * POOL * width, transcendentals=0,
            bytes_accessed=2 * width * (token_rows + rows),
        ),
    )(matrix)


def sparse_kernel(tbl_ref, q_ref, *refs):
    near_k, near_v = refs[0], refs[1]
    far_count = (len(refs) - 5) // 2
    far_k = refs[2:2 + far_count]
    far_v = refs[2 + far_count:2 + 2 * far_count]
    o_ref, kall_ref, vall_ref = refs[2 + 2 * far_count:]
    per_dev = q_ref.shape[0] // BLOCK
    sel = tbl_ref.shape[0] // per_dev
    near_rows = near_k.shape[0]
    kall_ref[0:near_rows, :] = near_k[...]
    vall_ref[0:near_rows, :] = near_v[...]
    offset = near_rows
    for kr, vr in zip(far_k, far_v):
        kall_ref[offset:offset + kr.shape[0], :] = kr[...]
        vall_ref[offset:offset + vr.shape[0], :] = vr[...]
        offset += kr.shape[0]
    last = offset // BLOCK - 1

    def one_block(i):
        row = pl.multiple_of(i * BLOCK, BLOCK)
        keys = []
        values = []
        for j in range(sel):
            start = pl.multiple_of(jnp.clip(tbl_ref[i * sel + j], 0, last) * BLOCK, BLOCK)
            keys.append(kall_ref[pl.ds(start, BLOCK), :])
            values.append(vall_ref[pl.ds(start, BLOCK), :])
        raw = lax.dot_general(
            q_ref[pl.ds(row, BLOCK), :], jnp.concatenate(keys, axis=0),
            (((1,), (1,)), ((), ())), preferred_element_type=jnp.float32,
        )
        running = jnp.max(raw, axis=1, keepdims=True)
        weights = jnp.exp2((raw - running) * EXP2_SCALE)
        totals = jnp.sum(weights, axis=1, keepdims=True)
        weighted = jnp.dot(
            weights.astype(jnp.bfloat16), jnp.concatenate(values, axis=0),
            preferred_element_type=jnp.float32,
        )
        o_ref[pl.ds(row, BLOCK), :] = (weighted / totals).astype(o_ref.dtype)

    def body(i, carry):
        for lane in range(PAIR):
            one_block(i * PAIR + lane)
        return carry

    lax.fori_loop(0, per_dev // PAIR, body, 0)
    for i in range(per_dev - per_dev % PAIR, per_dev):
        one_block(i)


def sparse_attention(tbl, queries, keys, values, far_keys, far_values, head_lo, heads, q_lo):
    rows = queries.shape[0]

    def column(h, t):
        return (0, h + head_lo)

    operands = [keys, values] + list(far_keys) + list(far_values)
    total_rows = keys.shape[0] + sum(k.shape[0] for k in far_keys)
    sel = tbl.shape[0] * BLOCK // rows
    cost = pl.CostEstimate(
        flops=4 * rows * sel * BLOCK * HD * heads,
        transcendentals=rows * sel * BLOCK * heads,
        bytes_accessed=2 * HD * heads * (2 * rows + 2 * total_rows),
    )
    return pl.pallas_call(
        sparse_kernel,
        out_shape=jax.ShapeDtypeStruct((rows, heads * HD), jnp.bfloat16),
        cost_estimate=cost,
        grid_spec=pltpu.PrefetchScalarGridSpec(
            num_scalar_prefetch=1,
            grid=(heads,),
            in_specs=[pl.BlockSpec((rows, HD), lambda h, t: (0, h + q_lo))]
            + [pl.BlockSpec((x.shape[0], HD), column) for x in operands],
            out_specs=pl.BlockSpec((rows, HD), lambda h, t: (0, h)),
            scratch_shapes=[
                pltpu.VMEM((total_rows, HD), jnp.bfloat16),
                pltpu.VMEM((total_rows, HD), jnp.bfloat16),
            ],
        ),
    )(tbl, queries, *operands)


def draft_kernel(q_ref, k_ref, v_ref, o_ref):
    pooling = pooling_matrix(o_ref.shape[0])
    pooled = jnp.dot(pooling, q_ref[...], preferred_element_type=jnp.float32).astype(jnp.bfloat16)
    raw = lax.dot_general(
        pooled, k_ref[...], (((1,), (1,)), ((), ())), preferred_element_type=jnp.float32
    )
    running = jnp.max(raw, axis=1, keepdims=True)
    weights = jnp.exp2((raw - running) * EXP2_SCALE)
    totals = jnp.sum(weights, axis=1, keepdims=True)
    weighted = jnp.dot(weights.astype(jnp.bfloat16), v_ref[...], preferred_element_type=jnp.float32)
    o_ref[...] = (weighted / totals).astype(o_ref.dtype)


def draft_attention(queries, keys, values, head_lo):
    token_rows, width = queries.shape
    rows = token_rows // POOL
    heads = width // HD
    key_rows = keys.shape[0]
    tile = min(DRAFT_ROWS, rows)
    cost = pl.CostEstimate(
        flops=4 * rows * key_rows * HD * heads + 2 * rows * tile * POOL * HD * heads,
        transcendentals=rows * key_rows * heads,
        bytes_accessed=2 * HD * heads * (token_rows + rows + 2 * key_rows),
    )
    return pl.pallas_call(
        draft_kernel,
        out_shape=jax.ShapeDtypeStruct((rows, width), jnp.bfloat16),
        cost_estimate=cost,
        grid=(heads, rows // tile),
        in_specs=[
            pl.BlockSpec((tile * POOL, HD), lambda h, r: (r, h)),
            pl.BlockSpec((key_rows, HD), lambda h, r: (0, h + head_lo)),
            pl.BlockSpec((key_rows, HD), lambda h, r: (0, h + head_lo)),
        ],
        out_specs=pl.BlockSpec((tile, HD), lambda h, r: (r, h)),
    )(queries, keys, values)


def head_permutes(matrix):
    count = lax.axis_size("head")
    me = lax.axis_index("head")
    rows, total = matrix.shape
    chunks = matrix.reshape(rows, count, total // count)
    by_shift = [lax.dynamic_index_in_dim(chunks, me, axis=1, keepdims=False)]
    for shift in range(1, count):
        piece = lax.dynamic_index_in_dim(chunks, (me + shift) % count, axis=1, keepdims=False)
        by_shift.append(
            lax.ppermute(piece, "head", [(i, (i + shift) % count) for i in range(count)])
        )
    stacked = jnp.stack(by_shift, axis=0)
    order = (me - jnp.arange(count, dtype=jnp.int32)) % count
    return jnp.take(stacked, order, axis=0).reshape(count * rows, total // count)


def on_device(query_in, key_in, value_in, block_lists):
    key_rows = lax.all_to_all(key_in, "head", split_axis=1, concat_axis=0, tiled=True)
    value_rows = head_permutes(value_in)
    seq_rows, width = key_rows.shape
    heads = width // HD
    first = max(1, heads // 2)
    spans = [(lo, n) for lo, n in ((0, first), (first, heads - first)) if n > 0]
    queries = lax.all_to_all(query_in, "head", split_axis=1, concat_axis=0, tiled=True)

    draft_keys = lax.all_gather(pool_tokens(key_rows), "seq", axis=0, tiled=True)
    draft_values = lax.all_gather(pool_tokens(value_rows), "seq", axis=0, tiled=True)

    seq_count = lax.axis_size("seq")
    seq_index = lax.axis_index("seq")
    per_dev = seq_rows // BLOCK
    block_total, select_count = block_lists.shape
    block_ids = jnp.arange(block_total, dtype=jnp.int32)
    touched = jnp.any(block_lists[:, :, None] == block_ids[None, None, :], axis=1)
    needed = jnp.any(touched.reshape(seq_count, per_dev, seq_count, per_dev), axis=1)
    slot_rank = jnp.cumsum(needed.astype(jnp.int32), axis=2) - 1
    send_need = lax.dynamic_index_in_dim(needed, seq_index, axis=1, keepdims=False)
    send_rank = lax.dynamic_index_in_dim(slot_rank, seq_index, axis=1, keepdims=False)
    slot_hit = send_need[:, None, :] & (
        send_rank[:, None, :] == jnp.arange(CAP, dtype=jnp.int32)[None, :, None]
    )
    send_idx = jnp.sum(
        jnp.where(slot_hit, jnp.arange(per_dev, dtype=jnp.int32)[None, None, :], 0), axis=2
    ).reshape(-1)
    def exchange(rows):
        blocks = jnp.take(rows.reshape(per_dev, BLOCK, width), send_idx, axis=0)
        outgoing = blocks.reshape(seq_count, CAP, BLOCK, width)
        arrivals = []
        for shift in range(1, seq_count):
            parcel = lax.dynamic_index_in_dim(
                outgoing, (seq_index + shift) % seq_count, axis=0, keepdims=False
            )
            arrivals.append(
                lax.ppermute(
                    parcel, "seq", [(i, (i + shift) % seq_count) for i in range(seq_count)]
                )
            )
        return [a.reshape(CAP * BLOCK, width) for a in arrivals]

    remote_keys = exchange(key_rows)
    remote_values = exchange(value_rows)

    own_lists = lax.dynamic_slice_in_dim(block_lists, seq_index * per_dev, per_dev, 0)
    owners = own_lists // per_dev
    within = own_lists % per_dev
    own_rank = lax.dynamic_index_in_dim(slot_rank, seq_index, axis=0, keepdims=False)
    ranks_used = jnp.clip(own_rank[owners, within], 0, CAP - 1)
    distance = (seq_index - owners) % seq_count
    joint_pos = jnp.where(distance == 0, within, per_dev + (distance - 1) * CAP + ranks_used)
    table = jnp.clip(joint_pos, 0, per_dev + (seq_count - 1) * CAP - 1).reshape(-1).astype(jnp.int32)

    pieces = []
    for index, (head_lo, count) in enumerate(spans):
        rows_part = sparse_attention(
            table, queries, key_rows, value_rows, remote_keys, remote_values,
            head_lo, count, head_lo,
        )
        if index == len(spans) - 1:
            rows_part, draft_keys, draft_values = lax.optimization_barrier(
                (rows_part, draft_keys, draft_values)
            )
        back = lax.all_to_all(rows_part, "head", split_axis=0, concat_axis=1, tiled=True)
        pieces.append(back.reshape(back.shape[0], -1, count * HD))
    sparse_out = jnp.concatenate(pieces, axis=2).reshape(pieces[0].shape[0], -1)
    draft_out = draft_attention(queries, draft_keys, draft_values, 0)
    return (draft_out, sparse_out)


def solution(mesh):
    return jax.shard_map(
        on_device,
        mesh=mesh,
        in_specs=(
            P(("groups", "seq", "head"), None),
            P(("groups", "seq", "head"), None),
            P(("groups", "seq", "head"), None),
            P("groups", None),
        ),
        out_specs=(P(("groups", "seq"), "head"), P(("groups", "seq", "head"), None)),
        check_vma=False,
    )
```

```python
import jax
import jax.numpy as jnp
from jax import lax
from jax.experimental import pallas as pl
from jax.experimental.pallas import tpu as pltpu
from jax.sharding import PartitionSpec as P

HD = 128
BLOCK = 128
POOL = 4
CAP = 2
SCALE = HD ** (-0.5)
DRAFT_ROWS = 128
PAIR = 2
EXP2_SCALE = SCALE * 1.4426950408889634


def pool_tokens(matrix):
    grouped = matrix.astype(jnp.float32).reshape(matrix.shape[0] // POOL, POOL, matrix.shape[1])
    return (grouped.sum(axis=1) * POOL ** (-0.5)).astype(jnp.bfloat16)


def sparse_kernel(tbl_ref, q_ref, *refs):
    near_k, near_v = refs[0], refs[1]
    far_count = (len(refs) - 5) // 2
    far_k = refs[2:2 + far_count]
    far_v = refs[2 + far_count:2 + 2 * far_count]
    o_ref, kall_ref, vall_ref = refs[2 + 2 * far_count:]
    per_dev = q_ref.shape[0] // BLOCK
    sel = tbl_ref.shape[0] // per_dev
    near_rows = near_k.shape[0]
    kall_ref[0:near_rows, :] = near_k[...]
    vall_ref[0:near_rows, :] = near_v[...]
    offset = near_rows
    for kr, vr in zip(far_k, far_v):
        kall_ref[offset:offset + kr.shape[0], :] = kr[...]
        vall_ref[offset:offset + vr.shape[0], :] = vr[...]
        offset += kr.shape[0]
    last = offset // BLOCK - 1

    def one_block(i):
        row = pl.multiple_of(i * BLOCK, BLOCK)
        keys = []
        values = []
        for j in range(sel):
            start = pl.multiple_of(jnp.clip(tbl_ref[i * sel + j], 0, last) * BLOCK, BLOCK)
            keys.append(kall_ref[pl.ds(start, BLOCK), :])
            values.append(vall_ref[pl.ds(start, BLOCK), :])
        raw = lax.dot_general(
            q_ref[pl.ds(row, BLOCK), :], jnp.concatenate(keys, axis=0),
            (((1,), (1,)), ((), ())), preferred_element_type=jnp.float32,
        )
        running = jnp.max(raw, axis=1, keepdims=True)
        weights = jnp.exp2((raw - running) * EXP2_SCALE)
        totals = jnp.sum(weights, axis=1, keepdims=True)
        weighted = jnp.dot(
            weights.astype(jnp.bfloat16), jnp.concatenate(values, axis=0),
            preferred_element_type=jnp.float32,
        )
        o_ref[pl.ds(row, BLOCK), :] = (weighted / totals).astype(o_ref.dtype)

    def body(i, carry):
        for lane in range(PAIR):
            one_block(i * PAIR + lane)
        return carry

    lax.fori_loop(0, per_dev // PAIR, body, 0)
    for i in range(per_dev - per_dev % PAIR, per_dev):
        one_block(i)


def sparse_attention(tbl, queries, keys, values, far_keys, far_values, head_lo, heads):
    rows = queries.shape[0]

    def column(h, t):
        return (0, h + head_lo)

    operands = [keys, values] + list(far_keys) + list(far_values)
    total_rows = keys.shape[0] + sum(k.shape[0] for k in far_keys)
    sel = tbl.shape[0] * BLOCK // rows
    cost = pl.CostEstimate(
        flops=4 * rows * sel * BLOCK * HD * heads,
        transcendentals=rows * sel * BLOCK * heads,
        bytes_accessed=2 * HD * heads * (2 * rows + 2 * total_rows),
    )
    return pl.pallas_call(
        sparse_kernel,
        out_shape=jax.ShapeDtypeStruct((rows, heads * HD), jnp.bfloat16),
        cost_estimate=cost,
        grid_spec=pltpu.PrefetchScalarGridSpec(
            num_scalar_prefetch=1,
            grid=(heads,),
            in_specs=[pl.BlockSpec((rows, HD), lambda h, t: (0, h))]
            + [pl.BlockSpec((x.shape[0], HD), column) for x in operands],
            out_specs=pl.BlockSpec((rows, HD), lambda h, t: (0, h)),
            scratch_shapes=[
                pltpu.VMEM((total_rows, HD), jnp.bfloat16),
                pltpu.VMEM((total_rows, HD), jnp.bfloat16),
            ],
        ),
    )(tbl, queries, *operands)


def draft_kernel(q_ref, k_ref, v_ref, o_ref):
    tile = o_ref.shape[0]
    token = lax.broadcasted_iota(jnp.int32, (tile, tile * POOL), 1)
    draft = lax.broadcasted_iota(jnp.int32, (tile, tile * POOL), 0)
    pooling = jnp.where(token // POOL == draft, POOL ** (-0.5), 0.0).astype(jnp.bfloat16)
    pooled = jnp.dot(pooling, q_ref[...], preferred_element_type=jnp.float32).astype(jnp.bfloat16)
    raw = lax.dot_general(
        pooled, k_ref[...], (((1,), (1,)), ((), ())), preferred_element_type=jnp.float32
    )
    running = jnp.max(raw, axis=1, keepdims=True)
    weights = jnp.exp2((raw - running) * EXP2_SCALE)
    totals = jnp.sum(weights, axis=1, keepdims=True)
    weighted = jnp.dot(weights.astype(jnp.bfloat16), v_ref[...], preferred_element_type=jnp.float32)
    o_ref[...] = (weighted / totals).astype(o_ref.dtype)


def draft_attention(queries, keys, values, head_lo):
    token_rows, width = queries.shape
    rows = token_rows // POOL
    heads = width // HD
    key_rows = keys.shape[0]
    tile = min(DRAFT_ROWS, rows)
    cost = pl.CostEstimate(
        flops=4 * rows * key_rows * HD * heads + 2 * rows * tile * POOL * HD * heads,
        transcendentals=rows * key_rows * heads,
        bytes_accessed=2 * HD * heads * (token_rows + rows + 2 * key_rows),
    )
    return pl.pallas_call(
        draft_kernel,
        out_shape=jax.ShapeDtypeStruct((rows, width), jnp.bfloat16),
        cost_estimate=cost,
        grid=(heads, rows // tile),
        in_specs=[
            pl.BlockSpec((tile * POOL, HD), lambda h, r: (r, h)),
            pl.BlockSpec((key_rows, HD), lambda h, r: (0, h + head_lo)),
            pl.BlockSpec((key_rows, HD), lambda h, r: (0, h + head_lo)),
        ],
        out_specs=pl.BlockSpec((tile, HD), lambda h, r: (r, h)),
    )(queries, keys, values)


def head_permutes(matrix):
    count = lax.axis_size("head")
    me = lax.axis_index("head")
    rows, total = matrix.shape
    chunks = matrix.reshape(rows, count, total // count)
    by_shift = [lax.dynamic_index_in_dim(chunks, me, axis=1, keepdims=False)]
    for shift in range(1, count):
        piece = lax.dynamic_index_in_dim(chunks, (me + shift) % count, axis=1, keepdims=False)
        by_shift.append(
            lax.ppermute(piece, "head", [(i, (i + shift) % count) for i in range(count)])
        )
    stacked = jnp.stack(by_shift, axis=0)
    order = (me - jnp.arange(count, dtype=jnp.int32)) % count
    return jnp.take(stacked, order, axis=0).reshape(count * rows, total // count)


def on_device(query_in, key_in, value_in, block_lists):
    key_rows = lax.all_to_all(key_in, "head", split_axis=1, concat_axis=0, tiled=True)
    value_rows = head_permutes(value_in)
    seq_rows, width = key_rows.shape
    head_count = lax.axis_size("head")
    heads = width // HD
    first = max(1, heads // 2)
    spans = [(lo, n) for lo, n in ((0, first), (first, heads - first)) if n > 0]
    grouped_q = query_in.reshape(query_in.shape[0], head_count, width)
    query_slices = [
        grouped_q[:, :, lo * HD:(lo + n) * HD].reshape(query_in.shape[0], -1) for lo, n in spans
    ]

    def query_a2a(piece):
        return lax.all_to_all(piece, "head", split_axis=1, concat_axis=0, tiled=True)

    draft_keys = lax.all_gather(pool_tokens(key_rows), "seq", axis=0, tiled=True)
    draft_values = lax.all_gather(pool_tokens(value_rows), "seq", axis=0, tiled=True)

    seq_count = lax.axis_size("seq")
    seq_index = lax.axis_index("seq")
    per_dev = seq_rows // BLOCK
    block_total, select_count = block_lists.shape
    block_ids = jnp.arange(block_total, dtype=jnp.int32)
    touched = jnp.any(block_lists[:, :, None] == block_ids[None, None, :], axis=1)
    needed = jnp.any(touched.reshape(seq_count, per_dev, seq_count, per_dev), axis=1)
    slot_rank = jnp.cumsum(needed.astype(jnp.int32), axis=2) - 1
    send_need = lax.dynamic_index_in_dim(needed, seq_index, axis=1, keepdims=False)
    send_rank = lax.dynamic_index_in_dim(slot_rank, seq_index, axis=1, keepdims=False)
    slot_hit = send_need[:, None, :] & (
        send_rank[:, None, :] == jnp.arange(CAP, dtype=jnp.int32)[None, :, None]
    )
    send_idx = jnp.sum(
        jnp.where(slot_hit, jnp.arange(per_dev, dtype=jnp.int32)[None, None, :], 0), axis=2
    ).reshape(-1)
    def exchange(rows):
        blocks = jnp.take(rows.reshape(per_dev, BLOCK, width), send_idx, axis=0)
        outgoing = blocks.reshape(seq_count, CAP, BLOCK, width)
        arrivals = []
        for shift in range(1, seq_count):
            parcel = lax.dynamic_index_in_dim(
                outgoing, (seq_index + shift) % seq_count, axis=0, keepdims=False
            )
            arrivals.append(
                lax.ppermute(
                    parcel, "seq", [(i, (i + shift) % seq_count) for i in range(seq_count)]
                )
            )
        return [a.reshape(CAP * BLOCK, width) for a in arrivals]

    remote_keys = exchange(key_rows)
    remote_values = exchange(value_rows)
    leading, remote_values = lax.optimization_barrier((query_slices[0], remote_values))
    query_parts = [query_a2a(leading)]
    later, remote_keys = lax.optimization_barrier((query_slices[1:], remote_keys))
    query_parts += [query_a2a(piece) for piece in later]

    own_lists = lax.dynamic_slice_in_dim(block_lists, seq_index * per_dev, per_dev, 0)
    owners = own_lists // per_dev
    within = own_lists % per_dev
    own_rank = lax.dynamic_index_in_dim(slot_rank, seq_index, axis=0, keepdims=False)
    ranks_used = jnp.clip(own_rank[owners, within], 0, CAP - 1)
    distance = (seq_index - owners) % seq_count
    joint_pos = jnp.where(distance == 0, within, per_dev + (distance - 1) * CAP + ranks_used)
    table = jnp.clip(joint_pos, 0, per_dev + (seq_count - 1) * CAP - 1).reshape(-1).astype(jnp.int32)

    pieces = []
    for index, ((head_lo, count), queries) in enumerate(zip(spans, query_parts)):
        rows_part = sparse_attention(
            table, queries, key_rows, value_rows, remote_keys, remote_values, head_lo, count,
        )
        if index == len(spans) - 1:
            rows_part, draft_keys, draft_values = lax.optimization_barrier(
                (rows_part, draft_keys, draft_values)
            )
        back = lax.all_to_all(rows_part, "head", split_axis=0, concat_axis=1, tiled=True)
        pieces.append(back.reshape(back.shape[0], -1, count * HD))
    sparse_out = jnp.concatenate(pieces, axis=2).reshape(pieces[0].shape[0], -1)
    draft_out = jnp.concatenate(
        [
            draft_attention(queries, draft_keys, draft_values, head_lo)
            for (head_lo, count), queries in zip(spans, query_parts)
        ],
        axis=1,
    )
    return (draft_out, sparse_out)


def solution(mesh):
    return jax.shard_map(
        on_device,
        mesh=mesh,
        in_specs=(
            P(("groups", "seq", "head"), None),
            P(("groups", "seq", "head"), None),
            P(("groups", "seq", "head"), None),
            P("groups", None),
        ),
        out_specs=(P(("groups", "seq"), "head"), P(("groups", "seq", "head"), None)),
        check_vma=False,
    )
```

```python
import jax
import jax.numpy as jnp
from jax import lax
from jax.experimental import pallas as pl
from jax.experimental.pallas import tpu as pltpu
from jax.sharding import PartitionSpec as P

HD = 128
BLOCK = 128
POOL = 4
CAP = 2
SCALE = HD ** (-0.5)
DRAFT_ROWS = 128
PAIR = 2
EXP2_SCALE = SCALE * 1.4426950408889634


def pool_tokens(matrix):
    grouped = matrix.astype(jnp.float32).reshape(matrix.shape[0] // POOL, POOL, matrix.shape[1])
    return (grouped.sum(axis=1) * POOL ** (-0.5)).astype(jnp.bfloat16)


def sparse_kernel(tbl_ref, q_ref, *refs):
    near_k, near_v = refs[0], refs[1]
    far_count = (len(refs) - 5) // 2
    far_k = refs[2:2 + far_count]
    far_v = refs[2 + far_count:2 + 2 * far_count]
    o_ref, kall_ref, vall_ref = refs[2 + 2 * far_count:]
    per_dev = q_ref.shape[0] // BLOCK
    sel = tbl_ref.shape[0] // per_dev
    near_rows = near_k.shape[0]
    kall_ref[0:near_rows, :] = near_k[...]
    vall_ref[0:near_rows, :] = near_v[...]
    offset = near_rows
    for kr, vr in zip(far_k, far_v):
        kall_ref[offset:offset + kr.shape[0], :] = kr[...]
        vall_ref[offset:offset + vr.shape[0], :] = vr[...]
        offset += kr.shape[0]
    last = offset // BLOCK - 1

    def one_block(i):
        row = pl.multiple_of(i * BLOCK, BLOCK)
        keys = []
        values = []
        for j in range(sel):
            start = pl.multiple_of(jnp.clip(tbl_ref[i * sel + j], 0, last) * BLOCK, BLOCK)
            keys.append(kall_ref[pl.ds(start, BLOCK), :])
            values.append(vall_ref[pl.ds(start, BLOCK), :])
        raw = lax.dot_general(
            q_ref[pl.ds(row, BLOCK), :], jnp.concatenate(keys, axis=0),
            (((1,), (1,)), ((), ())), preferred_element_type=jnp.float32,
        )
        running = jnp.max(raw, axis=1, keepdims=True)
        weights = jnp.exp2((raw - running) * EXP2_SCALE)
        totals = jnp.sum(weights, axis=1, keepdims=True)
        weighted = jnp.dot(
            weights.astype(jnp.bfloat16), jnp.concatenate(values, axis=0),
            preferred_element_type=jnp.float32,
        )
        o_ref[pl.ds(row, BLOCK), :] = (weighted / totals).astype(o_ref.dtype)

    def body(i, carry):
        for lane in range(PAIR):
            one_block(i * PAIR + lane)
        return carry

    lax.fori_loop(0, per_dev // PAIR, body, 0)
    for i in range(per_dev - per_dev % PAIR, per_dev):
        one_block(i)


def sparse_attention(tbl, queries, keys, values, far_keys, far_values, head_lo, heads, q_lo):
    rows = queries.shape[0]

    def column(h, t):
        return (0, h + head_lo)

    operands = [keys, values] + list(far_keys) + list(far_values)
    total_rows = keys.shape[0] + sum(k.shape[0] for k in far_keys)
    sel = tbl.shape[0] * BLOCK // rows
    cost = pl.CostEstimate(
        flops=4 * rows * sel * BLOCK * HD * heads,
        transcendentals=rows * sel * BLOCK * heads,
        bytes_accessed=2 * HD * heads * (2 * rows + 2 * total_rows),
    )
    return pl.pallas_call(
        sparse_kernel,
        out_shape=jax.ShapeDtypeStruct((rows, heads * HD), jnp.bfloat16),
        cost_estimate=cost,
        grid_spec=pltpu.PrefetchScalarGridSpec(
            num_scalar_prefetch=1,
            grid=(heads,),
            in_specs=[pl.BlockSpec((rows, HD), lambda h, t: (0, h + q_lo))]
            + [pl.BlockSpec((x.shape[0], HD), column) for x in operands],
            out_specs=pl.BlockSpec((rows, HD), lambda h, t: (0, h)),
            scratch_shapes=[
                pltpu.VMEM((total_rows, HD), jnp.bfloat16),
                pltpu.VMEM((total_rows, HD), jnp.bfloat16),
            ],
        ),
    )(tbl, queries, *operands)


def draft_kernel(q_ref, k_ref, v_ref, o_ref):
    tile = o_ref.shape[0]
    token = lax.broadcasted_iota(jnp.int32, (tile, tile * POOL), 1)
    draft = lax.broadcasted_iota(jnp.int32, (tile, tile * POOL), 0)
    pooling = jnp.where(token // POOL == draft, POOL ** (-0.5), 0.0).astype(jnp.bfloat16)
    pooled = jnp.dot(pooling, q_ref[...], preferred_element_type=jnp.float32).astype(jnp.bfloat16)
    raw = lax.dot_general(
        pooled, k_ref[...], (((1,), (1,)), ((), ())), preferred_element_type=jnp.float32
    )
    running = jnp.max(raw, axis=1, keepdims=True)
    weights = jnp.exp2((raw - running) * EXP2_SCALE)
    totals = jnp.sum(weights, axis=1, keepdims=True)
    weighted = jnp.dot(weights.astype(jnp.bfloat16), v_ref[...], preferred_element_type=jnp.float32)
    o_ref[...] = (weighted / totals).astype(o_ref.dtype)


def draft_attention(queries, keys, values, head_lo):
    token_rows, width = queries.shape
    rows = token_rows // POOL
    heads = width // HD
    key_rows = keys.shape[0]
    tile = min(DRAFT_ROWS, rows)
    cost = pl.CostEstimate(
        flops=4 * rows * key_rows * HD * heads + 2 * rows * tile * POOL * HD * heads,
        transcendentals=rows * key_rows * heads,
        bytes_accessed=2 * HD * heads * (token_rows + rows + 2 * key_rows),
    )
    return pl.pallas_call(
        draft_kernel,
        out_shape=jax.ShapeDtypeStruct((rows, width), jnp.bfloat16),
        cost_estimate=cost,
        grid=(heads, rows // tile),
        in_specs=[
            pl.BlockSpec((tile * POOL, HD), lambda h, r: (r, h)),
            pl.BlockSpec((key_rows, HD), lambda h, r: (0, h + head_lo)),
            pl.BlockSpec((key_rows, HD), lambda h, r: (0, h + head_lo)),
        ],
        out_specs=pl.BlockSpec((tile, HD), lambda h, r: (r, h)),
    )(queries, keys, values)


def head_permutes(matrix):
    count = lax.axis_size("head")
    me = lax.axis_index("head")
    rows, total = matrix.shape
    chunks = matrix.reshape(rows, count, total // count)
    by_shift = [lax.dynamic_index_in_dim(chunks, me, axis=1, keepdims=False)]
    for shift in range(1, count):
        piece = lax.dynamic_index_in_dim(chunks, (me + shift) % count, axis=1, keepdims=False)
        by_shift.append(
            lax.ppermute(piece, "head", [(i, (i + shift) % count) for i in range(count)])
        )
    stacked = jnp.stack(by_shift, axis=0)
    order = (me - jnp.arange(count, dtype=jnp.int32)) % count
    return jnp.take(stacked, order, axis=0).reshape(count * rows, total // count)


def parcel_kernel(tbl_ref, k_ref, v_ref, ko_ref, vo_ref):
    ko_ref[...] = k_ref[...]
    vo_ref[...] = v_ref[...]


def build_parcels(send_table, keys, values):
    slots = send_table.shape[0]
    width = keys.shape[1]
    pick = pl.BlockSpec((BLOCK, width), lambda s, t: (t[s], 0))
    place = pl.BlockSpec((BLOCK, width), lambda s, t: (s, 0))
    shape = jax.ShapeDtypeStruct((slots * BLOCK, width), keys.dtype)
    return pl.pallas_call(
        parcel_kernel,
        out_shape=(shape, shape),
        grid_spec=pltpu.PrefetchScalarGridSpec(
            num_scalar_prefetch=1,
            grid=(slots,),
            in_specs=[pick, pick],
            out_specs=(place, place),
        ),
        cost_estimate=pl.CostEstimate(
            flops=0, transcendentals=0, bytes_accessed=8 * slots * BLOCK * width
        ),
    )(send_table, keys, values)


def on_device(query_in, key_in, value_in, block_lists):
    key_rows = lax.all_to_all(key_in, "head", split_axis=1, concat_axis=0, tiled=True)
    value_rows = head_permutes(value_in)
    seq_rows, width = key_rows.shape
    head_count = lax.axis_size("head")
    heads = width // HD
    first = max(1, heads // 2)
    spans = [(lo, n) for lo, n in ((0, first), (first, heads - first)) if n > 0]
    queries = lax.all_to_all(query_in, "head", split_axis=1, concat_axis=0, tiled=True)

    draft_keys = lax.all_gather(pool_tokens(key_rows), "seq", axis=0, tiled=True)
    draft_values = lax.all_gather(pool_tokens(value_rows), "seq", axis=0, tiled=True)

    seq_count = lax.axis_size("seq")
    seq_index = lax.axis_index("seq")
    per_dev = seq_rows // BLOCK
    block_total, select_count = block_lists.shape
    block_ids = jnp.arange(block_total, dtype=jnp.int32)
    touched = jnp.any(block_lists[:, :, None] == block_ids[None, None, :], axis=1)
    needed = jnp.any(touched.reshape(seq_count, per_dev, seq_count, per_dev), axis=1)
    slot_rank = jnp.cumsum(needed.astype(jnp.int32), axis=2) - 1
    send_need = lax.dynamic_index_in_dim(needed, seq_index, axis=1, keepdims=False)
    send_rank = lax.dynamic_index_in_dim(slot_rank, seq_index, axis=1, keepdims=False)
    slot_hit = send_need[:, None, :] & (
        send_rank[:, None, :] == jnp.arange(CAP, dtype=jnp.int32)[None, :, None]
    )
    send_idx = jnp.sum(
        jnp.where(slot_hit, jnp.arange(per_dev, dtype=jnp.int32)[None, None, :], 0), axis=2
    )
    peers = (seq_index + jnp.arange(1, seq_count, dtype=jnp.int32)) % seq_count
    send_table = jnp.clip(jnp.take(send_idx, peers, axis=0), 0, per_dev - 1).reshape(-1)
    key_parcels, value_parcels = build_parcels(send_table, key_rows, value_rows)

    def exchange(parcels):
        arrivals = []
        for shift in range(1, seq_count):
            parcel = parcels[(shift - 1) * CAP * BLOCK:shift * CAP * BLOCK]
            arrivals.append(
                lax.ppermute(
                    parcel, "seq", [(i, (i + shift) % seq_count) for i in range(seq_count)]
                )
            )
        return arrivals

    remote_keys = exchange(key_parcels)
    remote_values = exchange(value_parcels)

    own_lists = lax.dynamic_slice_in_dim(block_lists, seq_index * per_dev, per_dev, 0)
    owners = own_lists // per_dev
    within = own_lists % per_dev
    own_rank = lax.dynamic_index_in_dim(slot_rank, seq_index, axis=0, keepdims=False)
    ranks_used = jnp.clip(own_rank[owners, within], 0, CAP - 1)
    distance = (seq_index - owners) % seq_count
    joint_pos = jnp.where(distance == 0, within, per_dev + (distance - 1) * CAP + ranks_used)
    table = jnp.clip(joint_pos, 0, per_dev + (seq_count - 1) * CAP - 1).reshape(-1).astype(jnp.int32)

    pieces = []
    for index, (head_lo, count) in enumerate(spans):
        rows_part = sparse_attention(
            table, queries, key_rows, value_rows, remote_keys, remote_values,
            head_lo, count, head_lo,
        )
        if index == len(spans) - 1:
            rows_part, draft_keys, draft_values = lax.optimization_barrier(
                (rows_part, draft_keys, draft_values)
            )
        back = lax.all_to_all(rows_part, "head", split_axis=0, concat_axis=1, tiled=True)
        pieces.append(back.reshape(back.shape[0], -1, count * HD))
    sparse_out = jnp.concatenate(pieces, axis=2).reshape(pieces[0].shape[0], -1)
    draft_out = draft_attention(queries, draft_keys, draft_values, 0)
    return (draft_out, sparse_out)


def solution(mesh):
    return jax.shard_map(
        on_device,
        mesh=mesh,
        in_specs=(
            P(("groups", "seq", "head"), None),
            P(("groups", "seq", "head"), None),
            P(("groups", "seq", "head"), None),
            P("groups", None),
        ),
        out_specs=(P(("groups", "seq"), "head"), P(("groups", "seq", "head"), None)),
        check_vma=False,
    )
```

```python
import jax
import jax.numpy as jnp
from jax import lax
from jax.experimental import pallas as pl
from jax.experimental.pallas import tpu as pltpu
from jax.sharding import PartitionSpec as P

HD = 128
BLOCK = 128
POOL = 4
CAP = 2
SCALE = HD ** (-0.5)
DRAFT_ROWS = 128
PAIR = 4
EXP2_SCALE = SCALE * 1.4426950408889634


def pool_tokens(matrix):
    grouped = matrix.astype(jnp.float32).reshape(matrix.shape[0] // POOL, POOL, matrix.shape[1])
    return (grouped.sum(axis=1) * POOL ** (-0.5)).astype(jnp.bfloat16)


def sparse_kernel(tbl_ref, q_ref, *refs):
    near_k, near_v = refs[0], refs[1]
    far_count = (len(refs) - 5) // 2
    far_k = refs[2:2 + far_count]
    far_v = refs[2 + far_count:2 + 2 * far_count]
    o_ref, kall_ref, vall_ref = refs[2 + 2 * far_count:]
    per_dev = q_ref.shape[0] // BLOCK
    sel = tbl_ref.shape[0] // per_dev
    near_rows = near_k.shape[0]
    kall_ref[0:near_rows, :] = near_k[...]
    vall_ref[0:near_rows, :] = near_v[...]
    offset = near_rows
    for kr, vr in zip(far_k, far_v):
        kall_ref[offset:offset + kr.shape[0], :] = kr[...]
        vall_ref[offset:offset + vr.shape[0], :] = vr[...]
        offset += kr.shape[0]
    last = offset // BLOCK - 1

    def one_block(i):
        row = pl.multiple_of(i * BLOCK, BLOCK)
        keys = []
        values = []
        for j in range(sel):
            start = pl.multiple_of(jnp.clip(tbl_ref[i * sel + j], 0, last) * BLOCK, BLOCK)
            keys.append(kall_ref[pl.ds(start, BLOCK), :])
            values.append(vall_ref[pl.ds(start, BLOCK), :])
        raw = lax.dot_general(
            q_ref[pl.ds(row, BLOCK), :], jnp.concatenate(keys, axis=0),
            (((1,), (1,)), ((), ())), preferred_element_type=jnp.float32,
        )
        running = jnp.max(raw, axis=1, keepdims=True)
        weights = jnp.exp2((raw - running) * EXP2_SCALE)
        totals = jnp.sum(weights, axis=1, keepdims=True)
        weighted = jnp.dot(
            weights.astype(jnp.bfloat16), jnp.concatenate(values, axis=0),
            preferred_element_type=jnp.float32,
        )
        o_ref[pl.ds(row, BLOCK), :] = (weighted / totals).astype(o_ref.dtype)

    def body(i, carry):
        for lane in range(PAIR):
            one_block(i * PAIR + lane)
        return carry

    lax.fori_loop(0, per_dev // PAIR, body, 0)
    for i in range(per_dev - per_dev % PAIR, per_dev):
        one_block(i)


def sparse_attention(tbl, queries, keys, values, far_keys, far_values, head_lo, heads):
    rows = queries.shape[0]

    def column(h, t):
        return (0, h + head_lo)

    operands = [keys, values] + list(far_keys) + list(far_values)
    total_rows = keys.shape[0] + sum(k.shape[0] for k in far_keys)
    sel = tbl.shape[0] * BLOCK // rows
    cost = pl.CostEstimate(
        flops=4 * rows * sel * BLOCK * HD * heads,
        transcendentals=rows * sel * BLOCK * heads,
        bytes_accessed=2 * HD * heads * (2 * rows + 2 * total_rows),
    )
    return pl.pallas_call(
        sparse_kernel,
        out_shape=jax.ShapeDtypeStruct((rows, heads * HD), jnp.bfloat16),
        cost_estimate=cost,
        grid_spec=pltpu.PrefetchScalarGridSpec(
            num_scalar_prefetch=1,
            grid=(heads,),
            in_specs=[pl.BlockSpec((rows, HD), lambda h, t: (0, h))]
            + [pl.BlockSpec((x.shape[0], HD), column) for x in operands],
            out_specs=pl.BlockSpec((rows, HD), lambda h, t: (0, h)),
            scratch_shapes=[
                pltpu.VMEM((total_rows, HD), jnp.bfloat16),
                pltpu.VMEM((total_rows, HD), jnp.bfloat16),
            ],
        ),
    )(tbl, queries, *operands)


def draft_kernel(q_ref, k_ref, v_ref, o_ref):
    tile = o_ref.shape[0]
    token = lax.broadcasted_iota(jnp.int32, (tile, tile * POOL), 1)
    draft = lax.broadcasted_iota(jnp.int32, (tile, tile * POOL), 0)
    pooling = jnp.where(token // POOL == draft, POOL ** (-0.5), 0.0).astype(jnp.bfloat16)
    pooled = jnp.dot(pooling, q_ref[...], preferred_element_type=jnp.float32).astype(jnp.bfloat16)
    raw = lax.dot_general(
        pooled, k_ref[...], (((1,), (1,)), ((), ())), preferred_element_type=jnp.float32
    )
    running = jnp.max(raw, axis=1, keepdims=True)
    weights = jnp.exp2((raw - running) * EXP2_SCALE)
    totals = jnp.sum(weights, axis=1, keepdims=True)
    weighted = jnp.dot(weights.astype(jnp.bfloat16), v_ref[...], preferred_element_type=jnp.float32)
    o_ref[...] = (weighted / totals).astype(o_ref.dtype)


def draft_attention(queries, keys, values, head_lo):
    token_rows, width = queries.shape
    rows = token_rows // POOL
    heads = width // HD
    key_rows = keys.shape[0]
    tile = min(DRAFT_ROWS, rows)
    cost = pl.CostEstimate(
        flops=4 * rows * key_rows * HD * heads + 2 * rows * tile * POOL * HD * heads,
        transcendentals=rows * key_rows * heads,
        bytes_accessed=2 * HD * heads * (token_rows + rows + 2 * key_rows),
    )
    return pl.pallas_call(
        draft_kernel,
        out_shape=jax.ShapeDtypeStruct((rows, width), jnp.bfloat16),
        cost_estimate=cost,
        grid=(heads, rows // tile),
        in_specs=[
            pl.BlockSpec((tile * POOL, HD), lambda h, r: (r, h)),
            pl.BlockSpec((key_rows, HD), lambda h, r: (0, h + head_lo)),
            pl.BlockSpec((key_rows, HD), lambda h, r: (0, h + head_lo)),
        ],
        out_specs=pl.BlockSpec((tile, HD), lambda h, r: (r, h)),
    )(queries, keys, values)


def head_permutes(matrix):
    count = lax.axis_size("head")
    me = lax.axis_index("head")
    rows, total = matrix.shape
    chunks = matrix.reshape(rows, count, total // count)
    by_shift = [lax.dynamic_index_in_dim(chunks, me, axis=1, keepdims=False)]
    for shift in range(1, count):
        piece = lax.dynamic_index_in_dim(chunks, (me + shift) % count, axis=1, keepdims=False)
        by_shift.append(
            lax.ppermute(piece, "head", [(i, (i + shift) % count) for i in range(count)])
        )
    stacked = jnp.stack(by_shift, axis=0)
    order = (me - jnp.arange(count, dtype=jnp.int32)) % count
    return jnp.take(stacked, order, axis=0).reshape(count * rows, total // count)


def on_device(query_in, key_in, value_in, block_lists):
    key_rows = lax.all_to_all(key_in, "head", split_axis=1, concat_axis=0, tiled=True)
    value_rows = head_permutes(value_in)
    seq_rows, width = key_rows.shape
    head_count = lax.axis_size("head")
    heads = width // HD
    first = max(1, heads // 2)
    spans = [(lo, n) for lo, n in ((0, first), (first, heads - first)) if n > 0]
    grouped_q = query_in.reshape(query_in.shape[0], head_count, width)
    query_slices = [
        grouped_q[:, :, lo * HD:(lo + n) * HD].reshape(query_in.shape[0], -1) for lo, n in spans
    ]

    def query_a2a(piece):
        return lax.all_to_all(piece, "head", split_axis=1, concat_axis=0, tiled=True)

    draft_keys = lax.all_gather(pool_tokens(key_rows), "seq", axis=0, tiled=True)
    draft_values = lax.all_gather(pool_tokens(value_rows), "seq", axis=0, tiled=True)

    seq_count = lax.axis_size("seq")
    seq_index = lax.axis_index("seq")
    per_dev = seq_rows // BLOCK
    block_total, select_count = block_lists.shape
    block_ids = jnp.arange(block_total, dtype=jnp.int32)
    touched = jnp.any(block_lists[:, :, None] == block_ids[None, None, :], axis=1)
    needed = jnp.any(touched.reshape(seq_count, per_dev, seq_count, per_dev), axis=1)
    slot_rank = jnp.cumsum(needed.astype(jnp.int32), axis=2) - 1
    send_need = lax.dynamic_index_in_dim(needed, seq_index, axis=1, keepdims=False)
    send_rank = lax.dynamic_index_in_dim(slot_rank, seq_index, axis=1, keepdims=False)
    slot_hit = send_need[:, None, :] & (
        send_rank[:, None, :] == jnp.arange(CAP, dtype=jnp.int32)[None, :, None]
    )
    send_idx = jnp.sum(
        jnp.where(slot_hit, jnp.arange(per_dev, dtype=jnp.int32)[None, None, :], 0), axis=2
    ).reshape(-1)
    def exchange(rows):
        blocks = jnp.take(rows.reshape(per_dev, BLOCK, width), send_idx, axis=0)
        outgoing = blocks.reshape(seq_count, CAP, BLOCK, width)
        arrivals = []
        for shift in range(1, seq_count):
            parcel = lax.dynamic_index_in_dim(
                outgoing, (seq_index + shift) % seq_count, axis=0, keepdims=False
            )
            arrivals.append(
                lax.ppermute(
                    parcel, "seq", [(i, (i + shift) % seq_count) for i in range(seq_count)]
                )
            )
        return [a.reshape(CAP * BLOCK, width) for a in arrivals]

    remote_keys = exchange(key_rows)
    remote_values = exchange(value_rows)
    leading, remote_values = lax.optimization_barrier((query_slices[0], remote_values))
    query_parts = [query_a2a(leading)]
    later, remote_keys = lax.optimization_barrier((query_slices[1:], remote_keys))
    query_parts += [query_a2a(piece) for piece in later]

    own_lists = lax.dynamic_slice_in_dim(block_lists, seq_index * per_dev, per_dev, 0)
    owners = own_lists // per_dev
    within = own_lists % per_dev
    own_rank = lax.dynamic_index_in_dim(slot_rank, seq_index, axis=0, keepdims=False)
    ranks_used = jnp.clip(own_rank[owners, within], 0, CAP - 1)
    distance = (seq_index - owners) % seq_count
    joint_pos = jnp.where(distance == 0, within, per_dev + (distance - 1) * CAP + ranks_used)
    table = jnp.clip(joint_pos, 0, per_dev + (seq_count - 1) * CAP - 1).reshape(-1).astype(jnp.int32)

    pieces = []
    for index, ((head_lo, count), queries) in enumerate(zip(spans, query_parts)):
        rows_part = sparse_attention(
            table, queries, key_rows, value_rows, remote_keys, remote_values, head_lo, count,
        )
        if index == len(spans) - 1:
            rows_part, draft_keys, draft_values = lax.optimization_barrier(
                (rows_part, draft_keys, draft_values)
            )
        back = lax.all_to_all(rows_part, "head", split_axis=0, concat_axis=1, tiled=True)
        pieces.append(back.reshape(back.shape[0], -1, count * HD))
    sparse_out = jnp.concatenate(pieces, axis=2).reshape(pieces[0].shape[0], -1)
    draft_out = jnp.concatenate(
        [
            draft_attention(queries, draft_keys, draft_values, head_lo)
            for (head_lo, count), queries in zip(spans, query_parts)
        ],
        axis=1,
    )
    return (draft_out, sparse_out)


def solution(mesh):
    return jax.shard_map(
        on_device,
        mesh=mesh,
        in_specs=(
            P(("groups", "seq", "head"), None),
            P(("groups", "seq", "head"), None),
            P(("groups", "seq", "head"), None),
            P("groups", None),
        ),
        out_specs=(P(("groups", "seq"), "head"), P(("groups", "seq", "head"), None)),
        check_vma=False,
    )
```

```python
import jax
import jax.numpy as jnp
from jax import lax
from jax.experimental import pallas as pl
from jax.experimental.pallas import tpu as pltpu
from jax.sharding import PartitionSpec as P

HD = 128
BLOCK = 128
POOL = 4
CAP = 2
SCALE = HD ** (-0.5)
DRAFT_ROWS = 128
PAIR = 4
EXP2_SCALE = SCALE * 1.4426950408889634


def pool_tokens(matrix):
    grouped = matrix.astype(jnp.float32).reshape(matrix.shape[0] // POOL, POOL, matrix.shape[1])
    return (grouped.sum(axis=1) * POOL ** (-0.5)).astype(jnp.bfloat16)


def sparse_kernel(tbl_ref, q_ref, *refs):
    near_k, near_v = refs[0], refs[1]
    far_count = (len(refs) - 5) // 2
    far_k = refs[2:2 + far_count]
    far_v = refs[2 + far_count:2 + 2 * far_count]
    o_ref, kall_ref, vall_ref = refs[2 + 2 * far_count:]
    per_dev = q_ref.shape[0] // BLOCK
    sel = tbl_ref.shape[0] // per_dev
    near_rows = near_k.shape[0]
    kall_ref[0:near_rows, :] = near_k[...]
    vall_ref[0:near_rows, :] = near_v[...]
    offset = near_rows
    for kr, vr in zip(far_k, far_v):
        kall_ref[offset:offset + kr.shape[0], :] = kr[...]
        vall_ref[offset:offset + vr.shape[0], :] = vr[...]
        offset += kr.shape[0]
    last = offset // BLOCK - 1

    def one_block(i):
        row = pl.multiple_of(i * BLOCK, BLOCK)
        keys = []
        values = []
        for j in range(sel):
            start = pl.multiple_of(jnp.clip(tbl_ref[i * sel + j], 0, last) * BLOCK, BLOCK)
            keys.append(kall_ref[pl.ds(start, BLOCK), :])
            values.append(vall_ref[pl.ds(start, BLOCK), :])
        raw = lax.dot_general(
            q_ref[pl.ds(row, BLOCK), :], jnp.concatenate(keys, axis=0),
            (((1,), (1,)), ((), ())), preferred_element_type=jnp.float32,
        )
        running = jnp.max(raw, axis=1, keepdims=True)
        weights = jnp.exp2((raw - running) * EXP2_SCALE)
        totals = jnp.sum(weights, axis=1, keepdims=True)
        weighted = jnp.dot(
            weights.astype(jnp.bfloat16), jnp.concatenate(values, axis=0),
            preferred_element_type=jnp.float32,
        )
        o_ref[pl.ds(row, BLOCK), :] = (weighted / totals).astype(o_ref.dtype)

    def body(i, carry):
        for lane in range(PAIR):
            one_block(i * PAIR + lane)
        return carry

    lax.fori_loop(0, per_dev // PAIR, body, 0)
    for i in range(per_dev - per_dev % PAIR, per_dev):
        one_block(i)


def sparse_attention(tbl, queries, keys, values, far_keys, far_values, head_lo, heads):
    rows = queries.shape[0]

    def column(h, t):
        return (0, h + head_lo)

    operands = [keys, values] + list(far_keys) + list(far_values)
    total_rows = keys.shape[0] + sum(k.shape[0] for k in far_keys)
    sel = tbl.shape[0] * BLOCK // rows
    cost = pl.CostEstimate(
        flops=4 * rows * sel * BLOCK * HD * heads,
        transcendentals=rows * sel * BLOCK * heads,
        bytes_accessed=2 * HD * heads * (2 * rows + 2 * total_rows),
    )
    return pl.pallas_call(
        sparse_kernel,
        out_shape=jax.ShapeDtypeStruct((rows, heads * HD), jnp.bfloat16),
        cost_estimate=cost,
        grid_spec=pltpu.PrefetchScalarGridSpec(
            num_scalar_prefetch=1,
            grid=(heads,),
            in_specs=[pl.BlockSpec((rows, HD), lambda h, t: (0, h))]
            + [pl.BlockSpec((x.shape[0], HD), column) for x in operands],
            out_specs=pl.BlockSpec((rows, HD), lambda h, t: (0, h)),
            scratch_shapes=[
                pltpu.VMEM((total_rows, HD), jnp.bfloat16),
                pltpu.VMEM((total_rows, HD), jnp.bfloat16),
            ],
        ),
    )(tbl, queries, *operands)


def draft_kernel(q_ref, k_ref, v_ref, o_ref):
    tile = o_ref.shape[0]
    token = lax.broadcasted_iota(jnp.int32, (tile, tile * POOL), 1)
    draft = lax.broadcasted_iota(jnp.int32, (tile, tile * POOL), 0)
    pooling = jnp.where(token // POOL == draft, POOL ** (-0.5), 0.0).astype(jnp.bfloat16)
    pooled = jnp.dot(pooling, q_ref[...], preferred_element_type=jnp.float32).astype(jnp.bfloat16)
    raw = lax.dot_general(
        pooled, k_ref[...], (((1,), (1,)), ((), ())), preferred_element_type=jnp.float32
    )
    running = jnp.max(raw, axis=1, keepdims=True)
    weights = jnp.exp2((raw - running) * EXP2_SCALE)
    totals = jnp.sum(weights, axis=1, keepdims=True)
    weighted = jnp.dot(weights.astype(jnp.bfloat16), v_ref[...], preferred_element_type=jnp.float32)
    o_ref[...] = (weighted / totals).astype(o_ref.dtype)


def draft_attention(queries, keys, values, head_lo):
    token_rows, width = queries.shape
    rows = token_rows // POOL
    heads = width // HD
    key_rows = keys.shape[0]
    tile = min(DRAFT_ROWS, rows)
    cost = pl.CostEstimate(
        flops=4 * rows * key_rows * HD * heads + 2 * rows * tile * POOL * HD * heads,
        transcendentals=rows * key_rows * heads,
        bytes_accessed=2 * HD * heads * (token_rows + rows + 2 * key_rows),
    )
    return pl.pallas_call(
        draft_kernel,
        out_shape=jax.ShapeDtypeStruct((rows, width), jnp.bfloat16),
        cost_estimate=cost,
        grid=(heads, rows // tile),
        in_specs=[
            pl.BlockSpec((tile * POOL, HD), lambda h, r: (r, h)),
            pl.BlockSpec((key_rows, HD), lambda h, r: (0, h + head_lo)),
            pl.BlockSpec((key_rows, HD), lambda h, r: (0, h + head_lo)),
        ],
        out_specs=pl.BlockSpec((tile, HD), lambda h, r: (r, h)),
    )(queries, keys, values)


def head_permutes(matrix):
    count = lax.axis_size("head")
    me = lax.axis_index("head")
    rows, total = matrix.shape
    chunks = matrix.reshape(rows, count, total // count)
    by_shift = [lax.dynamic_index_in_dim(chunks, me, axis=1, keepdims=False)]
    for shift in range(1, count):
        piece = lax.dynamic_index_in_dim(chunks, (me + shift) % count, axis=1, keepdims=False)
        by_shift.append(
            lax.ppermute(piece, "head", [(i, (i + shift) % count) for i in range(count)])
        )
    stacked = jnp.stack(by_shift, axis=0)
    order = (me - jnp.arange(count, dtype=jnp.int32)) % count
    return jnp.take(stacked, order, axis=0).reshape(count * rows, total // count)


def on_device(query_in, key_in, value_in, block_lists):
    token_rows, total = query_in.shape
    head_count = lax.axis_size("head")
    width = total // head_count
    seq_rows = token_rows * head_count
    heads = width // HD
    first = max(1, heads // 2)
    spans = [(lo, n) for lo, n in ((0, first), (first, heads - first)) if n > 0]

    def head_slice(matrix, lo, n):
        grouped = matrix.reshape(token_rows, head_count, width)
        return grouped[:, :, lo * HD:(lo + n) * HD].reshape(token_rows, -1)

    seq_count = lax.axis_size("seq")
    seq_index = lax.axis_index("seq")
    per_dev = seq_rows // BLOCK
    block_total, select_count = block_lists.shape
    block_ids = jnp.arange(block_total, dtype=jnp.int32)
    touched = jnp.any(block_lists[:, :, None] == block_ids[None, None, :], axis=1)
    needed = jnp.any(touched.reshape(seq_count, per_dev, seq_count, per_dev), axis=1)
    slot_rank = jnp.cumsum(needed.astype(jnp.int32), axis=2) - 1
    send_need = lax.dynamic_index_in_dim(needed, seq_index, axis=1, keepdims=False)
    send_rank = lax.dynamic_index_in_dim(slot_rank, seq_index, axis=1, keepdims=False)
    slot_hit = send_need[:, None, :] & (
        send_rank[:, None, :] == jnp.arange(CAP, dtype=jnp.int32)[None, :, None]
    )
    send_idx = jnp.sum(
        jnp.where(slot_hit, jnp.arange(per_dev, dtype=jnp.int32)[None, None, :], 0), axis=2
    ).reshape(-1)

    def exchange(rows):
        span_width = rows.shape[1]
        blocks = jnp.take(rows.reshape(per_dev, BLOCK, span_width), send_idx, axis=0)
        outgoing = blocks.reshape(seq_count, CAP, BLOCK, span_width)
        arrivals = []
        for shift in range(1, seq_count):
            parcel = lax.dynamic_index_in_dim(
                outgoing, (seq_index + shift) % seq_count, axis=0, keepdims=False
            )
            arrivals.append(
                lax.ppermute(
                    parcel, "seq", [(i, (i + shift) % seq_count) for i in range(seq_count)]
                )
            )
        return [a.reshape(CAP * BLOCK, span_width) for a in arrivals]

    own_lists = lax.dynamic_slice_in_dim(block_lists, seq_index * per_dev, per_dev, 0)
    owners = own_lists // per_dev
    within = own_lists % per_dev
    own_rank = lax.dynamic_index_in_dim(slot_rank, seq_index, axis=0, keepdims=False)
    ranks_used = jnp.clip(own_rank[owners, within], 0, CAP - 1)
    distance = (seq_index - owners) % seq_count
    joint_pos = jnp.where(distance == 0, within, per_dev + (distance - 1) * CAP + ranks_used)
    table = jnp.clip(joint_pos, 0, per_dev + (seq_count - 1) * CAP - 1).reshape(-1).astype(jnp.int32)

    staged = []
    for lo, n in spans:
        key_rows = lax.all_to_all(
            head_slice(key_in, lo, n), "head", split_axis=1, concat_axis=0, tiled=True
        )
        value_rows = head_permutes(head_slice(value_in, lo, n))
        remote_keys = exchange(key_rows)
        remote_values = exchange(value_rows)
        query_piece, remote_keys, remote_values = lax.optimization_barrier(
            (head_slice(query_in, lo, n), remote_keys, remote_values)
        )
        queries = lax.all_to_all(query_piece, "head", split_axis=1, concat_axis=0, tiled=True)
        draft_keys = lax.all_gather(pool_tokens(key_rows), "seq", axis=0, tiled=True)
        draft_values = lax.all_gather(pool_tokens(value_rows), "seq", axis=0, tiled=True)
        staged.append(
            (n, queries, key_rows, value_rows, remote_keys, remote_values, draft_keys, draft_values)
        )

    pieces = []
    drafts = []
    for index, item in enumerate(staged):
        n, queries, key_rows, value_rows, remote_keys, remote_values, draft_keys, draft_values = item
        rows_part = sparse_attention(
            table, queries, key_rows, value_rows, remote_keys, remote_values, 0, n,
        )
        if index == len(staged) - 1:
            rows_part, draft_keys, draft_values = lax.optimization_barrier(
                (rows_part, draft_keys, draft_values)
            )
        back = lax.all_to_all(rows_part, "head", split_axis=0, concat_axis=1, tiled=True)
        pieces.append(back.reshape(back.shape[0], -1, n * HD))
        drafts.append((queries, draft_keys, draft_values))
    sparse_out = jnp.concatenate(pieces, axis=2).reshape(pieces[0].shape[0], -1)
    draft_out = jnp.concatenate(
        [draft_attention(q, k, v, 0) for q, k, v in drafts], axis=1
    )
    return (draft_out, sparse_out)


def solution(mesh):
    return jax.shard_map(
        on_device,
        mesh=mesh,
        in_specs=(
            P(("groups", "seq", "head"), None),
            P(("groups", "seq", "head"), None),
            P(("groups", "seq", "head"), None),
            P("groups", None),
        ),
        out_specs=(P(("groups", "seq"), "head"), P(("groups", "seq", "head"), None)),
        check_vma=False,
    )
```

```python
import jax
import jax.numpy as jnp
from jax import lax
from jax.experimental import pallas as pl
from jax.experimental.pallas import tpu as pltpu
from jax.sharding import PartitionSpec as P

HD = 128
BLOCK = 128
POOL = 4
CAP = 2
SCALE = HD ** (-0.5)
DRAFT_ROWS = 128
PAIR = 4
EXP2_SCALE = SCALE * 1.4426950408889634


def pool_tokens(matrix):
    grouped = matrix.astype(jnp.float32).reshape(matrix.shape[0] // POOL, POOL, matrix.shape[1])
    return (grouped.sum(axis=1) * POOL ** (-0.5)).astype(jnp.bfloat16)


def sparse_kernel(tbl_ref, q_ref, *refs):
    near_k, near_v = refs[0], refs[1]
    far_count = (len(refs) - 5) // 2
    far_k = refs[2:2 + far_count]
    far_v = refs[2 + far_count:2 + 2 * far_count]
    o_ref, kall_ref, vall_ref = refs[2 + 2 * far_count:]
    per_dev = q_ref.shape[0] // BLOCK
    sel = tbl_ref.shape[0] // per_dev
    near_rows = near_k.shape[0]
    kall_ref[0:near_rows, :] = near_k[...]
    vall_ref[0:near_rows, :] = near_v[...]
    offset = near_rows
    for kr, vr in zip(far_k, far_v):
        kall_ref[offset:offset + kr.shape[0], :] = kr[...]
        vall_ref[offset:offset + vr.shape[0], :] = vr[...]
        offset += kr.shape[0]
    last = offset // BLOCK - 1

    def one_block(i):
        row = pl.multiple_of(i * BLOCK, BLOCK)
        keys = []
        values = []
        for j in range(sel):
            start = pl.multiple_of(jnp.clip(tbl_ref[i * sel + j], 0, last) * BLOCK, BLOCK)
            keys.append(kall_ref[pl.ds(start, BLOCK), :])
            values.append(vall_ref[pl.ds(start, BLOCK), :])
        raw = lax.dot_general(
            q_ref[pl.ds(row, BLOCK), :], jnp.concatenate(keys, axis=0),
            (((1,), (1,)), ((), ())), preferred_element_type=jnp.float32,
        )
        running = jnp.max(raw, axis=1, keepdims=True)
        weights = jnp.exp2((raw - running) * EXP2_SCALE)
        totals = jnp.sum(weights, axis=1, keepdims=True)
        weighted = jnp.dot(
            weights.astype(jnp.bfloat16), jnp.concatenate(values, axis=0),
            preferred_element_type=jnp.float32,
        )
        o_ref[pl.ds(row, BLOCK), :] = (weighted / totals).astype(o_ref.dtype)

    def body(i, carry):
        for lane in range(PAIR):
            one_block(i * PAIR + lane)
        return carry

    lax.fori_loop(0, per_dev // PAIR, body, 0)
    for i in range(per_dev - per_dev % PAIR, per_dev):
        one_block(i)


def sparse_attention(tbl, queries, keys, values, far_keys, far_values, head_lo, heads):
    rows = queries.shape[0]

    def column(h, t):
        return (0, h + head_lo)

    operands = [keys, values] + list(far_keys) + list(far_values)
    total_rows = keys.shape[0] + sum(k.shape[0] for k in far_keys)
    sel = tbl.shape[0] * BLOCK // rows
    cost = pl.CostEstimate(
        flops=4 * rows * sel * BLOCK * HD * heads,
        transcendentals=rows * sel * BLOCK * heads,
        bytes_accessed=2 * HD * heads * (2 * rows + 2 * total_rows),
    )
    return pl.pallas_call(
        sparse_kernel,
        out_shape=jax.ShapeDtypeStruct((rows, heads * HD), jnp.bfloat16),
        cost_estimate=cost,
        grid_spec=pltpu.PrefetchScalarGridSpec(
            num_scalar_prefetch=1,
            grid=(heads,),
            in_specs=[pl.BlockSpec((rows, HD), lambda h, t: (0, h))]
            + [pl.BlockSpec((x.shape[0], HD), column) for x in operands],
            out_specs=pl.BlockSpec((rows, HD), lambda h, t: (0, h)),
            scratch_shapes=[
                pltpu.VMEM((total_rows, HD), jnp.bfloat16),
                pltpu.VMEM((total_rows, HD), jnp.bfloat16),
            ],
        ),
    )(tbl, queries, *operands)


def draft_kernel(q_ref, k_ref, v_ref, o_ref):
    tile = o_ref.shape[0]
    token = lax.broadcasted_iota(jnp.int32, (tile, tile * POOL), 1)
    draft = lax.broadcasted_iota(jnp.int32, (tile, tile * POOL), 0)
    pooling = jnp.where(token // POOL == draft, POOL ** (-0.5), 0.0).astype(jnp.bfloat16)
    pooled = jnp.dot(pooling, q_ref[...], preferred_element_type=jnp.float32).astype(jnp.bfloat16)
    raw = lax.dot_general(
        pooled, k_ref[...], (((1,), (1,)), ((), ())), preferred_element_type=jnp.float32
    )
    running = jnp.max(raw, axis=1, keepdims=True)
    weights = jnp.exp2((raw - running) * EXP2_SCALE)
    totals = jnp.sum(weights, axis=1, keepdims=True)
    weighted = jnp.dot(weights.astype(jnp.bfloat16), v_ref[...], preferred_element_type=jnp.float32)
    o_ref[...] = (weighted / totals).astype(o_ref.dtype)


def draft_attention(queries, keys, values, head_lo):
    token_rows, width = queries.shape
    rows = token_rows // POOL
    heads = width // HD
    key_rows = keys.shape[0]
    tile = min(DRAFT_ROWS, rows)
    cost = pl.CostEstimate(
        flops=4 * rows * key_rows * HD * heads + 2 * rows * tile * POOL * HD * heads,
        transcendentals=rows * key_rows * heads,
        bytes_accessed=2 * HD * heads * (token_rows + rows + 2 * key_rows),
    )
    return pl.pallas_call(
        draft_kernel,
        out_shape=jax.ShapeDtypeStruct((rows, width), jnp.bfloat16),
        cost_estimate=cost,
        grid=(heads, rows // tile),
        in_specs=[
            pl.BlockSpec((tile * POOL, HD), lambda h, r: (r, h)),
            pl.BlockSpec((key_rows, HD), lambda h, r: (0, h + head_lo)),
            pl.BlockSpec((key_rows, HD), lambda h, r: (0, h + head_lo)),
        ],
        out_specs=pl.BlockSpec((tile, HD), lambda h, r: (r, h)),
    )(queries, keys, values)


def head_permutes(matrix):
    count = lax.axis_size("head")
    me = lax.axis_index("head")
    rows, total = matrix.shape
    chunks = matrix.reshape(rows, count, total // count)
    by_shift = [lax.dynamic_index_in_dim(chunks, me, axis=1, keepdims=False)]
    for shift in range(1, count):
        piece = lax.dynamic_index_in_dim(chunks, (me + shift) % count, axis=1, keepdims=False)
        by_shift.append(
            lax.ppermute(piece, "head", [(i, (i + shift) % count) for i in range(count)])
        )
    stacked = jnp.stack(by_shift, axis=0)
    order = (me - jnp.arange(count, dtype=jnp.int32)) % count
    return jnp.take(stacked, order, axis=0).reshape(count * rows, total // count)


def on_device(query_in, key_in, value_in, block_lists):
    key_rows = lax.all_to_all(key_in, "head", split_axis=1, concat_axis=0, tiled=True)
    value_rows = head_permutes(value_in)
    seq_rows, width = key_rows.shape
    head_count = lax.axis_size("head")
    heads = width // HD
    first = max(1, heads // 2)
    spans = [(lo, n) for lo, n in ((0, first), (first, heads - first)) if n > 0]
    grouped_q = query_in.reshape(query_in.shape[0], head_count, width)
    query_slices = [
        grouped_q[:, :, lo * HD:(lo + n) * HD].reshape(query_in.shape[0], -1) for lo, n in spans
    ]

    def query_a2a(piece):
        return lax.all_to_all(piece, "head", split_axis=1, concat_axis=0, tiled=True)

    draft_keys = lax.all_gather(pool_tokens(key_rows), "seq", axis=0, tiled=True)
    draft_values = lax.all_gather(pool_tokens(value_rows), "seq", axis=0, tiled=True)

    seq_count = lax.axis_size("seq")
    seq_index = lax.axis_index("seq")
    per_dev = seq_rows // BLOCK
    block_total, select_count = block_lists.shape
    block_ids = jnp.arange(block_total, dtype=jnp.int32)
    touched = jnp.any(block_lists[:, :, None] == block_ids[None, None, :], axis=1)
    needed = jnp.any(touched.reshape(seq_count, per_dev, seq_count, per_dev), axis=1)
    slot_rank = jnp.cumsum(needed.astype(jnp.int32), axis=2) - 1
    send_need = lax.dynamic_index_in_dim(needed, seq_index, axis=1, keepdims=False)
    send_rank = lax.dynamic_index_in_dim(slot_rank, seq_index, axis=1, keepdims=False)
    slot_hit = send_need[:, None, :] & (
        send_rank[:, None, :] == jnp.arange(CAP, dtype=jnp.int32)[None, :, None]
    )
    send_idx = jnp.sum(
        jnp.where(slot_hit, jnp.arange(per_dev, dtype=jnp.int32)[None, None, :], 0), axis=2
    ).reshape(-1)
    def exchange(rows):
        blocks = jnp.take(rows.reshape(per_dev, BLOCK, width), send_idx, axis=0)
        outgoing = blocks.reshape(seq_count, CAP, BLOCK, width)
        arrivals = []
        for shift in range(1, seq_count):
            parcel = lax.dynamic_index_in_dim(
                outgoing, (seq_index + shift) % seq_count, axis=0, keepdims=False
            )
            arrivals.append(
                lax.ppermute(
                    parcel, "seq", [(i, (i + shift) % seq_count) for i in range(seq_count)]
                )
            )
        return [a.reshape(CAP * BLOCK, width) for a in arrivals]

    own_lists = lax.dynamic_slice_in_dim(block_lists, seq_index * per_dev, per_dev, 0)
    owners = own_lists // per_dev
    within = own_lists % per_dev
    own_rank = lax.dynamic_index_in_dim(slot_rank, seq_index, axis=0, keepdims=False)
    ranks_used = jnp.clip(own_rank[owners, within], 0, CAP - 1)
    distance = (seq_index - owners) % seq_count
    joint_pos = jnp.where(distance == 0, within, per_dev + (distance - 1) * CAP + ranks_used)
    table = jnp.clip(joint_pos, 0, per_dev + (seq_count - 1) * CAP - 1).reshape(-1).astype(jnp.int32)

    remote_keys = exchange(key_rows)
    remote_values = exchange(value_rows)
    leading, remote_values, value_rows, table = lax.optimization_barrier(
        (query_slices[0], remote_values, value_rows, table)
    )
    query_parts = [query_a2a(leading)]
    later, remote_keys = lax.optimization_barrier((query_slices[1:], remote_keys))
    query_parts += [query_a2a(piece) for piece in later]

    pieces = []
    for index, ((head_lo, count), queries) in enumerate(zip(spans, query_parts)):
        rows_part = sparse_attention(
            table, queries, key_rows, value_rows, remote_keys, remote_values, head_lo, count,
        )
        if index == len(spans) - 1:
            rows_part, draft_keys, draft_values = lax.optimization_barrier(
                (rows_part, draft_keys, draft_values)
            )
        back = lax.all_to_all(rows_part, "head", split_axis=0, concat_axis=1, tiled=True)
        pieces.append(back.reshape(back.shape[0], -1, count * HD))
    sparse_out = jnp.concatenate(pieces, axis=2).reshape(pieces[0].shape[0], -1)
    draft_out = jnp.concatenate(
        [
            draft_attention(queries, draft_keys, draft_values, head_lo)
            for (head_lo, count), queries in zip(spans, query_parts)
        ],
        axis=1,
    )
    return (draft_out, sparse_out)


def solution(mesh):
    return jax.shard_map(
        on_device,
        mesh=mesh,
        in_specs=(
            P(("groups", "seq", "head"), None),
            P(("groups", "seq", "head"), None),
            P(("groups", "seq", "head"), None),
            P("groups", None),
        ),
        out_specs=(P(("groups", "seq"), "head"), P(("groups", "seq", "head"), None)),
        check_vma=False,
    )
```

```python
import jax
import jax.numpy as jnp
from jax import lax
from jax.experimental import pallas as pl
from jax.experimental.pallas import tpu as pltpu
from jax.sharding import PartitionSpec as P

HD = 128
BLOCK = 128
POOL = 4
CAP = 2
SCALE = HD ** (-0.5)
DRAFT_ROWS = 128
PAIR = 4
EXP2_SCALE = SCALE * 1.4426950408889634


def pool_tokens(matrix):
    grouped = matrix.astype(jnp.float32).reshape(matrix.shape[0] // POOL, POOL, matrix.shape[1])
    return (grouped.sum(axis=1) * POOL ** (-0.5)).astype(jnp.bfloat16)


def sparse_kernel(tbl_ref, q_ref, *refs):
    near_k, near_v = refs[0], refs[1]
    far_count = (len(refs) - 5) // 2
    far_k = refs[2:2 + far_count]
    far_v = refs[2 + far_count:2 + 2 * far_count]
    o_ref, kall_ref, vall_ref = refs[2 + 2 * far_count:]
    per_dev = q_ref.shape[0] // BLOCK
    sel = tbl_ref.shape[0] // per_dev
    near_rows = near_k.shape[0]
    kall_ref[0:near_rows, :] = near_k[...]
    vall_ref[0:near_rows, :] = near_v[...]
    offset = near_rows
    for kr, vr in zip(far_k, far_v):
        kall_ref[offset:offset + kr.shape[0], :] = kr[...]
        vall_ref[offset:offset + vr.shape[0], :] = vr[...]
        offset += kr.shape[0]
    last = offset // BLOCK - 1

    def one_block(i):
        row = pl.multiple_of(i * BLOCK, BLOCK)
        keys = []
        values = []
        for j in range(sel):
            start = pl.multiple_of(jnp.clip(tbl_ref[i * sel + j], 0, last) * BLOCK, BLOCK)
            keys.append(kall_ref[pl.ds(start, BLOCK), :])
            values.append(vall_ref[pl.ds(start, BLOCK), :])
        raw = lax.dot_general(
            q_ref[pl.ds(row, BLOCK), :], jnp.concatenate(keys, axis=0),
            (((1,), (1,)), ((), ())), preferred_element_type=jnp.float32,
        )
        running = jnp.max(raw, axis=1, keepdims=True)
        weights = jnp.exp2((raw - running) * EXP2_SCALE)
        totals = jnp.sum(weights, axis=1, keepdims=True)
        weighted = jnp.dot(
            weights.astype(jnp.bfloat16), jnp.concatenate(values, axis=0),
            preferred_element_type=jnp.float32,
        )
        o_ref[pl.ds(row, BLOCK), :] = (weighted / totals).astype(o_ref.dtype)

    def body(i, carry):
        for lane in range(PAIR):
            one_block(i * PAIR + lane)
        return carry

    lax.fori_loop(0, per_dev // PAIR, body, 0)
    for i in range(per_dev - per_dev % PAIR, per_dev):
        one_block(i)


def sparse_attention(tbl, queries, keys, values, far_keys, far_values, head_lo, heads):
    rows = queries.shape[0]

    def column(h, t):
        return (0, h + head_lo)

    operands = [keys, values] + list(far_keys) + list(far_values)
    total_rows = keys.shape[0] + sum(k.shape[0] for k in far_keys)
    sel = tbl.shape[0] * BLOCK // rows
    cost = pl.CostEstimate(
        flops=4 * rows * sel * BLOCK * HD * heads,
        transcendentals=rows * sel * BLOCK * heads,
        bytes_accessed=2 * HD * heads * (2 * rows + 2 * total_rows),
    )
    return pl.pallas_call(
        sparse_kernel,
        out_shape=jax.ShapeDtypeStruct((rows, heads * HD), jnp.bfloat16),
        cost_estimate=cost,
        grid_spec=pltpu.PrefetchScalarGridSpec(
            num_scalar_prefetch=1,
            grid=(heads,),
            in_specs=[pl.BlockSpec((rows, HD), lambda h, t: (0, h))]
            + [pl.BlockSpec((x.shape[0], HD), column) for x in operands],
            out_specs=pl.BlockSpec((rows, HD), lambda h, t: (0, h)),
            scratch_shapes=[
                pltpu.VMEM((total_rows, HD), jnp.bfloat16),
                pltpu.VMEM((total_rows, HD), jnp.bfloat16),
            ],
        ),
    )(tbl, queries, *operands)


def draft_kernel(q_ref, k_ref, v_ref, o_ref):
    tile = o_ref.shape[0]
    token = lax.broadcasted_iota(jnp.int32, (tile, tile * POOL), 1)
    draft = lax.broadcasted_iota(jnp.int32, (tile, tile * POOL), 0)
    pooling = jnp.where(token // POOL == draft, POOL ** (-0.5), 0.0).astype(jnp.bfloat16)
    pooled = jnp.dot(pooling, q_ref[...], preferred_element_type=jnp.float32).astype(jnp.bfloat16)
    raw = lax.dot_general(
        pooled, k_ref[...], (((1,), (1,)), ((), ())), preferred_element_type=jnp.float32
    )
    running = jnp.max(raw, axis=1, keepdims=True)
    weights = jnp.exp2((raw - running) * EXP2_SCALE)
    totals = jnp.sum(weights, axis=1, keepdims=True)
    weighted = jnp.dot(weights.astype(jnp.bfloat16), v_ref[...], preferred_element_type=jnp.float32)
    o_ref[...] = (weighted / totals).astype(o_ref.dtype)


def draft_attention(queries, keys, values, head_lo):
    token_rows, width = queries.shape
    rows = token_rows // POOL
    heads = width // HD
    key_rows = keys.shape[0]
    tile = min(DRAFT_ROWS, rows)
    cost = pl.CostEstimate(
        flops=4 * rows * key_rows * HD * heads + 2 * rows * tile * POOL * HD * heads,
        transcendentals=rows * key_rows * heads,
        bytes_accessed=2 * HD * heads * (token_rows + rows + 2 * key_rows),
    )
    return pl.pallas_call(
        draft_kernel,
        out_shape=jax.ShapeDtypeStruct((rows, width), jnp.bfloat16),
        cost_estimate=cost,
        grid=(heads, rows // tile),
        in_specs=[
            pl.BlockSpec((tile * POOL, HD), lambda h, r: (r, h)),
            pl.BlockSpec((key_rows, HD), lambda h, r: (0, h + head_lo)),
            pl.BlockSpec((key_rows, HD), lambda h, r: (0, h + head_lo)),
        ],
        out_specs=pl.BlockSpec((tile, HD), lambda h, r: (r, h)),
    )(queries, keys, values)


def head_permutes(matrix):
    count = lax.axis_size("head")
    me = lax.axis_index("head")
    rows, total = matrix.shape
    chunks = matrix.reshape(rows, count, total // count)
    by_shift = [lax.dynamic_index_in_dim(chunks, me, axis=1, keepdims=False)]
    for shift in range(1, count):
        piece = lax.dynamic_index_in_dim(chunks, (me + shift) % count, axis=1, keepdims=False)
        by_shift.append(
            lax.ppermute(piece, "head", [(i, (i + shift) % count) for i in range(count)])
        )
    stacked = jnp.stack(by_shift, axis=0)
    order = (me - jnp.arange(count, dtype=jnp.int32)) % count
    return jnp.take(stacked, order, axis=0).reshape(count * rows, total // count)


def on_device(query_in, key_in, value_in, block_lists):
    key_rows = lax.all_to_all(key_in, "head", split_axis=1, concat_axis=0, tiled=True)
    value_rows = head_permutes(value_in)
    seq_rows, width = key_rows.shape
    head_count = lax.axis_size("head")
    heads = width // HD
    first = max(1, heads // 2)
    spans = [(lo, n) for lo, n in ((0, first), (first, heads - first)) if n > 0]
    grouped_q = query_in.reshape(query_in.shape[0], head_count, width)
    query_slices = [
        grouped_q[:, :, lo * HD:(lo + n) * HD].reshape(query_in.shape[0], -1) for lo, n in spans
    ]

    def query_a2a(piece):
        return lax.all_to_all(piece, "head", split_axis=1, concat_axis=0, tiled=True)


    seq_count = lax.axis_size("seq")
    seq_index = lax.axis_index("seq")
    per_dev = seq_rows // BLOCK
    block_total, select_count = block_lists.shape
    block_ids = jnp.arange(block_total, dtype=jnp.int32)
    touched = jnp.any(block_lists[:, :, None] == block_ids[None, None, :], axis=1)
    needed = jnp.any(touched.reshape(seq_count, per_dev, seq_count, per_dev), axis=1)
    slot_rank = jnp.cumsum(needed.astype(jnp.int32), axis=2) - 1
    send_need = lax.dynamic_index_in_dim(needed, seq_index, axis=1, keepdims=False)
    send_rank = lax.dynamic_index_in_dim(slot_rank, seq_index, axis=1, keepdims=False)
    slot_hit = send_need[:, None, :] & (
        send_rank[:, None, :] == jnp.arange(CAP, dtype=jnp.int32)[None, :, None]
    )
    send_idx = jnp.sum(
        jnp.where(slot_hit, jnp.arange(per_dev, dtype=jnp.int32)[None, None, :], 0), axis=2
    ).reshape(-1)
    def exchange(rows):
        blocks = jnp.take(rows.reshape(per_dev, BLOCK, width), send_idx, axis=0)
        outgoing = blocks.reshape(seq_count, CAP, BLOCK, width)
        arrivals = []
        for shift in range(1, seq_count):
            parcel = lax.dynamic_index_in_dim(
                outgoing, (seq_index + shift) % seq_count, axis=0, keepdims=False
            )
            arrivals.append(
                lax.ppermute(
                    parcel, "seq", [(i, (i + shift) % seq_count) for i in range(seq_count)]
                )
            )
        return [a.reshape(CAP * BLOCK, width) for a in arrivals]

    own_lists = lax.dynamic_slice_in_dim(block_lists, seq_index * per_dev, per_dev, 0)
    owners = own_lists // per_dev
    within = own_lists % per_dev
    own_rank = lax.dynamic_index_in_dim(slot_rank, seq_index, axis=0, keepdims=False)
    ranks_used = jnp.clip(own_rank[owners, within], 0, CAP - 1)
    distance = (seq_index - owners) % seq_count
    joint_pos = jnp.where(distance == 0, within, per_dev + (distance - 1) * CAP + ranks_used)
    table = jnp.clip(joint_pos, 0, per_dev + (seq_count - 1) * CAP - 1).reshape(-1).astype(jnp.int32)

    remote_keys = exchange(key_rows)
    remote_values = exchange(value_rows)
    leading, remote_values, value_rows, table, pooled_keys, pooled_values = (
        lax.optimization_barrier(
            (
                query_slices[0], remote_values, value_rows, table,
                pool_tokens(key_rows), pool_tokens(value_rows),
            )
        )
    )
    draft_keys = lax.all_gather(pooled_keys, "seq", axis=0, tiled=True)
    draft_values = lax.all_gather(pooled_values, "seq", axis=0, tiled=True)
    query_parts = [query_a2a(leading)]
    later, remote_keys = lax.optimization_barrier((query_slices[1:], remote_keys))
    query_parts += [query_a2a(piece) for piece in later]

    pieces = []
    for index, ((head_lo, count), queries) in enumerate(zip(spans, query_parts)):
        rows_part = sparse_attention(
            table, queries, key_rows, value_rows, remote_keys, remote_values, head_lo, count,
        )
        if index == len(spans) - 1:
            rows_part, draft_keys, draft_values = lax.optimization_barrier(
                (rows_part, draft_keys, draft_values)
            )
        back = lax.all_to_all(rows_part, "head", split_axis=0, concat_axis=1, tiled=True)
        pieces.append(back.reshape(back.shape[0], -1, count * HD))
    sparse_out = jnp.concatenate(pieces, axis=2).reshape(pieces[0].shape[0], -1)
    draft_out = jnp.concatenate(
        [
            draft_attention(queries, draft_keys, draft_values, head_lo)
            for (head_lo, count), queries in zip(spans, query_parts)
        ],
        axis=1,
    )
    return (draft_out, sparse_out)


def solution(mesh):
    return jax.shard_map(
        on_device,
        mesh=mesh,
        in_specs=(
            P(("groups", "seq", "head"), None),
            P(("groups", "seq", "head"), None),
            P(("groups", "seq", "head"), None),
            P("groups", None),
        ),
        out_specs=(P(("groups", "seq"), "head"), P(("groups", "seq", "head"), None)),
        check_vma=False,
    )
```

```python
import functools

import jax
import jax.numpy as jnp
from jax import lax
from jax.experimental import pallas as pl
from jax.experimental.pallas import tpu as pltpu
from jax.sharding import PartitionSpec as P

HD = 128
BLOCK = 128
POOL = 4
CAP = 2
SCALE = HD ** (-0.5)
DRAFT_ROWS = 128
PAIR = 4
EXP2_SCALE = SCALE * 1.4426950408889634


def pool_tokens(matrix):
    grouped = matrix.astype(jnp.float32).reshape(matrix.shape[0] // POOL, POOL, matrix.shape[1])
    return (grouped.sum(axis=1) * POOL ** (-0.5)).astype(jnp.bfloat16)


def sparse_kernel(tbl_ref, q_ref, *refs):
    near_k, near_v = refs[0], refs[1]
    far_count = (len(refs) - 5) // 2
    far_k = refs[2:2 + far_count]
    far_v = refs[2 + far_count:2 + 2 * far_count]
    o_ref, kall_ref, vall_ref = refs[2 + 2 * far_count:]
    per_dev = q_ref.shape[0] // BLOCK
    sel = tbl_ref.shape[0] // per_dev
    near_rows = near_k.shape[0]
    kall_ref[0:near_rows, :] = near_k[...]
    vall_ref[0:near_rows, :] = near_v[...]
    offset = near_rows
    for kr, vr in zip(far_k, far_v):
        kall_ref[offset:offset + kr.shape[0], :] = kr[...]
        vall_ref[offset:offset + vr.shape[0], :] = vr[...]
        offset += kr.shape[0]
    last = offset // BLOCK - 1

    def one_block(i):
        row = pl.multiple_of(i * BLOCK, BLOCK)
        keys = []
        values = []
        for j in range(sel):
            start = pl.multiple_of(jnp.clip(tbl_ref[i * sel + j], 0, last) * BLOCK, BLOCK)
            keys.append(kall_ref[pl.ds(start, BLOCK), :])
            values.append(vall_ref[pl.ds(start, BLOCK), :])
        raw = lax.dot_general(
            q_ref[pl.ds(row, BLOCK), :], jnp.concatenate(keys, axis=0),
            (((1,), (1,)), ((), ())), preferred_element_type=jnp.float32,
        )
        running = jnp.max(raw, axis=1, keepdims=True)
        weights = jnp.exp2((raw - running) * EXP2_SCALE)
        totals = jnp.sum(weights, axis=1, keepdims=True)
        weighted = jnp.dot(
            weights.astype(jnp.bfloat16), jnp.concatenate(values, axis=0),
            preferred_element_type=jnp.float32,
        )
        o_ref[pl.ds(row, BLOCK), :] = (weighted / totals).astype(o_ref.dtype)

    def body(i, carry):
        for lane in range(PAIR):
            one_block(i * PAIR + lane)
        return carry

    lax.fori_loop(0, per_dev // PAIR, body, 0)
    for i in range(per_dev - per_dev % PAIR, per_dev):
        one_block(i)


def sparse_attention(tbl, queries, keys, values, far_keys, far_values, head_lo, heads):
    rows = queries.shape[0]

    def column(h, t):
        return (0, h + head_lo)

    operands = [keys, values] + list(far_keys) + list(far_values)
    total_rows = keys.shape[0] + sum(k.shape[0] for k in far_keys)
    sel = tbl.shape[0] * BLOCK // rows
    cost = pl.CostEstimate(
        flops=4 * rows * sel * BLOCK * HD * heads,
        transcendentals=rows * sel * BLOCK * heads,
        bytes_accessed=2 * HD * heads * (2 * rows + 2 * total_rows),
    )
    return pl.pallas_call(
        sparse_kernel,
        out_shape=jax.ShapeDtypeStruct((rows, heads * HD), jnp.bfloat16),
        cost_estimate=cost,
        grid_spec=pltpu.PrefetchScalarGridSpec(
            num_scalar_prefetch=1,
            grid=(heads,),
            in_specs=[pl.BlockSpec((rows, HD), lambda h, t: (0, h))]
            + [pl.BlockSpec((x.shape[0], HD), column) for x in operands],
            out_specs=pl.BlockSpec((rows, HD), lambda h, t: (0, h)),
            scratch_shapes=[
                pltpu.VMEM((total_rows, HD), jnp.bfloat16),
                pltpu.VMEM((total_rows, HD), jnp.bfloat16),
            ],
        ),
    )(tbl, queries, *operands)


def pooling_matrix(tile):
    token = lax.broadcasted_iota(jnp.int32, (tile, tile * POOL), 1)
    draft = lax.broadcasted_iota(jnp.int32, (tile, tile * POOL), 0)
    return jnp.where(token // POOL == draft, POOL ** (-0.5), 0.0).astype(jnp.bfloat16)


def draft_kernel(split, qa_ref, qb_ref, k_ref, v_ref, o_ref):
    pooling = pooling_matrix(o_ref.shape[0])
    chosen = jnp.where(pl.program_id(0) < split, qa_ref[...], qb_ref[...])
    pooled = jnp.dot(pooling, chosen, preferred_element_type=jnp.float32).astype(jnp.bfloat16)
    raw = lax.dot_general(
        pooled, k_ref[...], (((1,), (1,)), ((), ())), preferred_element_type=jnp.float32
    )
    running = jnp.max(raw, axis=1, keepdims=True)
    weights = jnp.exp2((raw - running) * EXP2_SCALE)
    totals = jnp.sum(weights, axis=1, keepdims=True)
    weighted = jnp.dot(weights.astype(jnp.bfloat16), v_ref[...], preferred_element_type=jnp.float32)
    o_ref[...] = (weighted / totals).astype(o_ref.dtype)


def draft_attention(leading, trailing, keys, values):
    token_rows = leading.shape[0]
    split = leading.shape[1] // HD
    later = trailing.shape[1] // HD
    rows = token_rows // POOL
    width = keys.shape[1]
    heads = width // HD
    key_rows = keys.shape[0]
    tile = min(DRAFT_ROWS, rows)
    cost = pl.CostEstimate(
        flops=4 * rows * key_rows * HD * heads + 2 * rows * tile * POOL * HD * heads,
        transcendentals=rows * key_rows * heads,
        bytes_accessed=2 * HD * heads * (2 * token_rows + rows + 2 * key_rows),
    )
    return pl.pallas_call(
        functools.partial(draft_kernel, split),
        out_shape=jax.ShapeDtypeStruct((rows, width), jnp.bfloat16),
        cost_estimate=cost,
        grid=(heads, rows // tile),
        in_specs=[
            pl.BlockSpec((tile * POOL, HD), lambda h, r: (r, jnp.minimum(h, split - 1))),
            pl.BlockSpec(
                (tile * POOL, HD), lambda h, r: (r, jnp.clip(h - split, 0, later - 1))
            ),
            pl.BlockSpec((key_rows, HD), lambda h, r: (0, h)),
            pl.BlockSpec((key_rows, HD), lambda h, r: (0, h)),
        ],
        out_specs=pl.BlockSpec((tile, HD), lambda h, r: (r, h)),
    )(leading, trailing, keys, values)


def head_permutes(matrix):
    count = lax.axis_size("head")
    me = lax.axis_index("head")
    rows, total = matrix.shape
    chunks = matrix.reshape(rows, count, total // count)
    by_shift = [lax.dynamic_index_in_dim(chunks, me, axis=1, keepdims=False)]
    for shift in range(1, count):
        piece = lax.dynamic_index_in_dim(chunks, (me + shift) % count, axis=1, keepdims=False)
        by_shift.append(
            lax.ppermute(piece, "head", [(i, (i + shift) % count) for i in range(count)])
        )
    stacked = jnp.stack(by_shift, axis=0)
    order = (me - jnp.arange(count, dtype=jnp.int32)) % count
    return jnp.take(stacked, order, axis=0).reshape(count * rows, total // count)


def on_device(query_in, key_in, value_in, block_lists):
    key_rows = lax.all_to_all(key_in, "head", split_axis=1, concat_axis=0, tiled=True)
    value_rows = head_permutes(value_in)
    seq_rows, width = key_rows.shape
    head_count = lax.axis_size("head")
    heads = width // HD
    first = max(1, heads // 2)
    spans = [(lo, n) for lo, n in ((0, first), (first, heads - first)) if n > 0]
    grouped_q = query_in.reshape(query_in.shape[0], head_count, width)
    query_slices = [
        grouped_q[:, :, lo * HD:(lo + n) * HD].reshape(query_in.shape[0], -1) for lo, n in spans
    ]

    def query_a2a(piece):
        return lax.all_to_all(piece, "head", split_axis=1, concat_axis=0, tiled=True)

    draft_keys = lax.all_gather(pool_tokens(key_rows), "seq", axis=0, tiled=True)
    draft_values = lax.all_gather(pool_tokens(value_rows), "seq", axis=0, tiled=True)

    seq_count = lax.axis_size("seq")
    seq_index = lax.axis_index("seq")
    per_dev = seq_rows // BLOCK
    block_total, select_count = block_lists.shape
    block_ids = jnp.arange(block_total, dtype=jnp.int32)
    touched = jnp.any(block_lists[:, :, None] == block_ids[None, None, :], axis=1)
    needed = jnp.any(touched.reshape(seq_count, per_dev, seq_count, per_dev), axis=1)
    slot_rank = jnp.cumsum(needed.astype(jnp.int32), axis=2) - 1
    send_need = lax.dynamic_index_in_dim(needed, seq_index, axis=1, keepdims=False)
    send_rank = lax.dynamic_index_in_dim(slot_rank, seq_index, axis=1, keepdims=False)
    slot_hit = send_need[:, None, :] & (
        send_rank[:, None, :] == jnp.arange(CAP, dtype=jnp.int32)[None, :, None]
    )
    send_idx = jnp.sum(
        jnp.where(slot_hit, jnp.arange(per_dev, dtype=jnp.int32)[None, None, :], 0), axis=2
    ).reshape(-1)
    def exchange(rows):
        blocks = jnp.take(rows.reshape(per_dev, BLOCK, width), send_idx, axis=0)
        outgoing = blocks.reshape(seq_count, CAP, BLOCK, width)
        arrivals = []
        for shift in range(1, seq_count):
            parcel = lax.dynamic_index_in_dim(
                outgoing, (seq_index + shift) % seq_count, axis=0, keepdims=False
            )
            arrivals.append(
                lax.ppermute(
                    parcel, "seq", [(i, (i + shift) % seq_count) for i in range(seq_count)]
                )
            )
        return [a.reshape(CAP * BLOCK, width) for a in arrivals]

    own_lists = lax.dynamic_slice_in_dim(block_lists, seq_index * per_dev, per_dev, 0)
    owners = own_lists // per_dev
    within = own_lists % per_dev
    own_rank = lax.dynamic_index_in_dim(slot_rank, seq_index, axis=0, keepdims=False)
    ranks_used = jnp.clip(own_rank[owners, within], 0, CAP - 1)
    distance = (seq_index - owners) % seq_count
    joint_pos = jnp.where(distance == 0, within, per_dev + (distance - 1) * CAP + ranks_used)
    table = jnp.clip(joint_pos, 0, per_dev + (seq_count - 1) * CAP - 1).reshape(-1).astype(jnp.int32)

    remote_keys = exchange(key_rows)
    remote_values = exchange(value_rows)
    leading, remote_values, value_rows, table = lax.optimization_barrier(
        (query_slices[0], remote_values, value_rows, table)
    )
    query_parts = [query_a2a(leading)]
    later, remote_keys = lax.optimization_barrier((query_slices[1:], remote_keys))
    query_parts += [query_a2a(piece) for piece in later]

    pieces = []
    for index, ((head_lo, count), queries) in enumerate(zip(spans, query_parts)):
        rows_part = sparse_attention(
            table, queries, key_rows, value_rows, remote_keys, remote_values, head_lo, count,
        )
        if index == len(spans) - 1:
            rows_part, draft_keys, draft_values = lax.optimization_barrier(
                (rows_part, draft_keys, draft_values)
            )
        back = lax.all_to_all(rows_part, "head", split_axis=0, concat_axis=1, tiled=True)
        pieces.append(back.reshape(back.shape[0], -1, count * HD))
    sparse_out = jnp.concatenate(pieces, axis=2).reshape(pieces[0].shape[0], -1)
    draft_out = draft_attention(query_parts[0], query_parts[-1], draft_keys, draft_values)
    return (draft_out, sparse_out)


def solution(mesh):
    return jax.shard_map(
        on_device,
        mesh=mesh,
        in_specs=(
            P(("groups", "seq", "head"), None),
            P(("groups", "seq", "head"), None),
            P(("groups", "seq", "head"), None),
            P("groups", None),
        ),
        out_specs=(P(("groups", "seq"), "head"), P(("groups", "seq", "head"), None)),
        check_vma=False,
    )
```

```python
import functools

import jax
import jax.numpy as jnp
from jax import lax
from jax.experimental import pallas as pl
from jax.experimental.pallas import tpu as pltpu
from jax.sharding import PartitionSpec as P

HD = 128
BLOCK = 128
POOL = 4
CAP = 2
SCALE = HD ** (-0.5)
DRAFT_ROWS = 128
PAIR = 8
EXP2_SCALE = SCALE * 1.4426950408889634


def pool_tokens(matrix):
    grouped = matrix.astype(jnp.float32).reshape(matrix.shape[0] // POOL, POOL, matrix.shape[1])
    return (grouped.sum(axis=1) * POOL ** (-0.5)).astype(jnp.bfloat16)


def sparse_kernel(tbl_ref, q_ref, *refs):
    near_k, near_v = refs[0], refs[1]
    far_count = (len(refs) - 5) // 2
    far_k = refs[2:2 + far_count]
    far_v = refs[2 + far_count:2 + 2 * far_count]
    o_ref, kall_ref, vall_ref = refs[2 + 2 * far_count:]
    per_dev = q_ref.shape[0] // BLOCK
    sel = tbl_ref.shape[0] // per_dev
    near_rows = near_k.shape[0]
    kall_ref[0:near_rows, :] = near_k[...]
    vall_ref[0:near_rows, :] = near_v[...]
    offset = near_rows
    for kr, vr in zip(far_k, far_v):
        kall_ref[offset:offset + kr.shape[0], :] = kr[...]
        vall_ref[offset:offset + vr.shape[0], :] = vr[...]
        offset += kr.shape[0]
    last = offset // BLOCK - 1

    def one_block(i):
        row = pl.multiple_of(i * BLOCK, BLOCK)
        keys = []
        values = []
        for j in range(sel):
            start = pl.multiple_of(jnp.clip(tbl_ref[i * sel + j], 0, last) * BLOCK, BLOCK)
            keys.append(kall_ref[pl.ds(start, BLOCK), :])
            values.append(vall_ref[pl.ds(start, BLOCK), :])
        raw = lax.dot_general(
            q_ref[pl.ds(row, BLOCK), :], jnp.concatenate(keys, axis=0),
            (((1,), (1,)), ((), ())), preferred_element_type=jnp.float32,
        )
        running = jnp.max(raw, axis=1, keepdims=True)
        weights = jnp.exp2((raw - running) * EXP2_SCALE)
        totals = jnp.sum(weights, axis=1, keepdims=True)
        weighted = jnp.dot(
            weights.astype(jnp.bfloat16), jnp.concatenate(values, axis=0),
            preferred_element_type=jnp.float32,
        )
        o_ref[pl.ds(row, BLOCK), :] = (weighted / totals).astype(o_ref.dtype)

    def body(i, carry):
        for lane in range(PAIR):
            one_block(i * PAIR + lane)
        return carry

    lax.fori_loop(0, per_dev // PAIR, body, 0)
    for i in range(per_dev - per_dev % PAIR, per_dev):
        one_block(i)


def sparse_attention(tbl, queries, keys, values, far_keys, far_values, head_lo, heads):
    rows = queries.shape[0]

    def column(h, t):
        return (0, h + head_lo)

    operands = [keys, values] + list(far_keys) + list(far_values)
    total_rows = keys.shape[0] + sum(k.shape[0] for k in far_keys)
    sel = tbl.shape[0] * BLOCK // rows
    cost = pl.CostEstimate(
        flops=4 * rows * sel * BLOCK * HD * heads,
        transcendentals=rows * sel * BLOCK * heads,
        bytes_accessed=2 * HD * heads * (2 * rows + 2 * total_rows),
    )
    return pl.pallas_call(
        sparse_kernel,
        out_shape=jax.ShapeDtypeStruct((rows, heads * HD), jnp.bfloat16),
        cost_estimate=cost,
        grid_spec=pltpu.PrefetchScalarGridSpec(
            num_scalar_prefetch=1,
            grid=(heads,),
            in_specs=[pl.BlockSpec((rows, HD), lambda h, t: (0, h))]
            + [pl.BlockSpec((x.shape[0], HD), column) for x in operands],
            out_specs=pl.BlockSpec((rows, HD), lambda h, t: (0, h)),
            scratch_shapes=[
                pltpu.VMEM((total_rows, HD), jnp.bfloat16),
                pltpu.VMEM((total_rows, HD), jnp.bfloat16),
            ],
        ),
    )(tbl, queries, *operands)


def pooling_matrix(tile):
    token = lax.broadcasted_iota(jnp.int32, (tile, tile * POOL), 1)
    draft = lax.broadcasted_iota(jnp.int32, (tile, tile * POOL), 0)
    return jnp.where(token // POOL == draft, POOL ** (-0.5), 0.0).astype(jnp.bfloat16)


def draft_kernel(split, qa_ref, qb_ref, k_ref, v_ref, o_ref):
    pooling = pooling_matrix(o_ref.shape[0])
    chosen = jnp.where(pl.program_id(0) < split, qa_ref[...], qb_ref[...])
    pooled = jnp.dot(pooling, chosen, preferred_element_type=jnp.float32).astype(jnp.bfloat16)
    raw = lax.dot_general(
        pooled, k_ref[...], (((1,), (1,)), ((), ())), preferred_element_type=jnp.float32
    )
    running = jnp.max(raw, axis=1, keepdims=True)
    weights = jnp.exp2((raw - running) * EXP2_SCALE)
    totals = jnp.sum(weights, axis=1, keepdims=True)
    weighted = jnp.dot(weights.astype(jnp.bfloat16), v_ref[...], preferred_element_type=jnp.float32)
    o_ref[...] = (weighted / totals).astype(o_ref.dtype)


def draft_attention(leading, trailing, keys, values):
    token_rows = leading.shape[0]
    split = leading.shape[1] // HD
    later = trailing.shape[1] // HD
    rows = token_rows // POOL
    width = keys.shape[1]
    heads = width // HD
    key_rows = keys.shape[0]
    tile = min(DRAFT_ROWS, rows)
    cost = pl.CostEstimate(
        flops=4 * rows * key_rows * HD * heads + 2 * rows * tile * POOL * HD * heads,
        transcendentals=rows * key_rows * heads,
        bytes_accessed=2 * HD * heads * (2 * token_rows + rows + 2 * key_rows),
    )
    return pl.pallas_call(
        functools.partial(draft_kernel, split),
        out_shape=jax.ShapeDtypeStruct((rows, width), jnp.bfloat16),
        cost_estimate=cost,
        grid=(heads, rows // tile),
        in_specs=[
            pl.BlockSpec((tile * POOL, HD), lambda h, r: (r, jnp.minimum(h, split - 1))),
            pl.BlockSpec(
                (tile * POOL, HD), lambda h, r: (r, jnp.clip(h - split, 0, later - 1))
            ),
            pl.BlockSpec((key_rows, HD), lambda h, r: (0, h)),
            pl.BlockSpec((key_rows, HD), lambda h, r: (0, h)),
        ],
        out_specs=pl.BlockSpec((tile, HD), lambda h, r: (r, h)),
    )(leading, trailing, keys, values)


def head_permutes(matrix):
    count = lax.axis_size("head")
    me = lax.axis_index("head")
    rows, total = matrix.shape
    chunks = matrix.reshape(rows, count, total // count)
    by_shift = [lax.dynamic_index_in_dim(chunks, me, axis=1, keepdims=False)]
    for shift in range(1, count):
        piece = lax.dynamic_index_in_dim(chunks, (me + shift) % count, axis=1, keepdims=False)
        by_shift.append(
            lax.ppermute(piece, "head", [(i, (i + shift) % count) for i in range(count)])
        )
    stacked = jnp.stack(by_shift, axis=0)
    order = (me - jnp.arange(count, dtype=jnp.int32)) % count
    return jnp.take(stacked, order, axis=0).reshape(count * rows, total // count)


def on_device(query_in, key_in, value_in, block_lists):
    key_rows = lax.all_to_all(key_in, "head", split_axis=1, concat_axis=0, tiled=True)
    value_rows = head_permutes(value_in)
    seq_rows, width = key_rows.shape
    head_count = lax.axis_size("head")
    heads = width // HD
    first = max(1, heads // 2)
    spans = [(lo, n) for lo, n in ((0, first), (first, heads - first)) if n > 0]
    grouped_q = query_in.reshape(query_in.shape[0], head_count, width)
    query_slices = [
        grouped_q[:, :, lo * HD:(lo + n) * HD].reshape(query_in.shape[0], -1) for lo, n in spans
    ]

    def query_a2a(piece):
        return lax.all_to_all(piece, "head", split_axis=1, concat_axis=0, tiled=True)

    draft_keys = lax.all_gather(pool_tokens(key_rows), "seq", axis=0, tiled=True)
    draft_values = lax.all_gather(pool_tokens(value_rows), "seq", axis=0, tiled=True)

    seq_count = lax.axis_size("seq")
    seq_index = lax.axis_index("seq")
    per_dev = seq_rows // BLOCK
    block_total, select_count = block_lists.shape
    block_ids = jnp.arange(block_total, dtype=jnp.int32)
    touched = jnp.any(block_lists[:, :, None] == block_ids[None, None, :], axis=1)
    needed = jnp.any(touched.reshape(seq_count, per_dev, seq_count, per_dev), axis=1)
    slot_rank = jnp.cumsum(needed.astype(jnp.int32), axis=2) - 1
    send_need = lax.dynamic_index_in_dim(needed, seq_index, axis=1, keepdims=False)
    send_rank = lax.dynamic_index_in_dim(slot_rank, seq_index, axis=1, keepdims=False)
    slot_hit = send_need[:, None, :] & (
        send_rank[:, None, :] == jnp.arange(CAP, dtype=jnp.int32)[None, :, None]
    )
    send_idx = jnp.sum(
        jnp.where(slot_hit, jnp.arange(per_dev, dtype=jnp.int32)[None, None, :], 0), axis=2
    ).reshape(-1)
    def exchange(rows):
        blocks = jnp.take(rows.reshape(per_dev, BLOCK, width), send_idx, axis=0)
        outgoing = blocks.reshape(seq_count, CAP, BLOCK, width)
        arrivals = []
        for shift in range(1, seq_count):
            parcel = lax.dynamic_index_in_dim(
                outgoing, (seq_index + shift) % seq_count, axis=0, keepdims=False
            )
            arrivals.append(
                lax.ppermute(
                    parcel, "seq", [(i, (i + shift) % seq_count) for i in range(seq_count)]
                )
            )
        return [a.reshape(CAP * BLOCK, width) for a in arrivals]

    own_lists = lax.dynamic_slice_in_dim(block_lists, seq_index * per_dev, per_dev, 0)
    owners = own_lists // per_dev
    within = own_lists % per_dev
    own_rank = lax.dynamic_index_in_dim(slot_rank, seq_index, axis=0, keepdims=False)
    ranks_used = jnp.clip(own_rank[owners, within], 0, CAP - 1)
    distance = (seq_index - owners) % seq_count
    joint_pos = jnp.where(distance == 0, within, per_dev + (distance - 1) * CAP + ranks_used)
    table = jnp.clip(joint_pos, 0, per_dev + (seq_count - 1) * CAP - 1).reshape(-1).astype(jnp.int32)

    remote_keys = exchange(key_rows)
    remote_values = exchange(value_rows)
    leading, remote_values, value_rows, table = lax.optimization_barrier(
        (query_slices[0], remote_values, value_rows, table)
    )
    query_parts = [query_a2a(leading)]
    later, remote_keys = lax.optimization_barrier((query_slices[1:], remote_keys))
    query_parts += [query_a2a(piece) for piece in later]

    pieces = []
    for index, ((head_lo, count), queries) in enumerate(zip(spans, query_parts)):
        rows_part = sparse_attention(
            table, queries, key_rows, value_rows, remote_keys, remote_values, head_lo, count,
        )
        if index == len(spans) - 1:
            rows_part, draft_keys, draft_values = lax.optimization_barrier(
                (rows_part, draft_keys, draft_values)
            )
        back = lax.all_to_all(rows_part, "head", split_axis=0, concat_axis=1, tiled=True)
        pieces.append(back.reshape(back.shape[0], -1, count * HD))
    sparse_out = jnp.concatenate(pieces, axis=2).reshape(pieces[0].shape[0], -1)
    draft_out = draft_attention(query_parts[0], query_parts[-1], draft_keys, draft_values)
    return (draft_out, sparse_out)


def solution(mesh):
    return jax.shard_map(
        on_device,
        mesh=mesh,
        in_specs=(
            P(("groups", "seq", "head"), None),
            P(("groups", "seq", "head"), None),
            P(("groups", "seq", "head"), None),
            P("groups", None),
        ),
        out_specs=(P(("groups", "seq"), "head"), P(("groups", "seq", "head"), None)),
        check_vma=False,
    )
```

```python
import functools

import jax
import jax.numpy as jnp
from jax import lax
from jax.experimental import pallas as pl
from jax.experimental.pallas import tpu as pltpu
from jax.sharding import PartitionSpec as P

HD = 128
BLOCK = 128
POOL = 4
CAP = 2
SCALE = HD ** (-0.5)
DRAFT_ROWS = 128
PAIR = 4
EXP2_SCALE = SCALE * 1.4426950408889634


def pool_tokens(matrix):
    grouped = matrix.astype(jnp.float32).reshape(matrix.shape[0] // POOL, POOL, matrix.shape[1])
    return (grouped.sum(axis=1) * POOL ** (-0.5)).astype(jnp.bfloat16)


def sparse_kernel(tbl_ref, q_ref, *refs):
    near_k, near_v = refs[0], refs[1]
    far_count = (len(refs) - 5) // 2
    far_k = refs[2:2 + far_count]
    far_v = refs[2 + far_count:2 + 2 * far_count]
    o_ref, kall_ref, vall_ref = refs[2 + 2 * far_count:]
    per_dev = q_ref.shape[0] // BLOCK
    sel = tbl_ref.shape[0] // per_dev
    near_rows = near_k.shape[0]
    kall_ref[0:near_rows, :] = near_k[...]
    vall_ref[0:near_rows, :] = near_v[...]
    offset = near_rows
    for kr, vr in zip(far_k, far_v):
        kall_ref[offset:offset + kr.shape[0], :] = kr[...]
        vall_ref[offset:offset + vr.shape[0], :] = vr[...]
        offset += kr.shape[0]
    last = offset // BLOCK - 1

    def one_block(i):
        row = pl.multiple_of(i * BLOCK, BLOCK)
        keys = []
        values = []
        for j in range(sel):
            start = pl.multiple_of(jnp.clip(tbl_ref[i * sel + j], 0, last) * BLOCK, BLOCK)
            keys.append(kall_ref[pl.ds(start, BLOCK), :])
            values.append(vall_ref[pl.ds(start, BLOCK), :])
        raw = lax.dot_general(
            q_ref[pl.ds(row, BLOCK), :], jnp.concatenate(keys, axis=0),
            (((1,), (1,)), ((), ())), preferred_element_type=jnp.float32,
        )
        running = jnp.max(raw, axis=1, keepdims=True)
        weights = jnp.exp2((raw - running) * EXP2_SCALE)
        totals = jnp.sum(weights, axis=1, keepdims=True)
        weighted = jnp.dot(
            weights.astype(jnp.bfloat16), jnp.concatenate(values, axis=0),
            preferred_element_type=jnp.float32,
        )
        o_ref[pl.ds(row, BLOCK), :] = (weighted / totals).astype(o_ref.dtype)

    def body(i, carry):
        for lane in range(PAIR):
            one_block(i * PAIR + lane)
        return carry

    lax.fori_loop(0, per_dev // PAIR, body, 0)
    for i in range(per_dev - per_dev % PAIR, per_dev):
        one_block(i)


def sparse_attention(tbl, queries, keys, values, far_keys, far_values, head_lo, heads):
    rows = queries.shape[0]

    def column(h, t):
        return (0, h + head_lo)

    operands = [keys, values] + list(far_keys) + list(far_values)
    total_rows = keys.shape[0] + sum(k.shape[0] for k in far_keys)
    sel = tbl.shape[0] * BLOCK // rows
    cost = pl.CostEstimate(
        flops=4 * rows * sel * BLOCK * HD * heads,
        transcendentals=rows * sel * BLOCK * heads,
        bytes_accessed=2 * HD * heads * (2 * rows + 2 * total_rows),
    )
    return pl.pallas_call(
        sparse_kernel,
        out_shape=jax.ShapeDtypeStruct((rows, heads * HD), jnp.bfloat16),
        cost_estimate=cost,
        grid_spec=pltpu.PrefetchScalarGridSpec(
            num_scalar_prefetch=1,
            grid=(heads,),
            in_specs=[pl.BlockSpec((rows, HD), lambda h, t: (0, h))]
            + [pl.BlockSpec((x.shape[0], HD), column) for x in operands],
            out_specs=pl.BlockSpec((rows, HD), lambda h, t: (0, h)),
            scratch_shapes=[
                pltpu.VMEM((total_rows, HD), jnp.bfloat16),
                pltpu.VMEM((total_rows, HD), jnp.bfloat16),
            ],
        ),
    )(tbl, queries, *operands)


def pooling_matrix(tile):
    token = lax.broadcasted_iota(jnp.int32, (tile, tile * POOL), 1)
    draft = lax.broadcasted_iota(jnp.int32, (tile, tile * POOL), 0)
    return jnp.where(token // POOL == draft, POOL ** (-0.5), 0.0).astype(jnp.bfloat16)


def draft_kernel(split, qa_ref, qb_ref, k_ref, v_ref, o_ref):
    pooling = pooling_matrix(o_ref.shape[0])
    chosen = jnp.where(pl.program_id(0) < split, qa_ref[...], qb_ref[...])
    pooled = jnp.dot(pooling, chosen, preferred_element_type=jnp.float32).astype(jnp.bfloat16)
    raw = lax.dot_general(
        pooled, k_ref[...], (((1,), (1,)), ((), ())), preferred_element_type=jnp.float32
    )
    running = jnp.max(raw, axis=1, keepdims=True)
    weights = jnp.exp2((raw - running) * EXP2_SCALE)
    totals = jnp.sum(weights, axis=1, keepdims=True)
    weighted = jnp.dot(weights.astype(jnp.bfloat16), v_ref[...], preferred_element_type=jnp.float32)
    o_ref[...] = (weighted / totals).astype(o_ref.dtype)


def draft_attention(leading, trailing, keys, values):
    token_rows = leading.shape[0]
    split = leading.shape[1] // HD
    later = trailing.shape[1] // HD
    rows = token_rows // POOL
    width = keys.shape[1]
    heads = width // HD
    key_rows = keys.shape[0]
    tile = min(DRAFT_ROWS, rows)
    cost = pl.CostEstimate(
        flops=4 * rows * key_rows * HD * heads + 2 * rows * tile * POOL * HD * heads,
        transcendentals=rows * key_rows * heads,
        bytes_accessed=2 * HD * heads * (2 * token_rows + rows + 2 * key_rows),
    )
    return pl.pallas_call(
        functools.partial(draft_kernel, split),
        out_shape=jax.ShapeDtypeStruct((rows, width), jnp.bfloat16),
        cost_estimate=cost,
        grid=(heads, rows // tile),
        in_specs=[
            pl.BlockSpec((tile * POOL, HD), lambda h, r: (r, jnp.minimum(h, split - 1))),
            pl.BlockSpec(
                (tile * POOL, HD), lambda h, r: (r, jnp.clip(h - split, 0, later - 1))
            ),
            pl.BlockSpec((key_rows, HD), lambda h, r: (0, h)),
            pl.BlockSpec((key_rows, HD), lambda h, r: (0, h)),
        ],
        out_specs=pl.BlockSpec((tile, HD), lambda h, r: (r, h)),
    )(leading, trailing, keys, values)


def head_permutes(matrix):
    count = lax.axis_size("head")
    me = lax.axis_index("head")
    rows, total = matrix.shape
    chunks = matrix.reshape(rows, count, total // count)
    by_shift = [lax.dynamic_index_in_dim(chunks, me, axis=1, keepdims=False)]
    for shift in range(1, count):
        piece = lax.dynamic_index_in_dim(chunks, (me + shift) % count, axis=1, keepdims=False)
        by_shift.append(
            lax.ppermute(piece, "head", [(i, (i + shift) % count) for i in range(count)])
        )
    stacked = jnp.stack(by_shift, axis=0)
    order = (me - jnp.arange(count, dtype=jnp.int32)) % count
    return jnp.take(stacked, order, axis=0).reshape(count * rows, total // count)


def on_device(query_in, key_in, value_in, block_lists):
    key_rows = head_permutes(key_in)
    value_rows = lax.all_to_all(value_in, "head", split_axis=1, concat_axis=0, tiled=True)
    seq_rows, width = key_rows.shape
    head_count = lax.axis_size("head")
    heads = width // HD
    first = max(1, heads // 2)
    spans = [(lo, n) for lo, n in ((0, first), (first, heads - first)) if n > 0]
    grouped_q = query_in.reshape(query_in.shape[0], head_count, width)
    query_slices = [
        grouped_q[:, :, lo * HD:(lo + n) * HD].reshape(query_in.shape[0], -1) for lo, n in spans
    ]

    def query_a2a(piece):
        return lax.all_to_all(piece, "head", split_axis=1, concat_axis=0, tiled=True)

    draft_keys = lax.all_gather(pool_tokens(key_rows), "seq", axis=0, tiled=True)
    draft_values = lax.all_gather(pool_tokens(value_rows), "seq", axis=0, tiled=True)

    seq_count = lax.axis_size("seq")
    seq_index = lax.axis_index("seq")
    per_dev = seq_rows // BLOCK
    block_total, select_count = block_lists.shape
    block_ids = jnp.arange(block_total, dtype=jnp.int32)
    touched = jnp.any(block_lists[:, :, None] == block_ids[None, None, :], axis=1)
    needed = jnp.any(touched.reshape(seq_count, per_dev, seq_count, per_dev), axis=1)
    slot_rank = jnp.cumsum(needed.astype(jnp.int32), axis=2) - 1
    send_need = lax.dynamic_index_in_dim(needed, seq_index, axis=1, keepdims=False)
    send_rank = lax.dynamic_index_in_dim(slot_rank, seq_index, axis=1, keepdims=False)
    slot_hit = send_need[:, None, :] & (
        send_rank[:, None, :] == jnp.arange(CAP, dtype=jnp.int32)[None, :, None]
    )
    send_idx = jnp.sum(
        jnp.where(slot_hit, jnp.arange(per_dev, dtype=jnp.int32)[None, None, :], 0), axis=2
    ).reshape(-1)
    def exchange(rows):
        blocks = jnp.take(rows.reshape(per_dev, BLOCK, width), send_idx, axis=0)
        outgoing = blocks.reshape(seq_count, CAP, BLOCK, width)
        arrivals = []
        for shift in range(1, seq_count):
            parcel = lax.dynamic_index_in_dim(
                outgoing, (seq_index + shift) % seq_count, axis=0, keepdims=False
            )
            arrivals.append(
                lax.ppermute(
                    parcel, "seq", [(i, (i + shift) % seq_count) for i in range(seq_count)]
                )
            )
        return [a.reshape(CAP * BLOCK, width) for a in arrivals]

    own_lists = lax.dynamic_slice_in_dim(block_lists, seq_index * per_dev, per_dev, 0)
    owners = own_lists // per_dev
    within = own_lists % per_dev
    own_rank = lax.dynamic_index_in_dim(slot_rank, seq_index, axis=0, keepdims=False)
    ranks_used = jnp.clip(own_rank[owners, within], 0, CAP - 1)
    distance = (seq_index - owners) % seq_count
    joint_pos = jnp.where(distance == 0, within, per_dev + (distance - 1) * CAP + ranks_used)
    table = jnp.clip(joint_pos, 0, per_dev + (seq_count - 1) * CAP - 1).reshape(-1).astype(jnp.int32)

    remote_keys = exchange(key_rows)
    remote_values = exchange(value_rows)
    leading, remote_keys, key_rows, table = lax.optimization_barrier(
        (query_slices[0], remote_keys, key_rows, table)
    )
    query_parts = [query_a2a(leading)]
    later, remote_values = lax.optimization_barrier((query_slices[1:], remote_values))
    query_parts += [query_a2a(piece) for piece in later]

    pieces = []
    for index, ((head_lo, count), queries) in enumerate(zip(spans, query_parts)):
        rows_part = sparse_attention(
            table, queries, key_rows, value_rows, remote_keys, remote_values, head_lo, count,
        )
        if index == len(spans) - 1:
            rows_part, draft_keys, draft_values = lax.optimization_barrier(
                (rows_part, draft_keys, draft_values)
            )
        back = lax.all_to_all(rows_part, "head", split_axis=0, concat_axis=1, tiled=True)
        pieces.append(back.reshape(back.shape[0], -1, count * HD))
    sparse_out = jnp.concatenate(pieces, axis=2).reshape(pieces[0].shape[0], -1)
    draft_out = draft_attention(query_parts[0], query_parts[-1], draft_keys, draft_values)
    return (draft_out, sparse_out)


def solution(mesh):
    return jax.shard_map(
        on_device,
        mesh=mesh,
        in_specs=(
            P(("groups", "seq", "head"), None),
            P(("groups", "seq", "head"), None),
            P(("groups", "seq", "head"), None),
            P("groups", None),
        ),
        out_specs=(P(("groups", "seq"), "head"), P(("groups", "seq", "head"), None)),
        check_vma=False,
    )
```

```python
import functools

import jax
import jax.numpy as jnp
from jax import lax
from jax.experimental import pallas as pl
from jax.experimental.pallas import tpu as pltpu
from jax.sharding import PartitionSpec as P

HD = 128
BLOCK = 128
POOL = 4
CAP = 2
SCALE = HD ** (-0.5)
DRAFT_ROWS = 128
PAIR = 4
SPLITS = 3
EXP2_SCALE = SCALE * 1.4426950408889634


def pool_tokens(matrix):
    grouped = matrix.astype(jnp.float32).reshape(matrix.shape[0] // POOL, POOL, matrix.shape[1])
    return (grouped.sum(axis=1) * POOL ** (-0.5)).astype(jnp.bfloat16)


def sparse_kernel(tbl_ref, q_ref, *refs):
    near_k, near_v = refs[0], refs[1]
    far_count = (len(refs) - 5) // 2
    far_k = refs[2:2 + far_count]
    far_v = refs[2 + far_count:2 + 2 * far_count]
    o_ref, kall_ref, vall_ref = refs[2 + 2 * far_count:]
    per_dev = q_ref.shape[0] // BLOCK
    sel = tbl_ref.shape[0] // per_dev
    near_rows = near_k.shape[0]
    kall_ref[0:near_rows, :] = near_k[...]
    vall_ref[0:near_rows, :] = near_v[...]
    offset = near_rows
    for kr, vr in zip(far_k, far_v):
        kall_ref[offset:offset + kr.shape[0], :] = kr[...]
        vall_ref[offset:offset + vr.shape[0], :] = vr[...]
        offset += kr.shape[0]
    last = offset // BLOCK - 1

    def one_block(i):
        row = pl.multiple_of(i * BLOCK, BLOCK)
        keys = []
        values = []
        for j in range(sel):
            start = pl.multiple_of(jnp.clip(tbl_ref[i * sel + j], 0, last) * BLOCK, BLOCK)
            keys.append(kall_ref[pl.ds(start, BLOCK), :])
            values.append(vall_ref[pl.ds(start, BLOCK), :])
        raw = lax.dot_general(
            q_ref[pl.ds(row, BLOCK), :], jnp.concatenate(keys, axis=0),
            (((1,), (1,)), ((), ())), preferred_element_type=jnp.float32,
        )
        running = jnp.max(raw, axis=1, keepdims=True)
        weights = jnp.exp2((raw - running) * EXP2_SCALE)
        totals = jnp.sum(weights, axis=1, keepdims=True)
        weighted = jnp.dot(
            weights.astype(jnp.bfloat16), jnp.concatenate(values, axis=0),
            preferred_element_type=jnp.float32,
        )
        o_ref[pl.ds(row, BLOCK), :] = (weighted / totals).astype(o_ref.dtype)

    def body(i, carry):
        for lane in range(PAIR):
            one_block(i * PAIR + lane)
        return carry

    lax.fori_loop(0, per_dev // PAIR, body, 0)
    for i in range(per_dev - per_dev % PAIR, per_dev):
        one_block(i)


def sparse_attention(tbl, queries, keys, values, far_keys, far_values, head_lo, heads):
    rows = queries.shape[0]

    def column(h, t):
        return (0, h + head_lo)

    operands = [keys, values] + list(far_keys) + list(far_values)
    total_rows = keys.shape[0] + sum(k.shape[0] for k in far_keys)
    sel = tbl.shape[0] * BLOCK // rows
    cost = pl.CostEstimate(
        flops=4 * rows * sel * BLOCK * HD * heads,
        transcendentals=rows * sel * BLOCK * heads,
        bytes_accessed=2 * HD * heads * (2 * rows + 2 * total_rows),
    )
    return pl.pallas_call(
        sparse_kernel,
        out_shape=jax.ShapeDtypeStruct((rows, heads * HD), jnp.bfloat16),
        cost_estimate=cost,
        grid_spec=pltpu.PrefetchScalarGridSpec(
            num_scalar_prefetch=1,
            grid=(heads,),
            in_specs=[pl.BlockSpec((rows, HD), lambda h, t: (0, h))]
            + [pl.BlockSpec((x.shape[0], HD), column) for x in operands],
            out_specs=pl.BlockSpec((rows, HD), lambda h, t: (0, h)),
            scratch_shapes=[
                pltpu.VMEM((total_rows, HD), jnp.bfloat16),
                pltpu.VMEM((total_rows, HD), jnp.bfloat16),
            ],
        ),
    )(tbl, queries, *operands)


def pooling_matrix(tile):
    token = lax.broadcasted_iota(jnp.int32, (tile, tile * POOL), 1)
    draft = lax.broadcasted_iota(jnp.int32, (tile, tile * POOL), 0)
    return jnp.where(token // POOL == draft, POOL ** (-0.5), 0.0).astype(jnp.bfloat16)


def draft_kernel(bounds, *refs):
    q_refs = refs[:len(bounds)]
    k_ref, v_ref, o_ref = refs[len(bounds):]
    head = pl.program_id(0)
    chosen = q_refs[-1][...]
    for bound, q_ref in zip(bounds[-2::-1], q_refs[-2::-1]):
        chosen = jnp.where(head < bound, q_ref[...], chosen)
    pooling = pooling_matrix(o_ref.shape[0])
    pooled = jnp.dot(pooling, chosen, preferred_element_type=jnp.float32).astype(jnp.bfloat16)
    raw = lax.dot_general(
        pooled, k_ref[...], (((1,), (1,)), ((), ())), preferred_element_type=jnp.float32
    )
    running = jnp.max(raw, axis=1, keepdims=True)
    weights = jnp.exp2((raw - running) * EXP2_SCALE)
    totals = jnp.sum(weights, axis=1, keepdims=True)
    weighted = jnp.dot(weights.astype(jnp.bfloat16), v_ref[...], preferred_element_type=jnp.float32)
    o_ref[...] = (weighted / totals).astype(o_ref.dtype)


def draft_attention(parts, keys, values):
    token_rows = parts[0].shape[0]
    rows = token_rows // POOL
    width = keys.shape[1]
    heads = width // HD
    key_rows = keys.shape[0]
    tile = min(DRAFT_ROWS, rows)
    bounds = []
    q_specs = []
    lo = 0
    for part in parts:
        n = part.shape[1] // HD
        q_specs.append(
            pl.BlockSpec(
                (tile * POOL, HD),
                functools.partial(lambda base, size, h, r: (r, jnp.clip(h - base, 0, size - 1)), lo, n),
            )
        )
        lo += n
        bounds.append(lo)
    cost = pl.CostEstimate(
        flops=4 * rows * key_rows * HD * heads + 2 * rows * tile * POOL * HD * heads,
        transcendentals=rows * key_rows * heads,
        bytes_accessed=2 * HD * heads * (2 * token_rows + rows + 2 * key_rows),
    )
    return pl.pallas_call(
        functools.partial(draft_kernel, tuple(bounds)),
        out_shape=jax.ShapeDtypeStruct((rows, width), jnp.bfloat16),
        cost_estimate=cost,
        grid=(heads, rows // tile),
        in_specs=q_specs + [
            pl.BlockSpec((key_rows, HD), lambda h, r: (0, h)),
            pl.BlockSpec((key_rows, HD), lambda h, r: (0, h)),
        ],
        out_specs=pl.BlockSpec((tile, HD), lambda h, r: (r, h)),
    )(*parts, keys, values)


def head_permutes(matrix):
    count = lax.axis_size("head")
    me = lax.axis_index("head")
    rows, total = matrix.shape
    chunks = matrix.reshape(rows, count, total // count)
    by_shift = [lax.dynamic_index_in_dim(chunks, me, axis=1, keepdims=False)]
    for shift in range(1, count):
        piece = lax.dynamic_index_in_dim(chunks, (me + shift) % count, axis=1, keepdims=False)
        by_shift.append(
            lax.ppermute(piece, "head", [(i, (i + shift) % count) for i in range(count)])
        )
    stacked = jnp.stack(by_shift, axis=0)
    order = (me - jnp.arange(count, dtype=jnp.int32)) % count
    return jnp.take(stacked, order, axis=0).reshape(count * rows, total // count)


def on_device(query_in, key_in, value_in, block_lists):
    key_rows = head_permutes(key_in)
    value_rows = lax.all_to_all(value_in, "head", split_axis=1, concat_axis=0, tiled=True)
    seq_rows, width = key_rows.shape
    head_count = lax.axis_size("head")
    heads = width // HD
    piece_count = min(SPLITS, heads)
    edges = [heads * k // piece_count for k in range(piece_count + 1)]
    spans = [(edges[k], edges[k + 1] - edges[k]) for k in range(piece_count)]
    grouped_q = query_in.reshape(query_in.shape[0], head_count, width)
    query_slices = [
        grouped_q[:, :, lo * HD:(lo + n) * HD].reshape(query_in.shape[0], -1) for lo, n in spans
    ]

    def query_a2a(piece):
        return lax.all_to_all(piece, "head", split_axis=1, concat_axis=0, tiled=True)

    draft_keys = lax.all_gather(pool_tokens(key_rows), "seq", axis=0, tiled=True)
    draft_values = lax.all_gather(pool_tokens(value_rows), "seq", axis=0, tiled=True)

    seq_count = lax.axis_size("seq")
    seq_index = lax.axis_index("seq")
    per_dev = seq_rows // BLOCK
    block_total, select_count = block_lists.shape
    block_ids = jnp.arange(block_total, dtype=jnp.int32)
    touched = jnp.any(block_lists[:, :, None] == block_ids[None, None, :], axis=1)
    needed = jnp.any(touched.reshape(seq_count, per_dev, seq_count, per_dev), axis=1)
    slot_rank = jnp.cumsum(needed.astype(jnp.int32), axis=2) - 1
    send_need = lax.dynamic_index_in_dim(needed, seq_index, axis=1, keepdims=False)
    send_rank = lax.dynamic_index_in_dim(slot_rank, seq_index, axis=1, keepdims=False)
    slot_hit = send_need[:, None, :] & (
        send_rank[:, None, :] == jnp.arange(CAP, dtype=jnp.int32)[None, :, None]
    )
    send_idx = jnp.sum(
        jnp.where(slot_hit, jnp.arange(per_dev, dtype=jnp.int32)[None, None, :], 0), axis=2
    ).reshape(-1)
    def exchange(rows):
        blocks = jnp.take(rows.reshape(per_dev, BLOCK, width), send_idx, axis=0)
        outgoing = blocks.reshape(seq_count, CAP, BLOCK, width)
        arrivals = []
        for shift in range(1, seq_count):
            parcel = lax.dynamic_index_in_dim(
                outgoing, (seq_index + shift) % seq_count, axis=0, keepdims=False
            )
            arrivals.append(
                lax.ppermute(
                    parcel, "seq", [(i, (i + shift) % seq_count) for i in range(seq_count)]
                )
            )
        return [a.reshape(CAP * BLOCK, width) for a in arrivals]

    own_lists = lax.dynamic_slice_in_dim(block_lists, seq_index * per_dev, per_dev, 0)
    owners = own_lists // per_dev
    within = own_lists % per_dev
    own_rank = lax.dynamic_index_in_dim(slot_rank, seq_index, axis=0, keepdims=False)
    ranks_used = jnp.clip(own_rank[owners, within], 0, CAP - 1)
    distance = (seq_index - owners) % seq_count
    joint_pos = jnp.where(distance == 0, within, per_dev + (distance - 1) * CAP + ranks_used)
    table = jnp.clip(joint_pos, 0, per_dev + (seq_count - 1) * CAP - 1).reshape(-1).astype(jnp.int32)

    remote_keys = exchange(key_rows)
    remote_values = exchange(value_rows)
    leading, remote_keys, key_rows, table = lax.optimization_barrier(
        (query_slices[0], remote_keys, key_rows, table)
    )
    query_parts = [query_a2a(leading)]
    later, remote_values = lax.optimization_barrier((query_slices[1:], remote_values))
    query_parts += [query_a2a(piece) for piece in later]

    pieces = []
    for index, ((head_lo, count), queries) in enumerate(zip(spans, query_parts)):
        rows_part = sparse_attention(
            table, queries, key_rows, value_rows, remote_keys, remote_values, head_lo, count,
        )
        if index == len(spans) - 1:
            rows_part, draft_keys, draft_values = lax.optimization_barrier(
                (rows_part, draft_keys, draft_values)
            )
        back = lax.all_to_all(rows_part, "head", split_axis=0, concat_axis=1, tiled=True)
        pieces.append(back.reshape(back.shape[0], -1, count * HD))
    sparse_out = jnp.concatenate(pieces, axis=2).reshape(pieces[0].shape[0], -1)
    draft_out = draft_attention(query_parts, draft_keys, draft_values)
    return (draft_out, sparse_out)


def solution(mesh):
    return jax.shard_map(
        on_device,
        mesh=mesh,
        in_specs=(
            P(("groups", "seq", "head"), None),
            P(("groups", "seq", "head"), None),
            P(("groups", "seq", "head"), None),
            P("groups", None),
        ),
        out_specs=(P(("groups", "seq"), "head"), P(("groups", "seq", "head"), None)),
        check_vma=False,
    )
```

```python
import functools

import jax
import jax.numpy as jnp
from jax import lax
from jax.experimental import pallas as pl
from jax.experimental.pallas import tpu as pltpu
from jax.sharding import PartitionSpec as P

HD = 128
BLOCK = 128
POOL = 4
CAP = 2
SCALE = HD ** (-0.5)
DRAFT_ROWS = 128
PAIR = 8
EXP2_SCALE = SCALE * 1.4426950408889634


def pool_tokens(matrix):
    grouped = matrix.astype(jnp.float32).reshape(matrix.shape[0] // POOL, POOL, matrix.shape[1])
    return (grouped.sum(axis=1) * POOL ** (-0.5)).astype(jnp.bfloat16)


def sparse_kernel(tbl_ref, q_ref, *refs):
    near_k, near_v = refs[0], refs[1]
    far_count = (len(refs) - 5) // 2
    far_k = refs[2:2 + far_count]
    far_v = refs[2 + far_count:2 + 2 * far_count]
    o_ref, kall_ref, vall_ref = refs[2 + 2 * far_count:]
    per_dev = q_ref.shape[0] // BLOCK
    sel = tbl_ref.shape[0] // per_dev
    near_rows = near_k.shape[0]
    kall_ref[0:near_rows, :] = near_k[...]
    vall_ref[0:near_rows, :] = near_v[...]
    offset = near_rows
    for kr, vr in zip(far_k, far_v):
        kall_ref[offset:offset + kr.shape[0], :] = kr[...]
        vall_ref[offset:offset + vr.shape[0], :] = vr[...]
        offset += kr.shape[0]
    last = offset // BLOCK - 1

    def one_block(i):
        row = pl.multiple_of(i * BLOCK, BLOCK)
        keys = []
        values = []
        for j in range(sel):
            start = pl.multiple_of(jnp.clip(tbl_ref[i * sel + j], 0, last) * BLOCK, BLOCK)
            keys.append(kall_ref[pl.ds(start, BLOCK), :])
            values.append(vall_ref[pl.ds(start, BLOCK), :])
        raw = lax.dot_general(
            q_ref[pl.ds(row, BLOCK), :], jnp.concatenate(keys, axis=0),
            (((1,), (1,)), ((), ())), preferred_element_type=jnp.float32,
        )
        running = jnp.max(raw, axis=1, keepdims=True)
        weights = jnp.exp2((raw - running) * EXP2_SCALE)
        totals = jnp.sum(weights, axis=1, keepdims=True)
        weighted = jnp.dot(
            weights.astype(jnp.bfloat16), jnp.concatenate(values, axis=0),
            preferred_element_type=jnp.float32,
        )
        o_ref[pl.ds(row, BLOCK), :] = (weighted / totals).astype(o_ref.dtype)

    def body(i, carry):
        for lane in range(PAIR):
            one_block(i * PAIR + lane)
        return carry

    lax.fori_loop(0, per_dev // PAIR, body, 0)
    for i in range(per_dev - per_dev % PAIR, per_dev):
        one_block(i)


def sparse_attention(tbl, queries, keys, values, far_keys, far_values, head_lo, heads):
    rows = queries.shape[0]

    def column(h, t):
        return (0, h + head_lo)

    operands = [keys, values] + list(far_keys) + list(far_values)
    total_rows = keys.shape[0] + sum(k.shape[0] for k in far_keys)
    sel = tbl.shape[0] * BLOCK // rows
    cost = pl.CostEstimate(
        flops=4 * rows * sel * BLOCK * HD * heads,
        transcendentals=rows * sel * BLOCK * heads,
        bytes_accessed=2 * HD * heads * (2 * rows + 2 * total_rows),
    )
    return pl.pallas_call(
        sparse_kernel,
        out_shape=jax.ShapeDtypeStruct((rows, heads * HD), jnp.bfloat16),
        cost_estimate=cost,
        grid_spec=pltpu.PrefetchScalarGridSpec(
            num_scalar_prefetch=1,
            grid=(heads,),
            in_specs=[pl.BlockSpec((rows, HD), lambda h, t: (0, h))]
            + [pl.BlockSpec((x.shape[0], HD), column) for x in operands],
            out_specs=pl.BlockSpec((rows, HD), lambda h, t: (0, h)),
            scratch_shapes=[
                pltpu.VMEM((total_rows, HD), jnp.bfloat16),
                pltpu.VMEM((total_rows, HD), jnp.bfloat16),
            ],
        ),
    )(tbl, queries, *operands)


def pooling_matrix(tile):
    token = lax.broadcasted_iota(jnp.int32, (tile, tile * POOL), 1)
    draft = lax.broadcasted_iota(jnp.int32, (tile, tile * POOL), 0)
    return jnp.where(token // POOL == draft, POOL ** (-0.5), 0.0).astype(jnp.bfloat16)


def draft_kernel(split, qa_ref, qb_ref, k_ref, v_ref, o_ref):
    pooling = pooling_matrix(o_ref.shape[0])
    chosen = jnp.where(pl.program_id(0) < split, qa_ref[...], qb_ref[...])
    pooled = jnp.dot(pooling, chosen, preferred_element_type=jnp.float32).astype(jnp.bfloat16)
    raw = lax.dot_general(
        pooled, k_ref[...], (((1,), (1,)), ((), ())), preferred_element_type=jnp.float32
    )
    running = jnp.max(raw, axis=1, keepdims=True)
    weights = jnp.exp2((raw - running) * EXP2_SCALE)
    totals = jnp.sum(weights, axis=1, keepdims=True)
    weighted = jnp.dot(weights.astype(jnp.bfloat16), v_ref[...], preferred_element_type=jnp.float32)
    o_ref[...] = (weighted / totals).astype(o_ref.dtype)


def draft_attention(leading, trailing, keys, values):
    token_rows = leading.shape[0]
    split = leading.shape[1] // HD
    later = trailing.shape[1] // HD
    rows = token_rows // POOL
    width = keys.shape[1]
    heads = width // HD
    key_rows = keys.shape[0]
    tile = min(DRAFT_ROWS, rows)
    cost = pl.CostEstimate(
        flops=4 * rows * key_rows * HD * heads + 2 * rows * tile * POOL * HD * heads,
        transcendentals=rows * key_rows * heads,
        bytes_accessed=2 * HD * heads * (2 * token_rows + rows + 2 * key_rows),
    )
    return pl.pallas_call(
        functools.partial(draft_kernel, split),
        out_shape=jax.ShapeDtypeStruct((rows, width), jnp.bfloat16),
        cost_estimate=cost,
        grid=(heads, rows // tile),
        in_specs=[
            pl.BlockSpec((tile * POOL, HD), lambda h, r: (r, jnp.minimum(h, split - 1))),
            pl.BlockSpec(
                (tile * POOL, HD), lambda h, r: (r, jnp.clip(h - split, 0, later - 1))
            ),
            pl.BlockSpec((key_rows, HD), lambda h, r: (0, h)),
            pl.BlockSpec((key_rows, HD), lambda h, r: (0, h)),
        ],
        out_specs=pl.BlockSpec((tile, HD), lambda h, r: (r, h)),
    )(leading, trailing, keys, values)


def head_permutes(matrix):
    count = lax.axis_size("head")
    me = lax.axis_index("head")
    rows, total = matrix.shape
    chunks = matrix.reshape(rows, count, total // count)
    by_shift = [lax.dynamic_index_in_dim(chunks, me, axis=1, keepdims=False)]
    for shift in range(1, count):
        piece = lax.dynamic_index_in_dim(chunks, (me + shift) % count, axis=1, keepdims=False)
        by_shift.append(
            lax.ppermute(piece, "head", [(i, (i + shift) % count) for i in range(count)])
        )
    stacked = jnp.stack(by_shift, axis=0)
    order = (me - jnp.arange(count, dtype=jnp.int32)) % count
    return jnp.take(stacked, order, axis=0).reshape(count * rows, total // count)


def on_device(query_in, key_in, value_in, block_lists):
    key_rows = head_permutes(key_in)
    value_rows = lax.all_to_all(value_in, "head", split_axis=1, concat_axis=0, tiled=True)
    seq_rows, width = key_rows.shape
    head_count = lax.axis_size("head")
    heads = width // HD
    first = max(1, heads // 2)
    spans = [(lo, n) for lo, n in ((0, first), (first, heads - first)) if n > 0]
    grouped_q = query_in.reshape(query_in.shape[0], head_count, width)
    query_slices = [
        grouped_q[:, :, lo * HD:(lo + n) * HD].reshape(query_in.shape[0], -1) for lo, n in spans
    ]

    def query_a2a(piece):
        return lax.all_to_all(piece, "head", split_axis=1, concat_axis=0, tiled=True)

    draft_keys = lax.all_gather(pool_tokens(key_rows), "seq", axis=0, tiled=True)
    draft_values = lax.all_gather(pool_tokens(value_rows), "seq", axis=0, tiled=True)

    seq_count = lax.axis_size("seq")
    seq_index = lax.axis_index("seq")
    per_dev = seq_rows // BLOCK
    block_total, select_count = block_lists.shape
    block_ids = jnp.arange(block_total, dtype=jnp.int32)
    touched = jnp.any(block_lists[:, :, None] == block_ids[None, None, :], axis=1)
    needed = jnp.any(touched.reshape(seq_count, per_dev, seq_count, per_dev), axis=1)
    slot_rank = jnp.cumsum(needed.astype(jnp.int32), axis=2) - 1
    send_need = lax.dynamic_index_in_dim(needed, seq_index, axis=1, keepdims=False)
    send_rank = lax.dynamic_index_in_dim(slot_rank, seq_index, axis=1, keepdims=False)
    slot_hit = send_need[:, None, :] & (
        send_rank[:, None, :] == jnp.arange(CAP, dtype=jnp.int32)[None, :, None]
    )
    send_idx = jnp.sum(
        jnp.where(slot_hit, jnp.arange(per_dev, dtype=jnp.int32)[None, None, :], 0), axis=2
    ).reshape(-1)
    def exchange(rows):
        blocks = jnp.take(rows.reshape(per_dev, BLOCK, width), send_idx, axis=0)
        outgoing = blocks.reshape(seq_count, CAP, BLOCK, width)
        arrivals = []
        for shift in range(1, seq_count):
            parcel = lax.dynamic_index_in_dim(
                outgoing, (seq_index + shift) % seq_count, axis=0, keepdims=False
            )
            arrivals.append(
                lax.ppermute(
                    parcel, "seq", [(i, (i + shift) % seq_count) for i in range(seq_count)]
                )
            )
        return [a.reshape(CAP * BLOCK, width) for a in arrivals]

    own_lists = lax.dynamic_slice_in_dim(block_lists, seq_index * per_dev, per_dev, 0)
    owners = own_lists // per_dev
    within = own_lists % per_dev
    own_rank = lax.dynamic_index_in_dim(slot_rank, seq_index, axis=0, keepdims=False)
    ranks_used = jnp.clip(own_rank[owners, within], 0, CAP - 1)
    distance = (seq_index - owners) % seq_count
    joint_pos = jnp.where(distance == 0, within, per_dev + (distance - 1) * CAP + ranks_used)
    table = jnp.clip(joint_pos, 0, per_dev + (seq_count - 1) * CAP - 1).reshape(-1).astype(jnp.int32)

    remote_keys = exchange(key_rows)
    remote_values = exchange(value_rows)
    leading, remote_keys, key_rows, table = lax.optimization_barrier(
        (query_slices[0], remote_keys, key_rows, table)
    )
    query_parts = [query_a2a(leading)]
    later, remote_values = lax.optimization_barrier((query_slices[1:], remote_values))
    query_parts += [query_a2a(piece) for piece in later]

    pieces = []
    for index, ((head_lo, count), queries) in enumerate(zip(spans, query_parts)):
        rows_part = sparse_attention(
            table, queries, key_rows, value_rows, remote_keys, remote_values, head_lo, count,
        )
        if index == len(spans) - 1:
            rows_part, draft_keys, draft_values = lax.optimization_barrier(
                (rows_part, draft_keys, draft_values)
            )
        back = lax.all_to_all(rows_part, "head", split_axis=0, concat_axis=1, tiled=True)
        pieces.append(back.reshape(back.shape[0], -1, count * HD))
    sparse_out = jnp.concatenate(pieces, axis=2).reshape(pieces[0].shape[0], -1)
    draft_out = draft_attention(query_parts[0], query_parts[-1], draft_keys, draft_values)
    return (draft_out, sparse_out)


def solution(mesh):
    return jax.shard_map(
        on_device,
        mesh=mesh,
        in_specs=(
            P(("groups", "seq", "head"), None),
            P(("groups", "seq", "head"), None),
            P(("groups", "seq", "head"), None),
            P("groups", None),
        ),
        out_specs=(P(("groups", "seq"), "head"), P(("groups", "seq", "head"), None)),
        check_vma=False,
    )
```
